256 devices in a mesh: seq: 64 (over x, z, core), head: 4 (over y).
Axes of the slice: x: 4, y: 4, z: 8, core: 2. Of those that a mesh axis runs over, the one named last changes fastest.
Arguments:
- features_in: bfloat16 [32768, 3072], P('seq', 'head'), may hold values from -66 to 66
- gate_in: bfloat16 [32768, 3072], P('seq', 'head'), may hold values from -6 to 6
- b_input: bfloat16 [32768, 128], P('seq'), may hold values from -0.0234375 to 0.0234375
- c_input: bfloat16 [32768, 128], P('seq'), may hold values from -6 to 6
- log_decay: bfloat16 [32768, 48], P('seq', 'head'), may hold values from -1 to 0, as said below
- row_target: int32 [32768], P('seq'), may hold values from 0 to 32767, as said below
- doc_lengths: int32 [4], replicated, may hold values from 1 to 16384, 32768 in all
- skip_gain: float32 [48], P('head'), may hold values from 0.5 to 1.5
- norm_gain: float32 [3072], P('head'), may hold values from 0.1 to 1.9
- out_weight: bfloat16 [3072, 1536], P('head'), may hold values from -0.109375 to 0.109375
Outputs:
- layer_out: bfloat16 [32768, 1536], P(('seq', 'head'))
The draws below stay inside these ranges and needn't reach their ends.
Inputs may be any that keep to these rules, and one draw needn't show every extreme that they name: row_target is a permutation; the rows of one device go to every device along seq, exactly 8 rows to each. `doc_lengths`: the lengths sum to 32768. `log_decay`: every decay is below one.
All inputs are finite; a program needn't handle non-finite values.
Results may differ from the reference program's by a relative error of at most 0.022.
Values may be sent and summed in bfloat16 or wider, within the bound.
No kernel may reach another device: no remote copies, remote signals or barrier semaphores. Data moves between devices by JAX's collectives and lax.ppermute only.
A program may use at most 128 MiB of HBM per device.

```python
import math
import jax
import jax.numpy as jnp
import numpy as np
from jax import lax

D_MODEL = 1536
ATTENTION_LANES = 48
HEAD_DIM = 64
STATE = 128
TOK_DEV = 512
BLOCK = 512
DOCS = 4
GROUP_HEADS = 12
GROUPS = 64
CAP = 8
STACKED_SPOTS = 32768
MOST_DOC = 16384


def shuffle_one(sub_key):
    return jax.random.permutation(sub_key, TOK_DEV)


def make_targets(key):
    key = jax.random.fold_in(key, 17)
    lookup_series = jax.random.split(key, 3)
    shards = STACKED_SPOTS // TOK_DEV
    offsets = jax.random.permutation(lookup_series[0], shards)[:GROUPS].astype(jnp.int32)
    slots = jnp.arange(TOK_DEV, dtype=jnp.int32)
    sources = jnp.arange(shards, dtype=jnp.int32)[:, None]
    target_dev = (sources - offsets[slots // CAP][None, :]) % shards
    shuffle_in = jax.vmap(shuffle_one)(jax.random.split(lookup_series[1], shards)).astype(jnp.int32)
    shuffle_out = jax.vmap(shuffle_one)(jax.random.split(lookup_series[2], shards)).astype(jnp.int32)
    target = target_dev * TOK_DEV + shuffle_out[target_dev, slots[None, :]]
    row_table = jnp.zeros((shards, TOK_DEV), jnp.int32).at[sources, shuffle_in].set(target)
    return row_table.reshape(STACKED_SPOTS)


def draw_row_target(key, part):
    return make_targets(key)


def draw_log_decay(key, part):
    targets = make_targets(key)
    key = jax.random.fold_in(key, 23)
    lookup_series = jax.random.split(key, 7)
    fast_share = 0.5
    fast_head = jax.random.uniform(lookup_series[0], (ATTENTION_LANES,)) < fast_share
    fast_rate = jnp.exp(jax.random.uniform(lookup_series[1], (ATTENTION_LANES,), minval=math.log(1.0 / 50.0), maxval=math.log(1.0 / 30.0)))
    slow_rate = jnp.exp(jax.random.uniform(lookup_series[2], (ATTENTION_LANES,), minval=math.log(0.03), maxval=math.log(0.25))) / STACKED_SPOTS
    head_rate = jnp.where(fast_head, fast_rate, slow_rate)
    roughness = jnp.exp(jax.random.uniform(lookup_series[3], (STACKED_SPOTS, ATTENTION_LANES), minval=math.log(0.5), maxval=math.log(2.0)))
    region = jnp.exp(jax.random.uniform(lookup_series[4], (STACKED_SPOTS // TOK_DEV,), minval=math.log(0.5), maxval=math.log(2.0)))
    concatenated_symbols = -head_rate[None, :] * roughness * jnp.repeat(region, TOK_DEV)[:, None]
    spike_location = jax.random.randint(lookup_series[5], (3,), 0, STACKED_SPOTS)
    spike_surcharge = jax.random.uniform(lookup_series[6], (3, ATTENTION_LANES), minval=0.2, maxval=0.5)
    concatenated_symbols = concatenated_symbols.at[spike_location].set(jnp.log(1.0 - spike_surcharge))
    return concatenated_symbols[targets].astype(jnp.bfloat16)


def draw_features_in(key, part):
    key = jax.random.fold_in(key, 31)
    lookup_series = jax.random.split(key, 3)
    columns = ATTENTION_LANES * HEAD_DIM
    head_number = (jnp.arange(columns) // HEAD_DIM).astype(jnp.float32)
    base_draw = jnp.clip(jax.random.normal(lookup_series[0], (STACKED_SPOTS, columns)), -4.0, 4.0)
    head_rise = 3.0 ** (head_number / (ATTENTION_LANES - 1))
    roughness = jnp.exp(jax.random.uniform(lookup_series[1], (columns,), minval=-0.6, maxval=0.6))
    row_scale = jnp.exp(jax.random.uniform(lookup_series[2], (STACKED_SPOTS, 1), minval=math.log(0.3), maxval=math.log(3.0)))
    return (base_draw * row_scale * head_rise[None, :] * roughness[None, :]).astype(jnp.bfloat16)


def block_scale(stream_key, dims, cuts, least, top_value):
    level = 1.0
    for dim, parts in cuts:
        heights = jax.random.uniform(jax.random.fold_in(jax.random.fold_in(stream_key, 6), dim), (parts,), jnp.float32, least / len(cuts), top_value / len(cuts))
        level = level * jnp.repeat(jnp.exp(heights), dims[dim] // parts).reshape((-1,) + (1,) * (len(dims) - 1 - dim))
    return level


def profile(amount, total, most, skew):
    loads = [(1 << 20) // math.isqrt(standing ** skew) + 1 for standing in range(2, amount + 1)]
    rest, counts = total - most - (amount - 1), [1] * (amount - 1)
    while rest > 0:
        free = [i for i in range(amount - 1) if counts[i] < most]
        pool, budget = sum([loads[i] for i in free]), rest
        for i in free:
            extra = min(most - counts[i], max(1, budget * loads[i] // pool), rest)
            counts[i] = counts[i] + extra
            rest = rest - extra
    return np.array([most] + counts)


def ragged_sizes(stream_key, amount, total, most, slope):
    if amount == 2:
        one = jax.random.randint(stream_key, (), max(1, total - most), min(most, total - 1) + 1)
        return jnp.stack([one, total - one])
    sizes = jnp.asarray(profile(amount, total, most, slope), jnp.int32)
    couples = (amount - 1) // 2
    giver, sink = sizes[1:1 + 2 * couples:2], sizes[2:2 + 2 * couples:2]
    slack = jnp.minimum(giver - 1, most - sink)
    moved = jax.random.randint(jax.random.fold_in(stream_key, 1), (couples,), 0, 1 << 20) % (slack + 1)
    sizes = sizes.at[1:1 + 2 * couples:2].set(giver - moved).at[2:2 + 2 * couples:2].set(sink + moved)
    return sizes[jax.random.permutation(jax.random.fold_in(stream_key, 2), amount)]


def centred(stream_key, shape, deviation, most, cuts=(), kind=jnp.bfloat16):
    array = deviation * jax.random.normal(stream_key, shape, jnp.float32)
    if cuts:
        array = array * block_scale(stream_key, shape, cuts, -0.22, 0.18)
    return jnp.clip(array, -most, most).astype(kind)


def setup_inputs(seed: int = 0) -> dict:
    key_list = jax.random.split(jax.random.key(seed), 11)
    return {
        "features_in": draw_features_in(jax.random.fold_in(key_list[10], 71), 0),
        "gate_in": centred(key_list[1], (STACKED_SPOTS, ATTENTION_LANES * HEAD_DIM), 1.0, 6.0, ((0, 64), (1, 4))),
        "b_input": centred(key_list[2], (STACKED_SPOTS, STATE), (STATE * TOK_DEV) ** -0.5, 0.0234375, ((0, 64),)),
        "c_input": centred(key_list[3], (STACKED_SPOTS, STATE), 1.0, 6.0, ((0, 64),)),
        "log_decay": draw_log_decay(jax.random.fold_in(key_list[10], 71), 0),
        "row_target": draw_row_target(jax.random.fold_in(key_list[10], 71), 0),
        "doc_lengths": ragged_sizes(key_list[6], DOCS, STACKED_SPOTS, MOST_DOC, 1).astype(jnp.int32),
        "skip_gain": jnp.clip(0.5 + 1.0 * jax.random.uniform(key_list[7], (ATTENTION_LANES,), jnp.float32) ** block_scale(key_list[7], (ATTENTION_LANES,), ((0, 4),), -0.2, 0.2), 0.5, 1.5),
        "norm_gain": jnp.clip(1.0 + 0.18 * jax.random.normal(key_list[8], (ATTENTION_LANES * HEAD_DIM,), jnp.float32), 0.1, 1.9),
        "out_weight": centred(key_list[9], (ATTENTION_LANES * HEAD_DIM, D_MODEL), (ATTENTION_LANES * HEAD_DIM) ** -0.5, 0.109375, ((0, 4),)),
    }


far_below = -1e+30
norm_eps = 1e-05

def doc_index(places, starts):
    return (lax.optimization_barrier(jnp.sum((starts[None, :] <= places[:, None]).astype(jnp.int32), axis=1)) - 1).astype(jnp.int32)

def state_terms(by_head, key_block, decay_block, doc_block, before):
    running = jnp.cumsum(decay_block.astype(jnp.float32), axis=0)
    same_doc = (doc_block == doc_block[-1]).astype(jnp.float32)
    closing_weight = jnp.exp(running[-1][None, :] - running) * same_doc[:, None]
    weighted = (key_block.astype(jnp.float32)[None, :, :] * closing_weight.T[:, :, None]).astype(jnp.bfloat16)
    block_state = jnp.einsum('hsn,shp->hpn', weighted.astype(jnp.float32), by_head.astype(jnp.float32))
    through = jnp.exp(running[-1]) * (doc_block[-1] == before).astype(jnp.float32)
    return (block_state, through, running)

def inner_terms(by_head, key_block, query_block, running, doc_block):
    length = running.shape[0]
    later = lax.broadcasted_iota(jnp.int32, (length, length), 0)
    earlier = lax.broadcasted_iota(jnp.int32, (length, length), 1)
    allowed = (later >= earlier) & (doc_block[:, None] == doc_block[None, :])
    running_heads = running.T
    decay_gaps = jnp.where(allowed[None, :, :], running_heads[:, :, None] - running_heads[:, None, :], far_below)
    products = jnp.einsum('tn,sn->ts', query_block.astype(jnp.float32), key_block.astype(jnp.float32))
    affinity_logits = (products[None, :, :] * jnp.exp(decay_gaps)).astype(jnp.bfloat16)
    return jnp.einsum('hts,shp->thp', affinity_logits.astype(jnp.float32), by_head.astype(jnp.float32))

def entry_terms(query_block, carry_state, running, doc_block, before):
    entry_weight = jnp.exp(running) * (doc_block == before).astype(jnp.float32)[:, None]
    carried = jnp.einsum('tn,hpn->thp', query_block.astype(jnp.float32), carry_state, precision=lax.Precision.HIGHEST)
    return carried * entry_weight[:, :, None]

def reference(features_in, gate_in, b_input, c_input, log_decay, row_target, doc_lengths, skip_gain, norm_gain, out_weight):
    source_row = jnp.zeros((STACKED_SPOTS,), jnp.int32).at[row_target].set(jnp.arange(STACKED_SPOTS, dtype=jnp.int32))
    features = features_in[source_row]
    gates = gate_in[source_row]
    key_rows = b_input[source_row]
    query_rows = c_input[source_row]
    decays = log_decay[source_row]
    doc_starts = (jnp.cumsum(doc_lengths) - doc_lengths).astype(jnp.int32)
    blocks = STACKED_SPOTS // BLOCK
    doc_ids = doc_index(jnp.arange(STACKED_SPOTS, dtype=jnp.int32), doc_starts).reshape(blocks, BLOCK)
    doc_before = doc_index(jnp.arange(blocks, dtype=jnp.int32) * BLOCK - 1, doc_starts)
    weights = out_weight.astype(jnp.float32).reshape(ATTENTION_LANES // GROUP_HEADS, GROUP_HEADS * HEAD_DIM, D_MODEL)

    def block_advance(carry_state, pieces):
        incoming_tile, gate_block, key_block, query_block, decay_block, doc_block, before = pieces
        by_head = incoming_tile.reshape(BLOCK, ATTENTION_LANES, HEAD_DIM)
        block_state, through, running = state_terms(by_head, key_block, decay_block, doc_block, before)
        mixed = inner_terms(by_head, key_block, query_block, running, doc_block)
        mixed = mixed + entry_terms(query_block, carry_state, running, doc_block, before)
        mixed = mixed + skip_gain[None, :, None] * by_head.astype(jnp.float32)
        gated = mixed.reshape(BLOCK, ATTENTION_LANES * HEAD_DIM) * jax.nn.silu(gate_block.astype(jnp.float32))
        row_scale = lax.rsqrt(lax.optimization_barrier(jnp.mean(gated * gated, axis=1)) + norm_eps)
        normed = (gated * row_scale[:, None] * norm_gain[None, :]).astype(jnp.bfloat16)
        grouped = normed.astype(jnp.float32).reshape(BLOCK, ATTENTION_LANES // GROUP_HEADS, GROUP_HEADS * HEAD_DIM)
        partial_value = jnp.einsum('tgk,gkd->gtd', grouped, weights).astype(jnp.bfloat16)
        partial_value = lax.optimization_barrier(partial_value)
        out_block = lax.optimization_barrier(jnp.sum(partial_value.astype(jnp.float32), axis=0)).astype(jnp.bfloat16)
        return (through[:, None, None] * carry_state + block_state, out_block)
    start_state = jnp.zeros((ATTENTION_LANES, HEAD_DIM, STATE), jnp.float32)
    final_state, outputs = lax.scan(block_advance, start_state, (features.reshape(blocks, BLOCK, ATTENTION_LANES * HEAD_DIM), gates.reshape(blocks, BLOCK, ATTENTION_LANES * HEAD_DIM), key_rows.reshape(blocks, BLOCK, STATE), query_rows.reshape(blocks, BLOCK, STATE), decays.reshape(blocks, BLOCK, ATTENTION_LANES), doc_ids, doc_before))
    return outputs.reshape(STACKED_SPOTS, D_MODEL)
```

```python
import jax
import jax.numpy as jnp
from jax import lax
from jax.sharding import PartitionSpec as P

ATTENTION_LANES = 48
HEAD_DIM = 64
BLOCK = 512


far_below = -1e30
norm_eps = 1e-05


def combine(earlier, later):
    return (earlier[0] * later[0], later[0][:, None, None] * earlier[1] + later[1])


def exclusive_prefix(kept, state, axis):
    length, here = (lax.axis_size(axis), lax.axis_index(axis))
    heads = kept.shape[0]
    span = (kept, state)
    before = (jnp.ones_like(kept), jnp.zeros_like(state))
    distance = 1
    while distance < length:
        packed = jnp.concatenate(
            [span[1], jnp.broadcast_to(span[0][:, None, None], (heads, 1, state.shape[2]))], axis=1
        ).astype(jnp.bfloat16)
        pairs = [(j, j + distance) for j in range(length - distance)]
        got = lax.ppermute(packed, axis, pairs).astype(jnp.float32)
        got = (got[:, -1, 0], got[:, :-1, :])
        reached = here >= distance
        new_before = combine(got, before)
        before = jax.tree.map(lambda a, b: jnp.where(reached, a, b), new_before, before)
        if distance * 2 < length:
            new_span = combine(got, span)
            span = jax.tree.map(lambda a, b: jnp.where(reached, a, b), new_span, span)
        distance *= 2
    return before


def doc_index(places, starts):
    return jnp.sum((starts[None, :] <= places[:, None]).astype(jnp.int32), axis=1) - 1


def state_terms(by_head, key_block, decay_block, doc_block, before):
    running = jnp.cumsum(decay_block.astype(jnp.float32), axis=0)
    same_doc = (doc_block == doc_block[-1]).astype(jnp.float32)
    closing_weight = jnp.exp(running[-1][None, :] - running) * same_doc[:, None]
    weighted = (key_block.astype(jnp.float32)[None, :, :] * closing_weight.T[:, :, None]).astype(
        jnp.bfloat16
    )
    block_state = jnp.einsum("hsn,shp->hpn", weighted, by_head, preferred_element_type=jnp.float32)
    through = jnp.exp(running[-1]) * (doc_block[-1] == before).astype(jnp.float32)
    return (block_state, through, running)


def inner_terms(by_head, key_block, query_block, running, doc_block):
    length = running.shape[0]
    later = lax.broadcasted_iota(jnp.int32, (length, length), 0)
    earlier = lax.broadcasted_iota(jnp.int32, (length, length), 1)
    allowed = (later >= earlier) & (doc_block[:, None] == doc_block[None, :])
    running_heads = running.T
    decay_gaps = jnp.where(
        allowed[None, :, :], running_heads[:, :, None] - running_heads[:, None, :], far_below
    )
    products = jnp.einsum("tn,sn->ts", query_block, key_block, preferred_element_type=jnp.float32)
    affinity_logits = (products[None, :, :] * jnp.exp(decay_gaps)).astype(jnp.bfloat16)
    return jnp.einsum("hts,shp->thp", affinity_logits, by_head, preferred_element_type=jnp.float32)


def entry_terms(query_block, carry_state, running, doc_block, before):
    entry_weight = jnp.exp(running) * (doc_block == before).astype(jnp.float32)[:, None]
    carried = jnp.einsum(
        "tn,hpn->thp", query_block.astype(jnp.float32), carry_state, precision=lax.Precision.HIGHEST
    )
    return carried * entry_weight[:, :, None]


def body(
    features_in,
    gate_in,
    b_input,
    c_input,
    log_decay,
    row_target,
    doc_lengths,
    skip_gain,
    norm_gain,
    out_weight,
):
    tok_dev = features_in.shape[0]
    heads_here = log_decay.shape[1]
    feats = features_in.shape[1]
    width = feats // heads_here
    n_state = b_input.shape[1]
    shards = lax.axis_size("seq")
    capacity = tok_dev // shards
    owner = row_target // tok_dev
    local_place = row_target - owner * tok_dev
    owner_hits = (owner[:, None] == lax.broadcasted_iota(jnp.int32, (tok_dev, shards), 1)).astype(
        jnp.int32
    )
    slot_rank = jnp.sum((jnp.cumsum(owner_hits, axis=0) - owner_hits) * owner_hits, axis=1)
    slot_index = owner * capacity + slot_rank
    place_hi = (local_place // 32).astype(jnp.bfloat16)
    place_lo = (local_place % 32).astype(jnp.bfloat16)
    rows_out = jnp.concatenate(
        [features_in, gate_in, b_input, c_input, log_decay, place_hi[:, None], place_lo[:, None]],
        axis=1,
    )
    to_slot = (
        lax.broadcasted_iota(jnp.int32, (tok_dev, tok_dev), 0) == slot_index[None, :]
    ).astype(jnp.bfloat16)
    packed = jnp.dot(to_slot, rows_out, preferred_element_type=jnp.float32).astype(jnp.bfloat16)
    moved = lax.all_to_all(
        packed.reshape(shards, capacity, packed.shape[1]), "seq", split_axis=0, concat_axis=0, tiled=True
    ).reshape(tok_dev, packed.shape[1])
    columns = packed.shape[1]
    arrived = (
        moved[:, columns - 2].astype(jnp.int32) * 32 + moved[:, columns - 1].astype(jnp.int32)
    )
    to_place = (
        lax.broadcasted_iota(jnp.int32, (tok_dev, tok_dev), 0) == arrived[None, :]
    ).astype(jnp.bfloat16)
    rows = jnp.dot(to_place, moved, preferred_element_type=jnp.float32).astype(jnp.bfloat16)
    features = rows[:, :feats]
    gate_rows = rows[:, feats : 2 * feats]
    key_full = rows[:, 2 * feats : 2 * feats + n_state]
    query_full = rows[:, 2 * feats + n_state : 2 * feats + 2 * n_state]
    decays = rows[:, 2 * feats + 2 * n_state : 2 * feats + 2 * n_state + heads_here]

    doc_starts = jnp.cumsum(doc_lengths) - doc_lengths
    first_place = lax.axis_index("seq") * tok_dev
    blocks = tok_dev // BLOCK
    places = first_place + lax.broadcasted_iota(jnp.int32, (tok_dev,), 0)
    doc_ids = doc_index(places, doc_starts).reshape(blocks, BLOCK)
    doc_before = doc_index(
        first_place + lax.broadcasted_iota(jnp.int32, (blocks,), 0) * BLOCK - 1, doc_starts
    )
    inputs_blocks = features.reshape(blocks, BLOCK, heads_here, width)
    key_blocks = key_full.reshape(blocks, BLOCK, n_state)
    query_blocks = query_full.reshape(blocks, BLOCK, n_state)
    decay_blocks = decays.reshape(blocks, BLOCK, heads_here)

    def state_pass(carry, pieces):
        carry_state, kept_share = carry
        by_head, key_block, query_block, decay_block, doc_block, before = pieces
        block_state, through, running = state_terms(
            by_head, key_block, decay_block, doc_block, before
        )
        new_carry = (through[:, None, None] * carry_state + block_state, through * kept_share)
        return (new_carry, (block_state, through, running))

    zero_state = jnp.zeros((heads_here, width, n_state), jnp.float32)
    ones_here = jnp.ones((heads_here,), jnp.float32)
    local_carry, block_outputs = lax.scan(
        state_pass,
        (zero_state, ones_here),
        (inputs_blocks, key_blocks, query_blocks, decay_blocks, doc_ids, doc_before),
    )
    local_state, local_kept = local_carry
    block_states, throughs, runnings = (block_outputs[0], block_outputs[1], block_outputs[2])
    entry_kept, entry_state = exclusive_prefix(local_kept, local_state, "seq")

    def mix_pass(carry_state, pieces):
        by_head, key_block, query_block, running, doc_block, before, block_state, through = pieces
        carried = entry_terms(query_block, carry_state, running, doc_block, before)
        mixed_block = (
            inner_terms(by_head, key_block, query_block, running, doc_block)
            + carried
            + skip_gain[None, :, None] * by_head.astype(jnp.float32)
        )
        return (through[:, None, None] * carry_state + block_state, mixed_block)

    final_state, mixed = lax.scan(
        mix_pass,
        entry_state,
        (
            inputs_blocks,
            key_blocks,
            query_blocks,
            runnings,
            doc_ids,
            doc_before,
            block_states,
            throughs,
        ),
    )
    mixed = mixed.reshape(tok_dev, heads_here * width)
    gated = mixed * jax.nn.silu(gate_rows.astype(jnp.float32))
    squares = lax.psum(jnp.sum(gated * gated, axis=1), "head")
    row_scale = lax.rsqrt(squares / (ATTENTION_LANES * HEAD_DIM) + norm_eps)
    normed = (gated * row_scale[:, None] * norm_gain[None, :]).astype(jnp.bfloat16)
    return lax.psum_scatter(
        jnp.dot(normed, out_weight, preferred_element_type=jnp.float32).astype(jnp.bfloat16),
        "head",
        scatter_dimension=0,
        tiled=True,
    )


def solution(mesh):
    in_specs = (
        P("seq", "head"),
        P("seq", "head"),
        P("seq", None),
        P("seq", None),
        P("seq", "head"),
        P("seq"),
        P(),
        P("head"),
        P("head"),
        P("head", None),
    )
    out_specs = P(("seq", "head"), None)
    return jax.shard_map(body, mesh=mesh, in_specs=in_specs, out_specs=out_specs, check_vma=False)
```

```python
import jax
import jax.numpy as jnp
from jax import lax
from jax.sharding import PartitionSpec as P

ATTENTION_LANES = 48
HEAD_DIM = 64
BLOCK = 512


far_below = -1e30
norm_eps = 1e-05


def combine(earlier, later):
    return (earlier[0] * later[0], later[0][:, None, None] * earlier[1] + later[1])


def exclusive_prefix(kept, state, axis, radix=4):
    length, here = (lax.axis_size(axis), lax.axis_index(axis))
    heads = kept.shape[0]
    span = (kept, state)
    before = (jnp.ones_like(kept), jnp.zeros_like(state))
    distance = 1
    while distance < length:
        packed = jnp.concatenate(
            [span[1], jnp.broadcast_to(span[0][:, None, None], (heads, 1, state.shape[2]))], axis=1
        ).astype(jnp.bfloat16)
        gots = []
        for step in range(1, radix):
            shift = step * distance
            if shift < length:
                pairs = [(j, j + shift) for j in range(length - shift)]
                gots.append((shift, lax.ppermute(packed, axis, pairs)))
        last = distance * radix >= length
        for shift, got in gots:
            got = got.astype(jnp.float32)
            got = (got[:, -1, 0], got[:, :-1, :])
            reached = here >= shift
            new_before = combine(got, before)
            before = jax.tree.map(lambda a, b: jnp.where(reached, a, b), new_before, before)
            if not last:
                new_span = combine(got, span)
                span = jax.tree.map(lambda a, b: jnp.where(reached, a, b), new_span, span)
        distance *= radix
    return before


def doc_index(places, starts):
    return jnp.sum((starts[None, :] <= places[:, None]).astype(jnp.int32), axis=1) - 1


def state_terms(by_head, key_block, decay_block, doc_block, before):
    running = jnp.cumsum(decay_block.astype(jnp.float32), axis=0)
    same_doc = (doc_block == doc_block[-1]).astype(jnp.float32)
    closing_weight = jnp.exp(running[-1][None, :] - running) * same_doc[:, None]
    weighted = (key_block.astype(jnp.float32)[None, :, :] * closing_weight.T[:, :, None]).astype(
        jnp.bfloat16
    )
    block_state = jnp.einsum("hsn,shp->hpn", weighted, by_head, preferred_element_type=jnp.float32)
    through = jnp.exp(running[-1]) * (doc_block[-1] == before).astype(jnp.float32)
    return (block_state, through, running)


def inner_terms(by_head, key_block, query_block, running, doc_block):
    length = running.shape[0]
    later = lax.broadcasted_iota(jnp.int32, (length, length), 0)
    earlier = lax.broadcasted_iota(jnp.int32, (length, length), 1)
    allowed = (later >= earlier) & (doc_block[:, None] == doc_block[None, :])
    running_heads = running.T
    decay_gaps = jnp.where(
        allowed[None, :, :], running_heads[:, :, None] - running_heads[:, None, :], far_below
    )
    products = jnp.einsum("tn,sn->ts", query_block, key_block, preferred_element_type=jnp.float32)
    affinity_logits = (products[None, :, :] * jnp.exp(decay_gaps)).astype(jnp.bfloat16)
    return jnp.einsum("hts,shp->thp", affinity_logits, by_head, preferred_element_type=jnp.float32)


def entry_terms(query_block, carry_state, running, doc_block, before):
    entry_weight = jnp.exp(running) * (doc_block == before).astype(jnp.float32)[:, None]
    carried = jnp.einsum(
        "tn,hpn->thp", query_block.astype(jnp.float32), carry_state, precision=lax.Precision.HIGHEST
    )
    return carried * entry_weight[:, :, None]


def body(
    features_in,
    gate_in,
    b_input,
    c_input,
    log_decay,
    row_target,
    doc_lengths,
    skip_gain,
    norm_gain,
    out_weight,
):
    tok_dev = features_in.shape[0]
    heads_here = log_decay.shape[1]
    feats = features_in.shape[1]
    width = feats // heads_here
    n_state = b_input.shape[1]
    shards = lax.axis_size("seq")
    capacity = tok_dev // shards
    owner = row_target // tok_dev
    local_place = row_target - owner * tok_dev
    owner_hits = (owner[:, None] == lax.broadcasted_iota(jnp.int32, (tok_dev, shards), 1)).astype(
        jnp.int32
    )
    slot_rank = jnp.sum((jnp.cumsum(owner_hits, axis=0) - owner_hits) * owner_hits, axis=1)
    slot_index = owner * capacity + slot_rank
    place_hi = (local_place // 32).astype(jnp.bfloat16)
    place_lo = (local_place % 32).astype(jnp.bfloat16)
    rows_out = jnp.concatenate(
        [features_in, gate_in, b_input, c_input, log_decay, place_hi[:, None], place_lo[:, None]],
        axis=1,
    )
    to_slot = (
        lax.broadcasted_iota(jnp.int32, (tok_dev, tok_dev), 0) == slot_index[None, :]
    ).astype(jnp.bfloat16)
    packed = jnp.dot(to_slot, rows_out, preferred_element_type=jnp.float32).astype(jnp.bfloat16)
    moved = lax.all_to_all(
        packed.reshape(shards, capacity, packed.shape[1]), "seq", split_axis=0, concat_axis=0, tiled=True
    ).reshape(tok_dev, packed.shape[1])
    columns = packed.shape[1]
    arrived = (
        moved[:, columns - 2].astype(jnp.int32) * 32 + moved[:, columns - 1].astype(jnp.int32)
    )
    to_place = (
        lax.broadcasted_iota(jnp.int32, (tok_dev, tok_dev), 0) == arrived[None, :]
    ).astype(jnp.bfloat16)
    rows = jnp.dot(to_place, moved, preferred_element_type=jnp.float32).astype(jnp.bfloat16)
    features = rows[:, :feats]
    gate_rows = rows[:, feats : 2 * feats]
    key_full = rows[:, 2 * feats : 2 * feats + n_state]
    query_full = rows[:, 2 * feats + n_state : 2 * feats + 2 * n_state]
    decays = rows[:, 2 * feats + 2 * n_state : 2 * feats + 2 * n_state + heads_here]

    doc_starts = jnp.cumsum(doc_lengths) - doc_lengths
    first_place = lax.axis_index("seq") * tok_dev
    blocks = tok_dev // BLOCK
    places = first_place + lax.broadcasted_iota(jnp.int32, (tok_dev,), 0)
    doc_ids = doc_index(places, doc_starts).reshape(blocks, BLOCK)
    doc_before = doc_index(
        first_place + lax.broadcasted_iota(jnp.int32, (blocks,), 0) * BLOCK - 1, doc_starts
    )
    inputs_blocks = features.reshape(blocks, BLOCK, heads_here, width)
    key_blocks = key_full.reshape(blocks, BLOCK, n_state)
    query_blocks = query_full.reshape(blocks, BLOCK, n_state)
    decay_blocks = decays.reshape(blocks, BLOCK, heads_here)

    def state_pass(carry, pieces):
        carry_state, kept_share = carry
        by_head, key_block, query_block, decay_block, doc_block, before = pieces
        block_state, through, running = state_terms(
            by_head, key_block, decay_block, doc_block, before
        )
        new_carry = (through[:, None, None] * carry_state + block_state, through * kept_share)
        return (new_carry, (block_state, through, running))

    zero_state = jnp.zeros((heads_here, width, n_state), jnp.float32)
    ones_here = jnp.ones((heads_here,), jnp.float32)
    local_carry, block_outputs = lax.scan(
        state_pass,
        (zero_state, ones_here),
        (inputs_blocks, key_blocks, query_blocks, decay_blocks, doc_ids, doc_before),
    )
    local_state, local_kept = local_carry
    block_states, throughs, runnings = (block_outputs[0], block_outputs[1], block_outputs[2])
    entry_kept, entry_state = exclusive_prefix(local_kept, local_state, "seq")

    def mix_pass(carry_state, pieces):
        by_head, key_block, query_block, running, doc_block, before, block_state, through = pieces
        carried = entry_terms(query_block, carry_state, running, doc_block, before)
        mixed_block = (
            inner_terms(by_head, key_block, query_block, running, doc_block)
            + carried
            + skip_gain[None, :, None] * by_head.astype(jnp.float32)
        )
        return (through[:, None, None] * carry_state + block_state, mixed_block)

    final_state, mixed = lax.scan(
        mix_pass,
        entry_state,
        (
            inputs_blocks,
            key_blocks,
            query_blocks,
            runnings,
            doc_ids,
            doc_before,
            block_states,
            throughs,
        ),
    )
    mixed = mixed.reshape(tok_dev, heads_here * width)
    gated = mixed * jax.nn.silu(gate_rows.astype(jnp.float32))
    squares = lax.psum(jnp.sum(gated * gated, axis=1), "head")
    row_scale = lax.rsqrt(squares / (ATTENTION_LANES * HEAD_DIM) + norm_eps)
    normed = (gated * row_scale[:, None] * norm_gain[None, :]).astype(jnp.bfloat16)
    return lax.psum_scatter(
        jnp.dot(normed, out_weight, preferred_element_type=jnp.float32).astype(jnp.bfloat16),
        "head",
        scatter_dimension=0,
        tiled=True,
    )


def solution(mesh):
    in_specs = (
        P("seq", "head"),
        P("seq", "head"),
        P("seq", None),
        P("seq", None),
        P("seq", "head"),
        P("seq"),
        P(),
        P("head"),
        P("head"),
        P("head", None),
    )
    out_specs = P(("seq", "head"), None)
    return jax.shard_map(body, mesh=mesh, in_specs=in_specs, out_specs=out_specs, check_vma=False)
```

```python
import jax
import jax.numpy as jnp
from jax import lax
from jax.sharding import PartitionSpec as P

ATTENTION_LANES = 48
HEAD_DIM = 64
BLOCK = 512


far_below = -1e30
norm_eps = 1e-05


def combine(earlier, later):
    return (earlier[0] * later[0], later[0][:, None, None] * earlier[1] + later[1])


def group_weights(kept, here):
    count = kept.shape[0]
    j = lax.broadcasted_iota(jnp.int32, (count, count), 0)
    k = lax.broadcasted_iota(jnp.int32, (count, count), 1)
    between = (j < k) & (k < here)
    after = j < k
    into_here = jnp.prod(jnp.where(between[:, :, None], kept[None, :, :], 1.0), axis=1)
    into_here = into_here * (lax.broadcasted_iota(jnp.int32, (count, 1), 0) < here)
    into_end = jnp.prod(jnp.where(after[:, :, None], kept[None, :, :], 1.0), axis=1)
    ahead = lax.broadcasted_iota(jnp.int32, (count, 1), 0) < here
    kept_before = jnp.prod(jnp.where(ahead, kept, 1.0), axis=0)
    return into_here, into_end, kept_before, jnp.prod(kept, axis=0)


def pack_state(kept, state):
    flat = jnp.broadcast_to(kept[:, None, None], (kept.shape[0], 1, state.shape[2]))
    return jnp.concatenate([state, flat], axis=1).astype(jnp.bfloat16)


def exclusive_prefix(kept, state, outer, inner):
    gathered = lax.all_gather(pack_state(kept, state), inner)
    g_kept = gathered[:, :, -1, 0].astype(jnp.float32)
    g_state = gathered[:, :, :-1, :].astype(jnp.float32)
    into_here, into_end, kept_before, kept_all = group_weights(g_kept, lax.axis_index(inner))
    local_before = jnp.einsum("jh,jhpn->hpn", into_here, g_state)
    group_total = jnp.einsum("jh,jhpn->hpn", into_end, g_state)
    totals = lax.all_gather(pack_state(kept_all, group_total), outer)
    t_kept = totals[:, :, -1, 0].astype(jnp.float32)
    t_state = totals[:, :, :-1, :].astype(jnp.float32)
    group_into, _, _, _ = group_weights(t_kept, lax.axis_index(outer))
    group_before = jnp.einsum("jh,jhpn->hpn", group_into, t_state)
    return kept_before[:, None, None] * group_before + local_before


def doc_index(places, starts):
    return jnp.sum((starts[None, :] <= places[:, None]).astype(jnp.int32), axis=1) - 1


def state_terms(by_head, key_block, decay_block, doc_block, before):
    running = jnp.cumsum(decay_block.astype(jnp.float32), axis=0)
    same_doc = (doc_block == doc_block[-1]).astype(jnp.float32)
    closing_weight = jnp.exp(running[-1][None, :] - running) * same_doc[:, None]
    weighted = (key_block.astype(jnp.float32)[None, :, :] * closing_weight.T[:, :, None]).astype(
        jnp.bfloat16
    )
    block_state = jnp.einsum("hsn,shp->hpn", weighted, by_head, preferred_element_type=jnp.float32)
    through = jnp.exp(running[-1]) * (doc_block[-1] == before).astype(jnp.float32)
    return (block_state, through, running)


def inner_terms(by_head, key_block, query_block, running, doc_block):
    length = running.shape[0]
    later = lax.broadcasted_iota(jnp.int32, (length, length), 0)
    earlier = lax.broadcasted_iota(jnp.int32, (length, length), 1)
    allowed = (later >= earlier) & (doc_block[:, None] == doc_block[None, :])
    running_heads = running.T
    decay_gaps = jnp.where(
        allowed[None, :, :], running_heads[:, :, None] - running_heads[:, None, :], far_below
    )
    products = jnp.einsum("tn,sn->ts", query_block, key_block, preferred_element_type=jnp.float32)
    affinity_logits = (products[None, :, :] * jnp.exp(decay_gaps)).astype(jnp.bfloat16)
    return jnp.einsum("hts,shp->thp", affinity_logits, by_head, preferred_element_type=jnp.float32)


def entry_terms(query_block, carry_state, running, doc_block, before):
    entry_weight = jnp.exp(running) * (doc_block == before).astype(jnp.float32)[:, None]
    carried = jnp.einsum(
        "tn,hpn->thp", query_block.astype(jnp.float32), carry_state, precision=lax.Precision.HIGHEST
    )
    return carried * entry_weight[:, :, None]


def body(
    features_in,
    gate_in,
    b_input,
    c_input,
    log_decay,
    row_target,
    doc_lengths,
    skip_gain,
    norm_gain,
    out_weight,
):
    tok_dev = features_in.shape[0]
    heads_here = log_decay.shape[1]
    feats = features_in.shape[1]
    width = feats // heads_here
    n_state = b_input.shape[1]
    shards = lax.axis_size(("sx", "sz"))
    capacity = tok_dev // shards
    owner = row_target // tok_dev
    local_place = row_target - owner * tok_dev
    owner_hits = (owner[:, None] == lax.broadcasted_iota(jnp.int32, (tok_dev, shards), 1)).astype(
        jnp.int32
    )
    slot_rank = jnp.sum((jnp.cumsum(owner_hits, axis=0) - owner_hits) * owner_hits, axis=1)
    slot_index = owner * capacity + slot_rank
    place_hi = (local_place // 32).astype(jnp.bfloat16)
    place_lo = (local_place % 32).astype(jnp.bfloat16)
    rows_out = jnp.concatenate(
        [features_in, gate_in, b_input, c_input, log_decay, place_hi[:, None], place_lo[:, None]],
        axis=1,
    )
    to_slot = (
        lax.broadcasted_iota(jnp.int32, (tok_dev, tok_dev), 0) == slot_index[None, :]
    ).astype(jnp.bfloat16)
    packed = jnp.dot(to_slot, rows_out, preferred_element_type=jnp.float32).astype(jnp.bfloat16)
    moved = lax.all_to_all(
        packed.reshape(shards, capacity, packed.shape[1]), ("sx", "sz"), split_axis=0, concat_axis=0, tiled=True
    ).reshape(tok_dev, packed.shape[1])
    columns = packed.shape[1]
    arrived = (
        moved[:, columns - 2].astype(jnp.int32) * 32 + moved[:, columns - 1].astype(jnp.int32)
    )
    to_place = (
        lax.broadcasted_iota(jnp.int32, (tok_dev, tok_dev), 0) == arrived[None, :]
    ).astype(jnp.bfloat16)
    rows = jnp.dot(to_place, moved, preferred_element_type=jnp.float32).astype(jnp.bfloat16)
    features = rows[:, :feats]
    gate_rows = rows[:, feats : 2 * feats]
    key_full = rows[:, 2 * feats : 2 * feats + n_state]
    query_full = rows[:, 2 * feats + n_state : 2 * feats + 2 * n_state]
    decays = rows[:, 2 * feats + 2 * n_state : 2 * feats + 2 * n_state + heads_here]

    doc_starts = jnp.cumsum(doc_lengths) - doc_lengths
    first_place = lax.axis_index(("sx", "sz")) * tok_dev
    blocks = tok_dev // BLOCK
    places = first_place + lax.broadcasted_iota(jnp.int32, (tok_dev,), 0)
    doc_ids = doc_index(places, doc_starts).reshape(blocks, BLOCK)
    doc_before = doc_index(
        first_place + lax.broadcasted_iota(jnp.int32, (blocks,), 0) * BLOCK - 1, doc_starts
    )
    inputs_blocks = features.reshape(blocks, BLOCK, heads_here, width)
    key_blocks = key_full.reshape(blocks, BLOCK, n_state)
    query_blocks = query_full.reshape(blocks, BLOCK, n_state)
    decay_blocks = decays.reshape(blocks, BLOCK, heads_here)

    def state_pass(carry, pieces):
        carry_state, kept_share = carry
        by_head, key_block, query_block, decay_block, doc_block, before = pieces
        block_state, through, running = state_terms(
            by_head, key_block, decay_block, doc_block, before
        )
        new_carry = (through[:, None, None] * carry_state + block_state, through * kept_share)
        return (new_carry, (block_state, through, running))

    zero_state = jnp.zeros((heads_here, width, n_state), jnp.float32)
    ones_here = jnp.ones((heads_here,), jnp.float32)
    local_carry, block_outputs = lax.scan(
        state_pass,
        (zero_state, ones_here),
        (inputs_blocks, key_blocks, query_blocks, decay_blocks, doc_ids, doc_before),
    )
    local_state, local_kept = local_carry
    block_states, throughs, runnings = (block_outputs[0], block_outputs[1], block_outputs[2])
    entry_state = exclusive_prefix(local_kept, local_state, "sx", "sz")

    def mix_pass(carry_state, pieces):
        by_head, key_block, query_block, running, doc_block, before, block_state, through = pieces
        carried = entry_terms(query_block, carry_state, running, doc_block, before)
        mixed_block = (
            inner_terms(by_head, key_block, query_block, running, doc_block)
            + carried
            + skip_gain[None, :, None] * by_head.astype(jnp.float32)
        )
        return (through[:, None, None] * carry_state + block_state, mixed_block)

    final_state, mixed = lax.scan(
        mix_pass,
        entry_state,
        (
            inputs_blocks,
            key_blocks,
            query_blocks,
            runnings,
            doc_ids,
            doc_before,
            block_states,
            throughs,
        ),
    )
    mixed = mixed.reshape(tok_dev, heads_here * width)
    gated = mixed * jax.nn.silu(gate_rows.astype(jnp.float32))
    squares = lax.psum(jnp.sum(gated * gated, axis=1), "head")
    row_scale = lax.rsqrt(squares / (ATTENTION_LANES * HEAD_DIM) + norm_eps)
    normed = (gated * row_scale[:, None] * norm_gain[None, :]).astype(jnp.bfloat16)
    return lax.psum_scatter(
        jnp.dot(normed, out_weight, preferred_element_type=jnp.float32).astype(jnp.bfloat16),
        "head",
        scatter_dimension=0,
        tiled=True,
    )


def solution(mesh):
    seq = mesh.shape["seq"]
    inner = 16 if seq % 16 == 0 else seq
    devices = mesh.devices.reshape(seq // inner, inner, mesh.shape["head"])
    split_mesh = jax.sharding.Mesh(devices, ("sx", "sz", "head"))
    rows = ("sx", "sz")
    in_specs = (
        P(rows, "head"),
        P(rows, "head"),
        P(rows, None),
        P(rows, None),
        P(rows, "head"),
        P(rows),
        P(),
        P("head"),
        P("head"),
        P("head", None),
    )
    out_specs = P(("sx", "sz", "head"), None)
    return jax.shard_map(
        body, mesh=split_mesh, in_specs=in_specs, out_specs=out_specs, check_vma=False
    )
```

```python
import jax
import jax.numpy as jnp
from jax import lax
from jax.sharding import PartitionSpec as P

ATTENTION_LANES = 48
HEAD_DIM = 64
BLOCK = 512


far_below = -1e30
norm_eps = 1e-05


def combine(earlier, later):
    return (earlier[0] * later[0], later[0][:, None, None] * earlier[1] + later[1])


def pack_state(kept, state):
    flat = jnp.broadcast_to(kept[:, None, None], (kept.shape[0], 1, state.shape[2]))
    return jnp.concatenate([state, flat], axis=1).astype(jnp.bfloat16)


def exclusive_prefix(kept, state, axis):
    length, here = (lax.axis_size(axis), lax.axis_index(axis))
    span = (kept, state)
    before = (jnp.ones_like(kept), jnp.zeros_like(state))
    distance = 1
    while distance < length:
        pairs = [(j, j + distance) for j in range(length - distance)]
        got = lax.ppermute(pack_state(*span), axis, pairs).astype(jnp.float32)
        got = (got[:, -1, 0], got[:, :-1, :])
        reached = here >= distance
        new_before = combine(got, before)
        before = jax.tree.map(lambda a, b: jnp.where(reached, a, b), new_before, before)
        if distance * 2 < length:
            new_span = combine(got, span)
            span = jax.tree.map(lambda a, b: jnp.where(reached, a, b), new_span, span)
        distance *= 2
    return before[1]


def doc_index(places, starts):
    return jnp.sum((starts[None, :] <= places[:, None]).astype(jnp.int32), axis=1) - 1


def state_terms(by_head, key_block, decay_block, doc_block, before):
    running = jnp.cumsum(decay_block.astype(jnp.float32), axis=0)
    same_doc = (doc_block == doc_block[-1]).astype(jnp.float32)
    closing_weight = jnp.exp(running[-1][None, :] - running) * same_doc[:, None]
    weighted = (key_block.astype(jnp.float32)[None, :, :] * closing_weight.T[:, :, None]).astype(
        jnp.bfloat16
    )
    block_state = jnp.einsum("hsn,shp->hpn", weighted, by_head, preferred_element_type=jnp.float32)
    through = jnp.exp(running[-1]) * (doc_block[-1] == before).astype(jnp.float32)
    return (block_state, through, running)


def inner_terms(by_head, key_block, query_block, running, doc_block):
    length = running.shape[0]
    later = lax.broadcasted_iota(jnp.int32, (length, length), 0)
    earlier = lax.broadcasted_iota(jnp.int32, (length, length), 1)
    allowed = (later >= earlier) & (doc_block[:, None] == doc_block[None, :])
    running_heads = running.T
    decay_gaps = jnp.where(
        allowed[None, :, :], running_heads[:, :, None] - running_heads[:, None, :], far_below
    )
    products = jnp.einsum("tn,sn->ts", query_block, key_block, preferred_element_type=jnp.float32)
    affinity_logits = (products[None, :, :] * jnp.exp(decay_gaps)).astype(jnp.bfloat16)
    return jnp.einsum("hts,shp->thp", affinity_logits, by_head, preferred_element_type=jnp.float32)


def entry_terms(query_block, carry_state, running, doc_block, before):
    entry_weight = jnp.exp(running) * (doc_block == before).astype(jnp.float32)[:, None]
    carried = jnp.einsum(
        "tn,hpn->thp", query_block.astype(jnp.float32), carry_state, precision=lax.Precision.HIGHEST
    )
    return carried * entry_weight[:, :, None]


def body(
    features_in,
    gate_in,
    b_input,
    c_input,
    log_decay,
    row_target,
    doc_lengths,
    skip_gain,
    norm_gain,
    out_weight,
):
    tok_dev = features_in.shape[0]
    heads_here = log_decay.shape[1]
    feats = features_in.shape[1]
    width = feats // heads_here
    n_state = b_input.shape[1]
    shards = lax.axis_size(("sx", "sz"))
    capacity = tok_dev // shards
    owner = row_target // tok_dev
    local_place = row_target - owner * tok_dev
    owner_hits = (owner[:, None] == lax.broadcasted_iota(jnp.int32, (tok_dev, shards), 1)).astype(
        jnp.int32
    )
    slot_rank = jnp.sum((jnp.cumsum(owner_hits, axis=0) - owner_hits) * owner_hits, axis=1)
    slot_index = owner * capacity + slot_rank
    place_hi = (local_place // 32).astype(jnp.bfloat16)
    place_lo = (local_place % 32).astype(jnp.bfloat16)
    rows_out = jnp.concatenate(
        [features_in, b_input, c_input, log_decay, place_hi[:, None], place_lo[:, None]], axis=1
    )
    to_slot = (
        lax.broadcasted_iota(jnp.int32, (tok_dev, tok_dev), 0) == slot_index[None, :]
    ).astype(jnp.bfloat16)

    def send(values):
        packed = jnp.dot(to_slot, values, preferred_element_type=jnp.float32).astype(jnp.bfloat16)
        return lax.all_to_all(
            packed.reshape(shards, capacity, packed.shape[1]),
            ("sx", "sz"),
            split_axis=0,
            concat_axis=0,
            tiled=True,
        ).reshape(tok_dev, packed.shape[1])

    moved = send(rows_out)
    columns = rows_out.shape[1]
    arrived = (
        moved[:, columns - 2].astype(jnp.int32) * 32 + moved[:, columns - 1].astype(jnp.int32)
    )
    to_place = (
        lax.broadcasted_iota(jnp.int32, (tok_dev, tok_dev), 0) == arrived[None, :]
    ).astype(jnp.bfloat16)

    def place(values):
        return jnp.dot(to_place, values, preferred_element_type=jnp.float32).astype(jnp.bfloat16)

    rows = place(moved)
    features = rows[:, :feats]
    key_full = rows[:, feats : feats + n_state]
    query_full = rows[:, feats + n_state : feats + 2 * n_state]
    decays = rows[:, feats + 2 * n_state : feats + 2 * n_state + heads_here]
    gate_moved = send(gate_in)

    doc_starts = jnp.cumsum(doc_lengths) - doc_lengths
    first_place = lax.axis_index(("sx", "sz")) * tok_dev
    blocks = tok_dev // BLOCK
    places = first_place + lax.broadcasted_iota(jnp.int32, (tok_dev,), 0)
    doc_ids = doc_index(places, doc_starts).reshape(blocks, BLOCK)
    doc_before = doc_index(
        first_place + lax.broadcasted_iota(jnp.int32, (blocks,), 0) * BLOCK - 1, doc_starts
    )
    inputs_blocks = features.reshape(blocks, BLOCK, heads_here, width)
    key_blocks = key_full.reshape(blocks, BLOCK, n_state)
    query_blocks = query_full.reshape(blocks, BLOCK, n_state)
    decay_blocks = decays.reshape(blocks, BLOCK, heads_here)

    def state_pass(carry, pieces):
        carry_state, kept_share = carry
        by_head, key_block, query_block, decay_block, doc_block, before = pieces
        block_state, through, running = state_terms(
            by_head, key_block, decay_block, doc_block, before
        )
        new_carry = (through[:, None, None] * carry_state + block_state, through * kept_share)
        return (new_carry, (block_state, through, running))

    zero_state = jnp.zeros((heads_here, width, n_state), jnp.float32)
    ones_here = jnp.ones((heads_here,), jnp.float32)
    local_carry, block_outputs = lax.scan(
        state_pass,
        (zero_state, ones_here),
        (inputs_blocks, key_blocks, query_blocks, decay_blocks, doc_ids, doc_before),
    )
    local_state, local_kept = local_carry
    block_states, throughs, runnings = (block_outputs[0], block_outputs[1], block_outputs[2])
    entry_state = exclusive_prefix(local_kept, local_state, ("sx", "sz"))

    def mix_pass(carry_state, pieces):
        by_head, key_block, query_block, running, doc_block, before, block_state, through = pieces
        carried = entry_terms(query_block, carry_state, running, doc_block, before)
        mixed_block = (
            inner_terms(by_head, key_block, query_block, running, doc_block)
            + carried
            + skip_gain[None, :, None] * by_head.astype(jnp.float32)
        )
        return (through[:, None, None] * carry_state + block_state, mixed_block)

    final_state, mixed = lax.scan(
        mix_pass,
        entry_state,
        (
            inputs_blocks,
            key_blocks,
            query_blocks,
            runnings,
            doc_ids,
            doc_before,
            block_states,
            throughs,
        ),
    )
    mixed = mixed.reshape(tok_dev, heads_here * width)
    gate_rows = place(gate_moved)
    gated = mixed * jax.nn.silu(gate_rows.astype(jnp.float32))
    squares = jnp.sum(gated * gated, axis=1)
    square_hi = squares.astype(jnp.bfloat16)
    square_lo = (squares - square_hi.astype(jnp.float32)).astype(jnp.bfloat16)
    unscaled = (gated * norm_gain[None, :]).astype(jnp.bfloat16)
    partial = jnp.dot(unscaled, out_weight, preferred_element_type=jnp.float32).astype(jnp.bfloat16)
    groups = lax.axis_size("head")
    chunk = tok_dev // groups
    d_model = partial.shape[1]
    extra = jnp.concatenate(
        [square_hi.reshape(groups, 1, chunk), square_lo.reshape(groups, 1, chunk)], axis=1
    )
    extra = jnp.pad(extra, ((0, 0), (0, 6), (0, d_model - chunk)))
    sent = jnp.concatenate([partial.reshape(groups, chunk, d_model), extra], axis=1)
    summed = lax.psum_scatter(
        sent.reshape(groups * (chunk + 8), d_model), "head", scatter_dimension=0, tiled=True
    )
    total_squares = summed[chunk, :chunk].astype(jnp.float32) + summed[
        chunk + 1, :chunk
    ].astype(jnp.float32)
    row_scale = lax.rsqrt(total_squares / (ATTENTION_LANES * HEAD_DIM) + norm_eps)
    return (summed[:chunk].astype(jnp.float32) * row_scale[:, None]).astype(jnp.bfloat16)


def solution(mesh):
    seq = mesh.shape["seq"]
    inner = 16 if seq % 16 == 0 else seq
    devices = mesh.devices.reshape(seq // inner, inner, mesh.shape["head"])
    split_mesh = jax.sharding.Mesh(devices, ("sx", "sz", "head"))
    rows = ("sx", "sz")
    in_specs = (
        P(rows, "head"),
        P(rows, "head"),
        P(rows, None),
        P(rows, None),
        P(rows, "head"),
        P(rows),
        P(),
        P("head"),
        P("head"),
        P("head", None),
    )
    out_specs = P(("sx", "sz", "head"), None)
    return jax.shard_map(
        body, mesh=split_mesh, in_specs=in_specs, out_specs=out_specs, check_vma=False
    )
```

```python
import jax
import jax.numpy as jnp
from jax import lax
from jax.sharding import PartitionSpec as P

ATTENTION_LANES = 48
ROWS = ("sx", "sz", "sc")
HEAD_DIM = 64
BLOCK = 512


far_below = -1e30
norm_eps = 1e-05


def combine(earlier, later):
    return (earlier[0] * later[0], later[0][:, None, None] * earlier[1] + later[1])


def pack_state(kept, state):
    flat = jnp.broadcast_to(kept[:, None, None], (kept.shape[0], 1, state.shape[2]))
    return jnp.concatenate([state, flat], axis=1).astype(jnp.bfloat16)


def group_weights(kept, here):
    count = kept.shape[0]
    j = lax.broadcasted_iota(jnp.int32, (count, count), 0)
    k = lax.broadcasted_iota(jnp.int32, (count, count), 1)
    ahead = lax.broadcasted_iota(jnp.int32, (count, 1), 0) < here
    between = (j < k) & (k < here)
    into_here = jnp.prod(jnp.where(between[:, :, None], kept[None, :, :], 1.0), axis=1) * ahead
    into_end = jnp.prod(jnp.where((j < k)[:, :, None], kept[None, :, :], 1.0), axis=1)
    kept_before = jnp.prod(jnp.where(ahead, kept, 1.0), axis=0)
    return into_here, into_end, kept_before, jnp.prod(kept, axis=0)


def exclusive_prefix(kept, state, axes):
    levels = []
    for level, axis in enumerate(axes):
        gathered = lax.all_gather(pack_state(kept, state), axis)
        g_kept = gathered[:, :, -1, 0].astype(jnp.float32)
        g_state = gathered[:, :, :-1, :].astype(jnp.float32)
        into_here, into_end, kept_before, kept_all = group_weights(g_kept, lax.axis_index(axis))
        levels.append((kept_before, jnp.einsum("jh,jhpn->hpn", into_here, g_state)))
        if level + 1 < len(axes):
            state = jnp.einsum("jh,jhpn->hpn", into_end, g_state)
            kept = kept_all
    result = levels[-1][1]
    for kept_before, local_before in reversed(levels[:-1]):
        result = kept_before[:, None, None] * result + local_before
    return result


def doc_index(places, starts):
    return jnp.sum((starts[None, :] <= places[:, None]).astype(jnp.int32), axis=1) - 1


def state_terms(by_head, key_block, decay_block, doc_block, before):
    running = jnp.cumsum(decay_block.astype(jnp.float32), axis=0)
    same_doc = (doc_block == doc_block[-1]).astype(jnp.float32)
    closing_weight = jnp.exp(running[-1][None, :] - running) * same_doc[:, None]
    weighted = (key_block.astype(jnp.float32)[None, :, :] * closing_weight.T[:, :, None]).astype(
        jnp.bfloat16
    )
    block_state = jnp.einsum("hsn,shp->hpn", weighted, by_head, preferred_element_type=jnp.float32)
    through = jnp.exp(running[-1]) * (doc_block[-1] == before).astype(jnp.float32)
    return (block_state, through, running)


def inner_terms(by_head, key_block, query_block, running, doc_block):
    length = running.shape[0]
    later = lax.broadcasted_iota(jnp.int32, (length, length), 0)
    earlier = lax.broadcasted_iota(jnp.int32, (length, length), 1)
    allowed = (later >= earlier) & (doc_block[:, None] == doc_block[None, :])
    running_heads = running.T
    decay_gaps = jnp.where(
        allowed[None, :, :], running_heads[:, :, None] - running_heads[:, None, :], far_below
    )
    products = jnp.einsum("tn,sn->ts", query_block, key_block, preferred_element_type=jnp.float32)
    affinity_logits = (products[None, :, :] * jnp.exp(decay_gaps)).astype(jnp.bfloat16)
    return jnp.einsum("hts,shp->thp", affinity_logits, by_head, preferred_element_type=jnp.float32)


def entry_terms(query_block, carry_state, running, doc_block, before):
    entry_weight = jnp.exp(running) * (doc_block == before).astype(jnp.float32)[:, None]
    carried = jnp.einsum(
        "tn,hpn->thp", query_block.astype(jnp.float32), carry_state, precision=lax.Precision.HIGHEST
    )
    return carried * entry_weight[:, :, None]


def body(
    features_in,
    gate_in,
    b_input,
    c_input,
    log_decay,
    row_target,
    doc_lengths,
    skip_gain,
    norm_gain,
    out_weight,
):
    tok_dev = features_in.shape[0]
    heads_here = log_decay.shape[1]
    feats = features_in.shape[1]
    width = feats // heads_here
    n_state = b_input.shape[1]
    shards = lax.axis_size(ROWS)
    capacity = tok_dev // shards
    owner = row_target // tok_dev
    local_place = row_target - owner * tok_dev
    owner_hits = (owner[:, None] == lax.broadcasted_iota(jnp.int32, (tok_dev, shards), 1)).astype(
        jnp.int32
    )
    slot_rank = jnp.sum((jnp.cumsum(owner_hits, axis=0) - owner_hits) * owner_hits, axis=1)
    slot_index = owner * capacity + slot_rank
    place_hi = (local_place // 32).astype(jnp.bfloat16)
    place_lo = (local_place % 32).astype(jnp.bfloat16)
    rows_out = jnp.concatenate(
        [features_in, gate_in, b_input, c_input, log_decay, place_hi[:, None], place_lo[:, None]],
        axis=1,
    )
    to_slot = (
        lax.broadcasted_iota(jnp.int32, (tok_dev, tok_dev), 0) == slot_index[None, :]
    ).astype(jnp.bfloat16)

    def send(values):
        packed = jnp.dot(to_slot, values, preferred_element_type=jnp.float32).astype(jnp.bfloat16)
        return lax.all_to_all(
            packed.reshape(shards, capacity, packed.shape[1]),
            ROWS,
            split_axis=0,
            concat_axis=0,
            tiled=True,
        ).reshape(tok_dev, packed.shape[1])

    moved = send(rows_out)
    columns = rows_out.shape[1]
    arrived = (
        moved[:, columns - 2].astype(jnp.int32) * 32 + moved[:, columns - 1].astype(jnp.int32)
    )
    to_place = (
        lax.broadcasted_iota(jnp.int32, (tok_dev, tok_dev), 0) == arrived[None, :]
    ).astype(jnp.bfloat16)

    def place(values):
        return jnp.dot(to_place, values, preferred_element_type=jnp.float32).astype(jnp.bfloat16)

    rows = place(moved)
    features = rows[:, :feats]
    gate_rows = rows[:, feats : 2 * feats]
    key_full = rows[:, 2 * feats : 2 * feats + n_state]
    query_full = rows[:, 2 * feats + n_state : 2 * feats + 2 * n_state]
    decays = rows[:, 2 * feats + 2 * n_state : 2 * feats + 2 * n_state + heads_here]

    doc_starts = jnp.cumsum(doc_lengths) - doc_lengths
    first_place = lax.axis_index(ROWS) * tok_dev
    blocks = tok_dev // BLOCK
    places = first_place + lax.broadcasted_iota(jnp.int32, (tok_dev,), 0)
    doc_ids = doc_index(places, doc_starts).reshape(blocks, BLOCK)
    doc_before = doc_index(
        first_place + lax.broadcasted_iota(jnp.int32, (blocks,), 0) * BLOCK - 1, doc_starts
    )
    inputs_blocks = features.reshape(blocks, BLOCK, heads_here, width)
    key_blocks = key_full.reshape(blocks, BLOCK, n_state)
    query_blocks = query_full.reshape(blocks, BLOCK, n_state)
    decay_blocks = decays.reshape(blocks, BLOCK, heads_here)

    def state_pass(carry, pieces):
        carry_state, kept_share = carry
        by_head, key_block, query_block, decay_block, doc_block, before = pieces
        block_state, through, running = state_terms(
            by_head, key_block, decay_block, doc_block, before
        )
        new_carry = (through[:, None, None] * carry_state + block_state, through * kept_share)
        return (new_carry, (block_state, through, running))

    zero_state = jnp.zeros((heads_here, width, n_state), jnp.float32)
    ones_here = jnp.ones((heads_here,), jnp.float32)
    local_carry, block_outputs = lax.scan(
        state_pass,
        (zero_state, ones_here),
        (inputs_blocks, key_blocks, query_blocks, decay_blocks, doc_ids, doc_before),
    )
    local_state, local_kept = local_carry
    block_states, throughs, runnings = (block_outputs[0], block_outputs[1], block_outputs[2])
    entry_state = exclusive_prefix(local_kept, local_state, ("sc", "sz", "sx"))

    def mix_pass(carry_state, pieces):
        by_head, key_block, query_block, running, doc_block, before, block_state, through = pieces
        carried = entry_terms(query_block, carry_state, running, doc_block, before)
        mixed_block = (
            inner_terms(by_head, key_block, query_block, running, doc_block)
            + carried
            + skip_gain[None, :, None] * by_head.astype(jnp.float32)
        )
        return (through[:, None, None] * carry_state + block_state, mixed_block)

    final_state, mixed = lax.scan(
        mix_pass,
        entry_state,
        (
            inputs_blocks,
            key_blocks,
            query_blocks,
            runnings,
            doc_ids,
            doc_before,
            block_states,
            throughs,
        ),
    )
    mixed = mixed.reshape(tok_dev, heads_here * width)
    gated = mixed * jax.nn.silu(gate_rows.astype(jnp.float32))
    squares = jnp.sum(gated * gated, axis=1)
    square_hi = squares.astype(jnp.bfloat16)
    square_lo = (squares - square_hi.astype(jnp.float32)).astype(jnp.bfloat16)
    unscaled = (gated * norm_gain[None, :]).astype(jnp.bfloat16)
    partial = jnp.dot(unscaled, out_weight, preferred_element_type=jnp.float32).astype(jnp.bfloat16)
    groups = lax.axis_size("head")
    chunk = tok_dev // groups
    d_model = partial.shape[1]
    extra = jnp.concatenate(
        [square_hi.reshape(groups, 1, chunk), square_lo.reshape(groups, 1, chunk)], axis=1
    )
    extra = jnp.pad(extra, ((0, 0), (0, 6), (0, d_model - chunk)))
    sent = jnp.concatenate([partial.reshape(groups, chunk, d_model), extra], axis=1)
    summed = lax.psum_scatter(
        sent.reshape(groups * (chunk + 8), d_model), "head", scatter_dimension=0, tiled=True
    )
    total_squares = summed[chunk, :chunk].astype(jnp.float32) + summed[
        chunk + 1, :chunk
    ].astype(jnp.float32)
    row_scale = lax.rsqrt(total_squares / (ATTENTION_LANES * HEAD_DIM) + norm_eps)
    return (summed[:chunk].astype(jnp.float32) * row_scale[:, None]).astype(jnp.bfloat16)


def solution(mesh):
    seq = mesh.shape["seq"]
    devices = mesh.devices.reshape(seq // 16, 8, 2, mesh.shape["head"])
    split_mesh = jax.sharding.Mesh(devices, ROWS + ("head",))
    in_specs = (
        P(ROWS, "head"),
        P(ROWS, "head"),
        P(ROWS, None),
        P(ROWS, None),
        P(ROWS, "head"),
        P(ROWS),
        P(),
        P("head"),
        P("head"),
        P("head", None),
    )
    out_specs = P(ROWS + ("head",), None)
    return jax.shard_map(
        body, mesh=split_mesh, in_specs=in_specs, out_specs=out_specs, check_vma=False
    )
```

```python
import jax
import jax.numpy as jnp
from jax import lax
from jax.sharding import PartitionSpec as P

ATTENTION_LANES = 48
ROWS = ("sx", "sz", "sc")
HEAD_DIM = 64
BLOCK = 512


far_below = -1e30
norm_eps = 1e-05


def combine(earlier, later):
    return (earlier[0] * later[0], later[0][:, None, None] * earlier[1] + later[1])


def pack_state(kept, state):
    flat = jnp.broadcast_to(kept[:, None, None], (kept.shape[0], 1, state.shape[2]))
    return jnp.concatenate([state, flat], axis=1).astype(jnp.bfloat16)


def group_weights(kept, here):
    count = kept.shape[0]
    j = lax.broadcasted_iota(jnp.int32, (count, count), 0)
    k = lax.broadcasted_iota(jnp.int32, (count, count), 1)
    ahead = lax.broadcasted_iota(jnp.int32, (count, 1), 0) < here
    between = (j < k) & (k < here)
    into_here = jnp.prod(jnp.where(between[:, :, None], kept[None, :, :], 1.0), axis=1) * ahead
    into_end = jnp.prod(jnp.where((j < k)[:, :, None], kept[None, :, :], 1.0), axis=1)
    kept_before = jnp.prod(jnp.where(ahead, kept, 1.0), axis=0)
    return into_here, into_end, kept_before, jnp.prod(kept, axis=0)


def gathered_level(kept, state, axis):
    gathered = lax.all_gather(pack_state(kept, state), axis)
    g_kept = gathered[:, :, -1, 0].astype(jnp.float32)
    into_here, into_end, kept_before, kept_all = group_weights(g_kept, lax.axis_index(axis))
    rows = state.shape[1]
    before = jnp.einsum("jh,jhpn->hpn", into_here, gathered.astype(jnp.float32))[:, :rows]
    total = jnp.einsum("jh,jhpn->hpn", into_end, gathered.astype(jnp.float32))[:, :rows]
    return before, kept_before, total, kept_all


def exclusive_prefix(kept, state, pair, line, lines):
    pair_before, pair_kept_before, pair_total, pair_kept = gathered_level(kept, state, pair)
    half = kept.shape[0] // 2
    mine = lax.axis_index(pair) * half
    part_total = lax.dynamic_slice_in_dim(pair_total, mine, half, 0)
    part_kept = lax.dynamic_slice_in_dim(pair_kept, mine, half, 0)
    line_before, line_kept_before, line_total, line_kept = gathered_level(
        part_kept, part_total, line
    )
    outer_before, _, _, _ = gathered_level(line_kept, line_total, lines)
    start_state = line_kept_before[:, None, None] * outer_before + line_before
    whole = lax.all_gather(start_state, pair, tiled=True)
    return pair_kept_before[:, None, None] * whole + pair_before


def doc_index(places, starts):
    return jnp.sum((starts[None, :] <= places[:, None]).astype(jnp.int32), axis=1) - 1


def state_terms(by_head, key_block, decay_block, doc_block, before):
    running = jnp.cumsum(decay_block.astype(jnp.float32), axis=0)
    same_doc = (doc_block == doc_block[-1]).astype(jnp.float32)
    closing_weight = jnp.exp(running[-1][None, :] - running) * same_doc[:, None]
    weighted = (key_block.astype(jnp.float32)[None, :, :] * closing_weight.T[:, :, None]).astype(
        jnp.bfloat16
    )
    block_state = jnp.einsum("hsn,shp->hpn", weighted, by_head, preferred_element_type=jnp.float32)
    through = jnp.exp(running[-1]) * (doc_block[-1] == before).astype(jnp.float32)
    return (block_state, through, running)


def inner_terms(by_head, key_block, query_block, running, doc_block):
    length = running.shape[0]
    later = lax.broadcasted_iota(jnp.int32, (length, length), 0)
    earlier = lax.broadcasted_iota(jnp.int32, (length, length), 1)
    allowed = (later >= earlier) & (doc_block[:, None] == doc_block[None, :])
    running_heads = running.T
    decay_gaps = jnp.where(
        allowed[None, :, :], running_heads[:, :, None] - running_heads[:, None, :], far_below
    )
    products = jnp.einsum("tn,sn->ts", query_block, key_block, preferred_element_type=jnp.float32)
    affinity_logits = (products[None, :, :] * jnp.exp(decay_gaps)).astype(jnp.bfloat16)
    return jnp.einsum("hts,shp->thp", affinity_logits, by_head, preferred_element_type=jnp.float32)


def entry_terms(query_block, carry_state, running, doc_block, before):
    entry_weight = jnp.exp(running) * (doc_block == before).astype(jnp.float32)[:, None]
    carried = jnp.einsum(
        "tn,hpn->thp", query_block.astype(jnp.float32), carry_state, precision=lax.Precision.HIGHEST
    )
    return carried * entry_weight[:, :, None]


def body(
    features_in,
    gate_in,
    b_input,
    c_input,
    log_decay,
    row_target,
    doc_lengths,
    skip_gain,
    norm_gain,
    out_weight,
):
    tok_dev = features_in.shape[0]
    heads_here = log_decay.shape[1]
    feats = features_in.shape[1]
    width = feats // heads_here
    n_state = b_input.shape[1]
    shards = lax.axis_size(ROWS)
    capacity = tok_dev // shards
    owner = row_target // tok_dev
    local_place = row_target - owner * tok_dev
    owner_hits = (owner[:, None] == lax.broadcasted_iota(jnp.int32, (tok_dev, shards), 1)).astype(
        jnp.int32
    )
    slot_rank = jnp.sum((jnp.cumsum(owner_hits, axis=0) - owner_hits) * owner_hits, axis=1)
    slot_index = owner * capacity + slot_rank
    place_hi = (local_place // 32).astype(jnp.bfloat16)
    place_lo = (local_place % 32).astype(jnp.bfloat16)
    rows_out = jnp.concatenate(
        [features_in, gate_in, b_input, c_input, log_decay, place_hi[:, None], place_lo[:, None]],
        axis=1,
    )
    to_slot = (
        lax.broadcasted_iota(jnp.int32, (tok_dev, tok_dev), 0) == slot_index[None, :]
    ).astype(jnp.bfloat16)

    def send(values):
        packed = jnp.dot(to_slot, values, preferred_element_type=jnp.float32).astype(jnp.bfloat16)
        return lax.all_to_all(
            packed.reshape(shards, capacity, packed.shape[1]),
            ROWS,
            split_axis=0,
            concat_axis=0,
            tiled=True,
        ).reshape(tok_dev, packed.shape[1])

    moved = send(rows_out)
    columns = rows_out.shape[1]
    arrived = (
        moved[:, columns - 2].astype(jnp.int32) * 32 + moved[:, columns - 1].astype(jnp.int32)
    )
    to_place = (
        lax.broadcasted_iota(jnp.int32, (tok_dev, tok_dev), 0) == arrived[None, :]
    ).astype(jnp.bfloat16)

    def place(values):
        return jnp.dot(to_place, values, preferred_element_type=jnp.float32).astype(jnp.bfloat16)

    rows = place(moved)
    features = rows[:, :feats]
    gate_rows = rows[:, feats : 2 * feats]
    key_full = rows[:, 2 * feats : 2 * feats + n_state]
    query_full = rows[:, 2 * feats + n_state : 2 * feats + 2 * n_state]
    decays = rows[:, 2 * feats + 2 * n_state : 2 * feats + 2 * n_state + heads_here]

    doc_starts = jnp.cumsum(doc_lengths) - doc_lengths
    first_place = lax.axis_index(ROWS) * tok_dev
    blocks = tok_dev // BLOCK
    places = first_place + lax.broadcasted_iota(jnp.int32, (tok_dev,), 0)
    doc_ids = doc_index(places, doc_starts).reshape(blocks, BLOCK)
    doc_before = doc_index(
        first_place + lax.broadcasted_iota(jnp.int32, (blocks,), 0) * BLOCK - 1, doc_starts
    )
    inputs_blocks = features.reshape(blocks, BLOCK, heads_here, width)
    key_blocks = key_full.reshape(blocks, BLOCK, n_state)
    query_blocks = query_full.reshape(blocks, BLOCK, n_state)
    decay_blocks = decays.reshape(blocks, BLOCK, heads_here)

    def state_pass(carry, pieces):
        carry_state, kept_share = carry
        by_head, key_block, query_block, decay_block, doc_block, before = pieces
        block_state, through, running = state_terms(
            by_head, key_block, decay_block, doc_block, before
        )
        new_carry = (through[:, None, None] * carry_state + block_state, through * kept_share)
        return (new_carry, (block_state, through, running))

    zero_state = jnp.zeros((heads_here, width, n_state), jnp.float32)
    ones_here = jnp.ones((heads_here,), jnp.float32)
    local_carry, block_outputs = lax.scan(
        state_pass,
        (zero_state, ones_here),
        (inputs_blocks, key_blocks, query_blocks, decay_blocks, doc_ids, doc_before),
    )
    local_state, local_kept = local_carry
    block_states, throughs, runnings = (block_outputs[0], block_outputs[1], block_outputs[2])
    entry_state = exclusive_prefix(local_kept, local_state, "sc", "sz", "sx")

    def mix_pass(carry_state, pieces):
        by_head, key_block, query_block, running, doc_block, before, block_state, through = pieces
        carried = entry_terms(query_block, carry_state, running, doc_block, before)
        mixed_block = (
            inner_terms(by_head, key_block, query_block, running, doc_block)
            + carried
            + skip_gain[None, :, None] * by_head.astype(jnp.float32)
        )
        return (through[:, None, None] * carry_state + block_state, mixed_block)

    final_state, mixed = lax.scan(
        mix_pass,
        entry_state,
        (
            inputs_blocks,
            key_blocks,
            query_blocks,
            runnings,
            doc_ids,
            doc_before,
            block_states,
            throughs,
        ),
    )
    mixed = mixed.reshape(tok_dev, heads_here * width)
    gated = mixed * jax.nn.silu(gate_rows.astype(jnp.float32))
    squares = jnp.sum(gated * gated, axis=1)
    square_hi = squares.astype(jnp.bfloat16)
    square_lo = (squares - square_hi.astype(jnp.float32)).astype(jnp.bfloat16)
    unscaled = (gated * norm_gain[None, :]).astype(jnp.bfloat16)
    partial = jnp.dot(unscaled, out_weight, preferred_element_type=jnp.float32).astype(jnp.bfloat16)
    groups = lax.axis_size("head")
    chunk = tok_dev // groups
    d_model = partial.shape[1]
    extra = jnp.concatenate(
        [square_hi.reshape(groups, 1, chunk), square_lo.reshape(groups, 1, chunk)], axis=1
    )
    extra = jnp.pad(extra, ((0, 0), (0, 6), (0, d_model - chunk)))
    sent = jnp.concatenate([partial.reshape(groups, chunk, d_model), extra], axis=1)
    summed = lax.psum_scatter(
        sent.reshape(groups * (chunk + 8), d_model), "head", scatter_dimension=0, tiled=True
    )
    total_squares = summed[chunk, :chunk].astype(jnp.float32) + summed[
        chunk + 1, :chunk
    ].astype(jnp.float32)
    row_scale = lax.rsqrt(total_squares / (ATTENTION_LANES * HEAD_DIM) + norm_eps)
    return (summed[:chunk].astype(jnp.float32) * row_scale[:, None]).astype(jnp.bfloat16)


def solution(mesh):
    seq = mesh.shape["seq"]
    devices = mesh.devices.reshape(seq // 16, 8, 2, mesh.shape["head"])
    split_mesh = jax.sharding.Mesh(devices, ROWS + ("head",))
    in_specs = (
        P(ROWS, "head"),
        P(ROWS, "head"),
        P(ROWS, None),
        P(ROWS, None),
        P(ROWS, "head"),
        P(ROWS),
        P(),
        P("head"),
        P("head"),
        P("head", None),
    )
    out_specs = P(ROWS + ("head",), None)
    return jax.shard_map(
        body, mesh=split_mesh, in_specs=in_specs, out_specs=out_specs, check_vma=False
    )
```

```python
import jax
import jax.numpy as jnp
from jax import lax
from jax.sharding import PartitionSpec as P

ATTENTION_LANES = 48
ROWS = ("sx", "sz", "sc")
HEAD_DIM = 64
BLOCK = 512


far_below = -1e30
norm_eps = 1e-05


def combine(earlier, later):
    return (earlier[0] * later[0], later[0][:, None, None] * earlier[1] + later[1])


def pack_state(kept, state):
    flat = jnp.broadcast_to(kept[:, None, None], (kept.shape[0], 1, state.shape[2]))
    return jnp.concatenate([state, flat], axis=1).astype(jnp.bfloat16)


def group_weights(kept, here):
    count = kept.shape[0]
    j = lax.broadcasted_iota(jnp.int32, (count, count), 0)
    k = lax.broadcasted_iota(jnp.int32, (count, count), 1)
    ahead = lax.broadcasted_iota(jnp.int32, (count, 1), 0) < here
    between = (j < k) & (k < here)
    into_here = jnp.prod(jnp.where(between[:, :, None], kept[None, :, :], 1.0), axis=1) * ahead
    into_end = jnp.prod(jnp.where((j < k)[:, :, None], kept[None, :, :], 1.0), axis=1)
    kept_before = jnp.prod(jnp.where(ahead, kept, 1.0), axis=0)
    return into_here, into_end, kept_before, jnp.prod(kept, axis=0)


def gathered_level(kept, state, axis):
    gathered = lax.all_gather(pack_state(kept, state), axis)
    g_kept = gathered[:, :, -1, 0].astype(jnp.float32)
    into_here, into_end, kept_before, kept_all = group_weights(g_kept, lax.axis_index(axis))
    rows = state.shape[1]
    before = jnp.einsum("jh,jhpn->hpn", into_here, gathered.astype(jnp.float32))[:, :rows]
    total = jnp.einsum("jh,jhpn->hpn", into_end, gathered.astype(jnp.float32))[:, :rows]
    return before, kept_before, total, kept_all


def exclusive_prefix(kept, state, pair, lines):
    pair_before, pair_kept_before, pair_total, pair_kept = gathered_level(kept, state, pair)
    half = kept.shape[0] // 2
    mine = lax.axis_index(pair) * half
    part_total = lax.dynamic_slice_in_dim(pair_total, mine, half, 0)
    part_kept = lax.dynamic_slice_in_dim(pair_kept, mine, half, 0)
    start_state, _, _, _ = gathered_level(part_kept, part_total, lines)
    whole = lax.all_gather(start_state, pair, tiled=True)
    return pair_kept_before[:, None, None] * whole + pair_before


def doc_index(places, starts):
    return jnp.sum((starts[None, :] <= places[:, None]).astype(jnp.int32), axis=1) - 1


def state_terms(by_head, key_block, decay_block, doc_block, before):
    running = jnp.cumsum(decay_block.astype(jnp.float32), axis=0)
    same_doc = (doc_block == doc_block[-1]).astype(jnp.float32)
    closing_weight = jnp.exp(running[-1][None, :] - running) * same_doc[:, None]
    weighted = (key_block.astype(jnp.float32)[None, :, :] * closing_weight.T[:, :, None]).astype(
        jnp.bfloat16
    )
    block_state = jnp.einsum("hsn,shp->hpn", weighted, by_head, preferred_element_type=jnp.float32)
    through = jnp.exp(running[-1]) * (doc_block[-1] == before).astype(jnp.float32)
    return (block_state, through, running)


def inner_terms(by_head, key_block, query_block, running, doc_block):
    length = running.shape[0]
    later = lax.broadcasted_iota(jnp.int32, (length, length), 0)
    earlier = lax.broadcasted_iota(jnp.int32, (length, length), 1)
    allowed = (later >= earlier) & (doc_block[:, None] == doc_block[None, :])
    running_heads = running.T
    decay_gaps = jnp.where(
        allowed[None, :, :], running_heads[:, :, None] - running_heads[:, None, :], far_below
    )
    products = jnp.einsum("tn,sn->ts", query_block, key_block, preferred_element_type=jnp.float32)
    affinity_logits = (products[None, :, :] * jnp.exp(decay_gaps)).astype(jnp.bfloat16)
    return jnp.einsum("hts,shp->thp", affinity_logits, by_head, preferred_element_type=jnp.float32)


def entry_terms(query_block, carry_state, running, doc_block, before):
    entry_weight = jnp.exp(running) * (doc_block == before).astype(jnp.float32)[:, None]
    carried = jnp.einsum(
        "tn,hpn->thp", query_block.astype(jnp.float32), carry_state, precision=lax.Precision.HIGHEST
    )
    return carried * entry_weight[:, :, None]


def body(
    features_in,
    gate_in,
    b_input,
    c_input,
    log_decay,
    row_target,
    doc_lengths,
    skip_gain,
    norm_gain,
    out_weight,
):
    tok_dev = features_in.shape[0]
    heads_here = log_decay.shape[1]
    feats = features_in.shape[1]
    width = feats // heads_here
    n_state = b_input.shape[1]
    shards = lax.axis_size(ROWS)
    capacity = tok_dev // shards
    owner = row_target // tok_dev
    local_place = row_target - owner * tok_dev
    owner_hits = (owner[:, None] == lax.broadcasted_iota(jnp.int32, (tok_dev, shards), 1)).astype(
        jnp.int32
    )
    slot_rank = jnp.sum((jnp.cumsum(owner_hits, axis=0) - owner_hits) * owner_hits, axis=1)
    slot_index = owner * capacity + slot_rank
    place_hi = (local_place // 32).astype(jnp.bfloat16)
    place_lo = (local_place % 32).astype(jnp.bfloat16)
    rows_out = jnp.concatenate(
        [features_in, gate_in, b_input, c_input, log_decay, place_hi[:, None], place_lo[:, None]],
        axis=1,
    )
    to_slot = (
        lax.broadcasted_iota(jnp.int32, (tok_dev, tok_dev), 0) == slot_index[None, :]
    ).astype(jnp.bfloat16)

    def send(values):
        packed = jnp.dot(to_slot, values, preferred_element_type=jnp.float32).astype(jnp.bfloat16)
        return lax.all_to_all(
            packed.reshape(shards, capacity, packed.shape[1]),
            ROWS,
            split_axis=0,
            concat_axis=0,
            tiled=True,
        ).reshape(tok_dev, packed.shape[1])

    moved = send(rows_out)
    columns = rows_out.shape[1]
    arrived = (
        moved[:, columns - 2].astype(jnp.int32) * 32 + moved[:, columns - 1].astype(jnp.int32)
    )
    to_place = (
        lax.broadcasted_iota(jnp.int32, (tok_dev, tok_dev), 0) == arrived[None, :]
    ).astype(jnp.bfloat16)

    def place(values):
        return jnp.dot(to_place, values, preferred_element_type=jnp.float32).astype(jnp.bfloat16)

    rows = place(moved)
    features = rows[:, :feats]
    gate_rows = rows[:, feats : 2 * feats]
    key_full = rows[:, 2 * feats : 2 * feats + n_state]
    query_full = rows[:, 2 * feats + n_state : 2 * feats + 2 * n_state]
    decays = rows[:, 2 * feats + 2 * n_state : 2 * feats + 2 * n_state + heads_here]

    doc_starts = jnp.cumsum(doc_lengths) - doc_lengths
    first_place = lax.axis_index(ROWS) * tok_dev
    blocks = tok_dev // BLOCK
    places = first_place + lax.broadcasted_iota(jnp.int32, (tok_dev,), 0)
    doc_ids = doc_index(places, doc_starts).reshape(blocks, BLOCK)
    doc_before = doc_index(
        first_place + lax.broadcasted_iota(jnp.int32, (blocks,), 0) * BLOCK - 1, doc_starts
    )
    inputs_blocks = features.reshape(blocks, BLOCK, heads_here, width)
    key_blocks = key_full.reshape(blocks, BLOCK, n_state)
    query_blocks = query_full.reshape(blocks, BLOCK, n_state)
    decay_blocks = decays.reshape(blocks, BLOCK, heads_here)

    def state_pass(carry, pieces):
        carry_state, kept_share = carry
        by_head, key_block, query_block, decay_block, doc_block, before = pieces
        block_state, through, running = state_terms(
            by_head, key_block, decay_block, doc_block, before
        )
        new_carry = (through[:, None, None] * carry_state + block_state, through * kept_share)
        return (new_carry, (block_state, through, running))

    zero_state = jnp.zeros((heads_here, width, n_state), jnp.float32)
    ones_here = jnp.ones((heads_here,), jnp.float32)
    local_carry, block_outputs = lax.scan(
        state_pass,
        (zero_state, ones_here),
        (inputs_blocks, key_blocks, query_blocks, decay_blocks, doc_ids, doc_before),
    )
    local_state, local_kept = local_carry
    block_states, throughs, runnings = (block_outputs[0], block_outputs[1], block_outputs[2])
    entry_state = exclusive_prefix(local_kept, local_state, "sc", ("sx", "sz"))

    def mix_pass(carry_state, pieces):
        by_head, key_block, query_block, running, doc_block, before, block_state, through = pieces
        carried = entry_terms(query_block, carry_state, running, doc_block, before)
        mixed_block = (
            inner_terms(by_head, key_block, query_block, running, doc_block)
            + carried
            + skip_gain[None, :, None] * by_head.astype(jnp.float32)
        )
        return (through[:, None, None] * carry_state + block_state, mixed_block)

    final_state, mixed = lax.scan(
        mix_pass,
        entry_state,
        (
            inputs_blocks,
            key_blocks,
            query_blocks,
            runnings,
            doc_ids,
            doc_before,
            block_states,
            throughs,
        ),
    )
    mixed = mixed.reshape(tok_dev, heads_here * width)
    gated = mixed * jax.nn.silu(gate_rows.astype(jnp.float32))
    squares = jnp.sum(gated * gated, axis=1)
    square_hi = squares.astype(jnp.bfloat16)
    square_lo = (squares - square_hi.astype(jnp.float32)).astype(jnp.bfloat16)
    unscaled = (gated * norm_gain[None, :]).astype(jnp.bfloat16)
    partial = jnp.dot(unscaled, out_weight, preferred_element_type=jnp.float32).astype(jnp.bfloat16)
    groups = lax.axis_size("head")
    chunk = tok_dev // groups
    d_model = partial.shape[1]
    extra = jnp.concatenate(
        [square_hi.reshape(groups, 1, chunk), square_lo.reshape(groups, 1, chunk)], axis=1
    )
    extra = jnp.pad(extra, ((0, 0), (0, 6), (0, d_model - chunk)))
    sent = jnp.concatenate([partial.reshape(groups, chunk, d_model), extra], axis=1)
    summed = lax.psum_scatter(
        sent.reshape(groups * (chunk + 8), d_model), "head", scatter_dimension=0, tiled=True
    )
    total_squares = summed[chunk, :chunk].astype(jnp.float32) + summed[
        chunk + 1, :chunk
    ].astype(jnp.float32)
    row_scale = lax.rsqrt(total_squares / (ATTENTION_LANES * HEAD_DIM) + norm_eps)
    return (summed[:chunk].astype(jnp.float32) * row_scale[:, None]).astype(jnp.bfloat16)


def solution(mesh):
    seq = mesh.shape["seq"]
    devices = mesh.devices.reshape(seq // 16, 8, 2, mesh.shape["head"])
    split_mesh = jax.sharding.Mesh(devices, ROWS + ("head",))
    in_specs = (
        P(ROWS, "head"),
        P(ROWS, "head"),
        P(ROWS, None),
        P(ROWS, None),
        P(ROWS, "head"),
        P(ROWS),
        P(),
        P("head"),
        P("head"),
        P("head", None),
    )
    out_specs = P(ROWS + ("head",), None)
    return jax.shard_map(
        body, mesh=split_mesh, in_specs=in_specs, out_specs=out_specs, check_vma=False
    )
```

```python
import jax
import jax.numpy as jnp
from jax import lax
from jax.sharding import PartitionSpec as P

ATTENTION_LANES = 48
ROWS = ("xh", "xl", "zh", "zm", "zl", "sc")
LEVELS = ("zl", "zm", "zh", "xl", "xh")
HEAD_DIM = 64
BLOCK = 512


far_below = -1e30
norm_eps = 1e-05


def combine(earlier, later):
    return (earlier[0] * later[0], later[0][:, None, None] * earlier[1] + later[1])


def pack_state(kept, state):
    flat = jnp.broadcast_to(kept[:, None, None], (kept.shape[0], 1, state.shape[2]))
    return jnp.concatenate([state, flat], axis=1).astype(jnp.bfloat16)


def group_weights(kept, here):
    count = kept.shape[0]
    j = lax.broadcasted_iota(jnp.int32, (count, count), 0)
    k = lax.broadcasted_iota(jnp.int32, (count, count), 1)
    ahead = lax.broadcasted_iota(jnp.int32, (count, 1), 0) < here
    between = (j < k) & (k < here)
    into_here = jnp.prod(jnp.where(between[:, :, None], kept[None, :, :], 1.0), axis=1) * ahead
    into_end = jnp.prod(jnp.where((j < k)[:, :, None], kept[None, :, :], 1.0), axis=1)
    kept_before = jnp.prod(jnp.where(ahead, kept, 1.0), axis=0)
    return into_here, into_end, kept_before, jnp.prod(kept, axis=0)


def gathered_level(kept, state, axis):
    gathered = lax.all_gather(pack_state(kept, state), axis)
    g_kept = gathered[:, :, -1, 0].astype(jnp.float32)
    into_here, into_end, kept_before, kept_all = group_weights(g_kept, lax.axis_index(axis))
    rows = state.shape[1]
    before = jnp.einsum("jh,jhpn->hpn", into_here, gathered.astype(jnp.float32))[:, :rows]
    total = jnp.einsum("jh,jhpn->hpn", into_end, gathered.astype(jnp.float32))[:, :rows]
    return before, kept_before, total, kept_all


def exclusive_prefix(kept, state, pair, levels):
    pair_before, pair_kept_before, pair_total, pair_kept = gathered_level(kept, state, pair)
    half = kept.shape[0] // 2
    mine = lax.axis_index(pair) * half
    part_total = lax.dynamic_slice_in_dim(pair_total, mine, half, 0)
    part_kept = lax.dynamic_slice_in_dim(pair_kept, mine, half, 0)
    found = []
    for level, axis in enumerate(levels):
        before, kept_before, part_total, part_kept = gathered_level(part_kept, part_total, axis)
        found.append((before, kept_before))
    start_state = found[-1][0]
    for before, kept_before in reversed(found[:-1]):
        start_state = kept_before[:, None, None] * start_state + before
    whole = lax.all_gather(start_state, pair, tiled=True)
    return pair_kept_before[:, None, None] * whole + pair_before


def doc_index(places, starts):
    return jnp.sum((starts[None, :] <= places[:, None]).astype(jnp.int32), axis=1) - 1


def state_terms(by_head, key_block, decay_block, doc_block, before):
    running = jnp.cumsum(decay_block.astype(jnp.float32), axis=0)
    same_doc = (doc_block == doc_block[-1]).astype(jnp.float32)
    closing_weight = jnp.exp(running[-1][None, :] - running) * same_doc[:, None]
    weighted = (key_block.astype(jnp.float32)[None, :, :] * closing_weight.T[:, :, None]).astype(
        jnp.bfloat16
    )
    block_state = jnp.einsum("hsn,shp->hpn", weighted, by_head, preferred_element_type=jnp.float32)
    through = jnp.exp(running[-1]) * (doc_block[-1] == before).astype(jnp.float32)
    return (block_state, through, running)


def inner_terms(by_head, key_block, query_block, running, doc_block):
    length = running.shape[0]
    later = lax.broadcasted_iota(jnp.int32, (length, length), 0)
    earlier = lax.broadcasted_iota(jnp.int32, (length, length), 1)
    allowed = (later >= earlier) & (doc_block[:, None] == doc_block[None, :])
    running_heads = running.T
    decay_gaps = jnp.where(
        allowed[None, :, :], running_heads[:, :, None] - running_heads[:, None, :], far_below
    )
    products = jnp.einsum("tn,sn->ts", query_block, key_block, preferred_element_type=jnp.float32)
    affinity_logits = (products[None, :, :] * jnp.exp(decay_gaps)).astype(jnp.bfloat16)
    return jnp.einsum("hts,shp->thp", affinity_logits, by_head, preferred_element_type=jnp.float32)


def entry_terms(query_block, carry_state, running, doc_block, before):
    entry_weight = jnp.exp(running) * (doc_block == before).astype(jnp.float32)[:, None]
    carried = jnp.einsum(
        "tn,hpn->thp", query_block.astype(jnp.float32), carry_state, precision=lax.Precision.HIGHEST
    )
    return carried * entry_weight[:, :, None]


def body(
    features_in,
    gate_in,
    b_input,
    c_input,
    log_decay,
    row_target,
    doc_lengths,
    skip_gain,
    norm_gain,
    out_weight,
):
    tok_dev = features_in.shape[0]
    heads_here = log_decay.shape[1]
    feats = features_in.shape[1]
    width = feats // heads_here
    n_state = b_input.shape[1]
    shards = lax.axis_size(ROWS)
    capacity = tok_dev // shards
    owner = row_target // tok_dev
    local_place = row_target - owner * tok_dev
    owner_hits = (owner[:, None] == lax.broadcasted_iota(jnp.int32, (tok_dev, shards), 1)).astype(
        jnp.int32
    )
    slot_rank = jnp.sum((jnp.cumsum(owner_hits, axis=0) - owner_hits) * owner_hits, axis=1)
    slot_index = owner * capacity + slot_rank
    place_hi = (local_place // 32).astype(jnp.bfloat16)
    place_lo = (local_place % 32).astype(jnp.bfloat16)
    rows_out = jnp.concatenate(
        [features_in, gate_in, b_input, c_input, log_decay, place_hi[:, None], place_lo[:, None]],
        axis=1,
    )
    to_slot = (
        lax.broadcasted_iota(jnp.int32, (tok_dev, tok_dev), 0) == slot_index[None, :]
    ).astype(jnp.bfloat16)

    def send(values):
        packed = jnp.dot(to_slot, values, preferred_element_type=jnp.float32).astype(jnp.bfloat16)
        return lax.all_to_all(
            packed.reshape(shards, capacity, packed.shape[1]),
            ROWS,
            split_axis=0,
            concat_axis=0,
            tiled=True,
        ).reshape(tok_dev, packed.shape[1])

    moved = send(rows_out)
    columns = rows_out.shape[1]
    arrived = (
        moved[:, columns - 2].astype(jnp.int32) * 32 + moved[:, columns - 1].astype(jnp.int32)
    )
    to_place = (
        lax.broadcasted_iota(jnp.int32, (tok_dev, tok_dev), 0) == arrived[None, :]
    ).astype(jnp.bfloat16)

    def place(values):
        return jnp.dot(to_place, values, preferred_element_type=jnp.float32).astype(jnp.bfloat16)

    rows = place(moved)
    features = rows[:, :feats]
    gate_rows = rows[:, feats : 2 * feats]
    key_full = rows[:, 2 * feats : 2 * feats + n_state]
    query_full = rows[:, 2 * feats + n_state : 2 * feats + 2 * n_state]
    decays = rows[:, 2 * feats + 2 * n_state : 2 * feats + 2 * n_state + heads_here]

    doc_starts = jnp.cumsum(doc_lengths) - doc_lengths
    first_place = lax.axis_index(ROWS) * tok_dev
    blocks = tok_dev // BLOCK
    places = first_place + lax.broadcasted_iota(jnp.int32, (tok_dev,), 0)
    doc_ids = doc_index(places, doc_starts).reshape(blocks, BLOCK)
    doc_before = doc_index(
        first_place + lax.broadcasted_iota(jnp.int32, (blocks,), 0) * BLOCK - 1, doc_starts
    )
    inputs_blocks = features.reshape(blocks, BLOCK, heads_here, width)
    key_blocks = key_full.reshape(blocks, BLOCK, n_state)
    query_blocks = query_full.reshape(blocks, BLOCK, n_state)
    decay_blocks = decays.reshape(blocks, BLOCK, heads_here)

    def state_pass(carry, pieces):
        carry_state, kept_share = carry
        by_head, key_block, query_block, decay_block, doc_block, before = pieces
        block_state, through, running = state_terms(
            by_head, key_block, decay_block, doc_block, before
        )
        new_carry = (through[:, None, None] * carry_state + block_state, through * kept_share)
        return (new_carry, (block_state, through, running))

    zero_state = jnp.zeros((heads_here, width, n_state), jnp.float32)
    ones_here = jnp.ones((heads_here,), jnp.float32)
    local_carry, block_outputs = lax.scan(
        state_pass,
        (zero_state, ones_here),
        (inputs_blocks, key_blocks, query_blocks, decay_blocks, doc_ids, doc_before),
    )
    local_state, local_kept = local_carry
    block_states, throughs, runnings = (block_outputs[0], block_outputs[1], block_outputs[2])
    entry_state = exclusive_prefix(local_kept, local_state, "sc", LEVELS)

    def mix_pass(carry_state, pieces):
        by_head, key_block, query_block, running, doc_block, before, block_state, through = pieces
        carried = entry_terms(query_block, carry_state, running, doc_block, before)
        mixed_block = (
            inner_terms(by_head, key_block, query_block, running, doc_block)
            + carried
            + skip_gain[None, :, None] * by_head.astype(jnp.float32)
        )
        return (through[:, None, None] * carry_state + block_state, mixed_block)

    final_state, mixed = lax.scan(
        mix_pass,
        entry_state,
        (
            inputs_blocks,
            key_blocks,
            query_blocks,
            runnings,
            doc_ids,
            doc_before,
            block_states,
            throughs,
        ),
    )
    mixed = mixed.reshape(tok_dev, heads_here * width)
    gated = mixed * jax.nn.silu(gate_rows.astype(jnp.float32))
    squares = jnp.sum(gated * gated, axis=1)
    square_hi = squares.astype(jnp.bfloat16)
    square_lo = (squares - square_hi.astype(jnp.float32)).astype(jnp.bfloat16)
    unscaled = (gated * norm_gain[None, :]).astype(jnp.bfloat16)
    partial = jnp.dot(unscaled, out_weight, preferred_element_type=jnp.float32).astype(jnp.bfloat16)
    groups = lax.axis_size("head")
    chunk = tok_dev // groups
    d_model = partial.shape[1]
    extra = jnp.concatenate(
        [square_hi.reshape(groups, 1, chunk), square_lo.reshape(groups, 1, chunk)], axis=1
    )
    extra = jnp.pad(extra, ((0, 0), (0, 6), (0, d_model - chunk)))
    sent = jnp.concatenate([partial.reshape(groups, chunk, d_model), extra], axis=1)
    summed = lax.psum_scatter(
        sent.reshape(groups * (chunk + 8), d_model), "head", scatter_dimension=0, tiled=True
    )
    total_squares = summed[chunk, :chunk].astype(jnp.float32) + summed[
        chunk + 1, :chunk
    ].astype(jnp.float32)
    row_scale = lax.rsqrt(total_squares / (ATTENTION_LANES * HEAD_DIM) + norm_eps)
    return (summed[:chunk].astype(jnp.float32) * row_scale[:, None]).astype(jnp.bfloat16)


def solution(mesh):
    seq = mesh.shape["seq"]
    devices = mesh.devices.reshape(seq // 32, 2, 2, 2, 2, 2, mesh.shape["head"])
    split_mesh = jax.sharding.Mesh(devices, ROWS + ("head",))
    in_specs = (
        P(ROWS, "head"),
        P(ROWS, "head"),
        P(ROWS, None),
        P(ROWS, None),
        P(ROWS, "head"),
        P(ROWS),
        P(),
        P("head"),
        P("head"),
        P("head", None),
    )
    out_specs = P(ROWS + ("head",), None)
    return jax.shard_map(
        body, mesh=split_mesh, in_specs=in_specs, out_specs=out_specs, check_vma=False
    )
```

```python
import jax
import jax.numpy as jnp
from jax import lax
from jax.sharding import PartitionSpec as P

ATTENTION_LANES = 48
ROWS = ("sx", "sz", "sc")
HEAD_DIM = 64
BLOCK = 512


far_below = -1e30
norm_eps = 1e-05


def combine(earlier, later):
    return (earlier[0] * later[0], later[0][:, None, None] * earlier[1] + later[1])


def pack_state(kept, state):
    flat = jnp.broadcast_to(kept[:, None, None], (kept.shape[0], 1, state.shape[2]))
    return jnp.concatenate([state, flat], axis=1).astype(jnp.bfloat16)


def group_weights(kept, here):
    count = kept.shape[0]
    j = lax.broadcasted_iota(jnp.int32, (count, count), 0)
    k = lax.broadcasted_iota(jnp.int32, (count, count), 1)
    ahead = lax.broadcasted_iota(jnp.int32, (count, 1), 0) < here
    between = (j < k) & (k < here)
    into_here = jnp.prod(jnp.where(between[:, :, None], kept[None, :, :], 1.0), axis=1) * ahead
    into_end = jnp.prod(jnp.where((j < k)[:, :, None], kept[None, :, :], 1.0), axis=1)
    kept_before = jnp.prod(jnp.where(ahead, kept, 1.0), axis=0)
    return into_here, into_end, kept_before, jnp.prod(kept, axis=0)


def gathered_level(kept, state, axis):
    gathered = lax.all_gather(pack_state(kept, state), axis)
    g_kept = gathered[:, :, -1, 0].astype(jnp.float32)
    into_here, into_end, kept_before, kept_all = group_weights(g_kept, lax.axis_index(axis))
    rows = state.shape[1]
    before = jnp.einsum("jh,jhpn->hpn", into_here, gathered.astype(jnp.float32))[:, :rows]
    total = jnp.einsum("jh,jhpn->hpn", into_end, gathered.astype(jnp.float32))[:, :rows]
    return before, kept_before, total, kept_all


def exclusive_prefix(kept, state, pair, line, lines):
    pair_before, pair_kept_before, pair_total, pair_kept = gathered_level(kept, state, pair)
    half = kept.shape[0] // 2
    mine = lax.axis_index(pair) * half
    part_total = lax.dynamic_slice_in_dim(pair_total, mine, half, 0)
    part_kept = lax.dynamic_slice_in_dim(pair_kept, mine, half, 0)
    line_before, line_kept_before, line_total, line_kept = gathered_level(
        part_kept, part_total, line
    )
    outer_before, _, _, _ = gathered_level(line_kept, line_total, lines)
    start_state = line_kept_before[:, None, None] * outer_before + line_before
    whole = lax.all_gather(start_state, pair, tiled=True)
    return pair_kept_before[:, None, None] * whole + pair_before


def doc_index(places, starts):
    return jnp.sum((starts[None, :] <= places[:, None]).astype(jnp.int32), axis=1) - 1


def state_terms(by_head, key_block, decay_block, doc_block, before):
    running = jnp.cumsum(decay_block.astype(jnp.float32), axis=0)
    same_doc = (doc_block == doc_block[-1]).astype(jnp.float32)
    closing_weight = jnp.exp(running[-1][None, :] - running) * same_doc[:, None]
    weighted = (key_block.astype(jnp.float32)[None, :, :] * closing_weight.T[:, :, None]).astype(
        jnp.bfloat16
    )
    block_state = jnp.einsum("hsn,shp->hpn", weighted, by_head, preferred_element_type=jnp.float32)
    through = jnp.exp(running[-1]) * (doc_block[-1] == before).astype(jnp.float32)
    return (block_state, through, running)


def inner_terms(by_head, key_block, query_block, running, doc_block):
    length = running.shape[0]
    later = lax.broadcasted_iota(jnp.int32, (length, length), 0)
    earlier = lax.broadcasted_iota(jnp.int32, (length, length), 1)
    allowed = (later >= earlier) & (doc_block[:, None] == doc_block[None, :])
    running_heads = running.T
    decay_gaps = jnp.where(
        allowed[None, :, :], running_heads[:, :, None] - running_heads[:, None, :], far_below
    )
    products = jnp.einsum("tn,sn->ts", query_block, key_block, preferred_element_type=jnp.float32)
    affinity_logits = (products[None, :, :] * jnp.exp(decay_gaps)).astype(jnp.bfloat16)
    return jnp.einsum("hts,shp->thp", affinity_logits, by_head, preferred_element_type=jnp.float32)


def entry_terms(query_block, carry_state, running, doc_block, before):
    entry_weight = jnp.exp(running) * (doc_block == before).astype(jnp.float32)[:, None]
    carried = jnp.einsum(
        "tn,hpn->thp", query_block.astype(jnp.float32), carry_state, precision=lax.Precision.HIGHEST
    )
    return carried * entry_weight[:, :, None]


def body(
    features_in,
    gate_in,
    b_input,
    c_input,
    log_decay,
    row_target,
    doc_lengths,
    skip_gain,
    norm_gain,
    out_weight,
):
    tok_dev = features_in.shape[0]
    heads_here = log_decay.shape[1]
    feats = features_in.shape[1]
    width = feats // heads_here
    n_state = b_input.shape[1]
    shards = lax.axis_size(ROWS)
    capacity = tok_dev // shards
    owner = row_target // tok_dev
    local_place = row_target - owner * tok_dev
    owner_hits = (owner[:, None] == lax.broadcasted_iota(jnp.int32, (tok_dev, shards), 1)).astype(
        jnp.int32
    )
    slot_rank = jnp.sum((jnp.cumsum(owner_hits, axis=0) - owner_hits) * owner_hits, axis=1)
    slot_index = owner * capacity + slot_rank
    place_hi = (local_place // 32).astype(jnp.bfloat16)
    place_lo = (local_place % 32).astype(jnp.bfloat16)
    rows_out = jnp.concatenate(
        [features_in, gate_in, b_input, c_input, log_decay, place_hi[:, None], place_lo[:, None]],
        axis=1,
    )
    to_slot = (
        lax.broadcasted_iota(jnp.int32, (tok_dev, tok_dev), 0) == slot_index[None, :]
    ).astype(jnp.bfloat16)

    def send(values):
        packed = jnp.dot(to_slot, values, preferred_element_type=jnp.float32).astype(jnp.bfloat16)
        return lax.all_to_all(
            packed.reshape(shards, capacity, packed.shape[1]),
            ROWS,
            split_axis=0,
            concat_axis=0,
            tiled=True,
        ).reshape(tok_dev, packed.shape[1])

    moved = send(rows_out)
    columns = rows_out.shape[1]
    arrived = (
        moved[:, columns - 2].astype(jnp.int32) * 32 + moved[:, columns - 1].astype(jnp.int32)
    )
    to_place = (
        lax.broadcasted_iota(jnp.int32, (tok_dev, tok_dev), 0) == arrived[None, :]
    ).astype(jnp.bfloat16)

    def place(values):
        return jnp.dot(to_place, values, preferred_element_type=jnp.float32).astype(jnp.bfloat16)

    rows = place(moved)
    features = rows[:, :feats]
    gate_rows = rows[:, feats : 2 * feats]
    key_full = rows[:, 2 * feats : 2 * feats + n_state]
    query_full = rows[:, 2 * feats + n_state : 2 * feats + 2 * n_state]
    decays = rows[:, 2 * feats + 2 * n_state : 2 * feats + 2 * n_state + heads_here]

    doc_starts = jnp.cumsum(doc_lengths) - doc_lengths
    first_place = lax.axis_index(ROWS) * tok_dev
    blocks = tok_dev // BLOCK
    places = first_place + lax.broadcasted_iota(jnp.int32, (tok_dev,), 0)
    doc_ids = doc_index(places, doc_starts).reshape(blocks, BLOCK)
    doc_before = doc_index(
        first_place + lax.broadcasted_iota(jnp.int32, (blocks,), 0) * BLOCK - 1, doc_starts
    )
    inputs_blocks = features.reshape(blocks, BLOCK, heads_here, width)
    key_blocks = key_full.reshape(blocks, BLOCK, n_state)
    query_blocks = query_full.reshape(blocks, BLOCK, n_state)
    decay_blocks = decays.reshape(blocks, BLOCK, heads_here)

    def state_pass(carry, pieces):
        carry_state, kept_share = carry
        by_head, key_block, query_block, decay_block, doc_block, before = pieces
        block_state, through, running = state_terms(
            by_head, key_block, decay_block, doc_block, before
        )
        new_carry = (through[:, None, None] * carry_state + block_state, through * kept_share)
        return (new_carry, (block_state, through, running))

    zero_state = jnp.zeros((heads_here, width, n_state), jnp.float32)
    ones_here = jnp.ones((heads_here,), jnp.float32)
    local_carry, block_outputs = lax.scan(
        state_pass,
        (zero_state, ones_here),
        (inputs_blocks, key_blocks, query_blocks, decay_blocks, doc_ids, doc_before),
    )
    local_state, local_kept = local_carry
    block_states, throughs, runnings = (block_outputs[0], block_outputs[1], block_outputs[2])
    entry_state = exclusive_prefix(local_kept, local_state, "sc", "sz", "sx")

    def mix_pass(carry_state, pieces):
        by_head, key_block, query_block, running, doc_block, before, block_state, through = pieces
        carried = entry_terms(query_block, carry_state, running, doc_block, before)
        mixed_block = (
            inner_terms(by_head, key_block, query_block, running, doc_block)
            + carried
            + skip_gain[None, :, None] * by_head.astype(jnp.float32)
        )
        return (through[:, None, None] * carry_state + block_state, mixed_block)

    final_state, mixed = lax.scan(
        mix_pass,
        entry_state,
        (
            inputs_blocks,
            key_blocks,
            query_blocks,
            runnings,
            doc_ids,
            doc_before,
            block_states,
            throughs,
        ),
    )
    mixed = mixed.reshape(tok_dev, heads_here * width)
    gated = mixed * jax.nn.silu(gate_rows.astype(jnp.float32))
    squares = jnp.sum(gated * gated, axis=1)
    square_hi = squares.astype(jnp.bfloat16)
    square_lo = (squares - square_hi.astype(jnp.float32)).astype(jnp.bfloat16)
    unscaled = (gated * norm_gain[None, :]).astype(jnp.bfloat16)
    partial = jnp.dot(unscaled, out_weight, preferred_element_type=jnp.float32).astype(jnp.bfloat16)
    groups = lax.axis_size("head")
    chunk = tok_dev // groups
    d_model = partial.shape[1]
    extra = jnp.concatenate(
        [square_hi.reshape(groups, 1, chunk), square_lo.reshape(groups, 1, chunk)], axis=1
    )
    extra = jnp.pad(extra, ((0, 0), (0, 6), (0, d_model - chunk)))
    sent = jnp.concatenate([partial.reshape(groups, chunk, d_model), extra], axis=1)
    arrived_parts = lax.all_to_all(sent, "head", split_axis=0, concat_axis=0, tiled=True)
    summed = jnp.sum(arrived_parts.astype(jnp.float32), axis=0)
    total_squares = summed[chunk, :chunk] + summed[chunk + 1, :chunk]
    row_scale = lax.rsqrt(total_squares / (ATTENTION_LANES * HEAD_DIM) + norm_eps)
    return (summed[:chunk] * row_scale[:, None]).astype(jnp.bfloat16)


def solution(mesh):
    seq = mesh.shape["seq"]
    devices = mesh.devices.reshape(seq // 16, 8, 2, mesh.shape["head"])
    split_mesh = jax.sharding.Mesh(devices, ROWS + ("head",))
    in_specs = (
        P(ROWS, "head"),
        P(ROWS, "head"),
        P(ROWS, None),
        P(ROWS, None),
        P(ROWS, "head"),
        P(ROWS),
        P(),
        P("head"),
        P("head"),
        P("head", None),
    )
    out_specs = P(ROWS + ("head",), None)
    return jax.shard_map(
        body, mesh=split_mesh, in_specs=in_specs, out_specs=out_specs, check_vma=False
    )
```

```python
import jax
import jax.numpy as jnp
from jax import lax
from jax.sharding import PartitionSpec as P

ATTENTION_LANES = 48
ROWS = ("sx", "sz", "sc")
HEAD_DIM = 64
BLOCK = 512


far_below = -1e30
norm_eps = 1e-05


def combine(earlier, later):
    return (earlier[0] * later[0], later[0][:, None, None] * earlier[1] + later[1])


def pack_state(kept, state):
    flat = jnp.broadcast_to(kept[:, None, None], (kept.shape[0], 1, state.shape[2]))
    return jnp.concatenate([state, flat], axis=1).astype(jnp.bfloat16)


def group_weights(kept, here):
    count = kept.shape[0]
    j = lax.broadcasted_iota(jnp.int32, (count, count), 0)
    k = lax.broadcasted_iota(jnp.int32, (count, count), 1)
    ahead = lax.broadcasted_iota(jnp.int32, (count, 1), 0) < here
    between = (j < k) & (k < here)
    into_here = jnp.prod(jnp.where(between[:, :, None], kept[None, :, :], 1.0), axis=1) * ahead
    into_end = jnp.prod(jnp.where((j < k)[:, :, None], kept[None, :, :], 1.0), axis=1)
    kept_before = jnp.prod(jnp.where(ahead, kept, 1.0), axis=0)
    return into_here, into_end, kept_before, jnp.prod(kept, axis=0)


def gathered_level(kept, state, axis):
    gathered = lax.all_gather(pack_state(kept, state), axis)
    g_kept = gathered[:, :, -1, 0].astype(jnp.float32)
    into_here, into_end, kept_before, kept_all = group_weights(g_kept, lax.axis_index(axis))
    rows = state.shape[1]
    before = jnp.einsum("jh,jhpn->hpn", into_here, gathered.astype(jnp.float32))[:, :rows]
    total = jnp.einsum("jh,jhpn->hpn", into_end, gathered.astype(jnp.float32))[:, :rows]
    return before, kept_before, total, kept_all


def exclusive_prefix(kept, state, pair, line, lines):
    pair_before, pair_kept_before, pair_total, pair_kept = gathered_level(kept, state, pair)
    half = kept.shape[0] // 2
    mine = lax.axis_index(pair) * half
    part_total = lax.dynamic_slice_in_dim(pair_total, mine, half, 0)
    part_kept = lax.dynamic_slice_in_dim(pair_kept, mine, half, 0)
    line_before, line_kept_before, line_total, line_kept = gathered_level(
        part_kept, part_total, line
    )
    outer_before, _, _, _ = gathered_level(line_kept, line_total, lines)
    start_state = line_kept_before[:, None, None] * outer_before + line_before
    whole = lax.all_gather(start_state, pair, tiled=True)
    return pair_kept_before[:, None, None] * whole + pair_before


def doc_index(places, starts):
    return jnp.sum((starts[None, :] <= places[:, None]).astype(jnp.int32), axis=1) - 1


def state_terms(by_head, key_block, decay_block, doc_block, before):
    running = jnp.cumsum(decay_block.astype(jnp.float32), axis=0)
    same_doc = (doc_block == doc_block[-1]).astype(jnp.float32)
    closing_weight = jnp.exp(running[-1][None, :] - running) * same_doc[:, None]
    weighted = (key_block.astype(jnp.float32)[None, :, :] * closing_weight.T[:, :, None]).astype(
        jnp.bfloat16
    )
    block_state = jnp.einsum("hsn,shp->hpn", weighted, by_head, preferred_element_type=jnp.float32)
    through = jnp.exp(running[-1]) * (doc_block[-1] == before).astype(jnp.float32)
    return (block_state, through, running)


def inner_terms(by_head, key_block, query_block, running, doc_block):
    length = running.shape[0]
    later = lax.broadcasted_iota(jnp.int32, (length, length), 0)
    earlier = lax.broadcasted_iota(jnp.int32, (length, length), 1)
    allowed = (later >= earlier) & (doc_block[:, None] == doc_block[None, :])
    running_heads = running.T
    decay_gaps = jnp.where(
        allowed[None, :, :], running_heads[:, :, None] - running_heads[:, None, :], far_below
    )
    products = jnp.einsum("tn,sn->ts", query_block, key_block, preferred_element_type=jnp.float32)
    affinity_logits = (products[None, :, :] * jnp.exp(decay_gaps)).astype(jnp.bfloat16)
    return jnp.einsum("hts,shp->thp", affinity_logits, by_head, preferred_element_type=jnp.float32)


def entry_terms(query_block, carry_state, running, doc_block, before):
    entry_weight = jnp.exp(running) * (doc_block == before).astype(jnp.float32)[:, None]
    carried = jnp.einsum(
        "tn,hpn->thp", query_block.astype(jnp.float32), carry_state, precision=lax.Precision.HIGHEST
    )
    return carried * entry_weight[:, :, None]


def body(
    features_in,
    gate_in,
    b_input,
    c_input,
    log_decay,
    row_target,
    doc_lengths,
    skip_gain,
    norm_gain,
    out_weight,
):
    tok_dev = features_in.shape[0]
    heads_here = log_decay.shape[1]
    feats = features_in.shape[1]
    width = feats // heads_here
    n_state = b_input.shape[1]
    shards = lax.axis_size(ROWS)
    capacity = tok_dev // shards
    owner = row_target // tok_dev
    local_place = row_target - owner * tok_dev
    owner_hits = (owner[:, None] == lax.broadcasted_iota(jnp.int32, (tok_dev, shards), 1)).astype(
        jnp.int32
    )
    slot_rank = jnp.sum((jnp.cumsum(owner_hits, axis=0) - owner_hits) * owner_hits, axis=1)
    slot_index = owner * capacity + slot_rank
    place_hi = (local_place // 32).astype(jnp.bfloat16)
    place_lo = (local_place % 32).astype(jnp.bfloat16)
    rows_out = jnp.concatenate(
        [features_in, gate_in, b_input, c_input, log_decay, place_hi[:, None], place_lo[:, None]],
        axis=1,
    )
    from_slot = (
        jnp.zeros((tok_dev,), jnp.int32).at[slot_index].set(lax.iota(jnp.int32, tok_dev))
    )

    def send(values):
        packed = jnp.take(values, from_slot, axis=0, mode="clip")
        return lax.all_to_all(
            packed.reshape(shards, capacity, packed.shape[1]),
            ROWS,
            split_axis=0,
            concat_axis=0,
            tiled=True,
        ).reshape(tok_dev, packed.shape[1])

    moved = send(rows_out)
    columns = rows_out.shape[1]
    arrived = (
        moved[:, columns - 2].astype(jnp.int32) * 32 + moved[:, columns - 1].astype(jnp.int32)
    )
    from_place = jnp.zeros((tok_dev,), jnp.int32).at[arrived].set(lax.iota(jnp.int32, tok_dev))

    def place(values):
        return jnp.take(values, from_place, axis=0, mode="clip")

    rows = place(moved)
    features = rows[:, :feats]
    gate_rows = rows[:, feats : 2 * feats]
    key_full = rows[:, 2 * feats : 2 * feats + n_state]
    query_full = rows[:, 2 * feats + n_state : 2 * feats + 2 * n_state]
    decays = rows[:, 2 * feats + 2 * n_state : 2 * feats + 2 * n_state + heads_here]

    doc_starts = jnp.cumsum(doc_lengths) - doc_lengths
    first_place = lax.axis_index(ROWS) * tok_dev
    blocks = tok_dev // BLOCK
    places = first_place + lax.broadcasted_iota(jnp.int32, (tok_dev,), 0)
    doc_ids = doc_index(places, doc_starts).reshape(blocks, BLOCK)
    doc_before = doc_index(
        first_place + lax.broadcasted_iota(jnp.int32, (blocks,), 0) * BLOCK - 1, doc_starts
    )
    inputs_blocks = features.reshape(blocks, BLOCK, heads_here, width)
    key_blocks = key_full.reshape(blocks, BLOCK, n_state)
    query_blocks = query_full.reshape(blocks, BLOCK, n_state)
    decay_blocks = decays.reshape(blocks, BLOCK, heads_here)

    def state_pass(carry, pieces):
        carry_state, kept_share = carry
        by_head, key_block, query_block, decay_block, doc_block, before = pieces
        block_state, through, running = state_terms(
            by_head, key_block, decay_block, doc_block, before
        )
        new_carry = (through[:, None, None] * carry_state + block_state, through * kept_share)
        return (new_carry, (block_state, through, running))

    zero_state = jnp.zeros((heads_here, width, n_state), jnp.float32)
    ones_here = jnp.ones((heads_here,), jnp.float32)
    local_carry, block_outputs = lax.scan(
        state_pass,
        (zero_state, ones_here),
        (inputs_blocks, key_blocks, query_blocks, decay_blocks, doc_ids, doc_before),
    )
    local_state, local_kept = local_carry
    block_states, throughs, runnings = (block_outputs[0], block_outputs[1], block_outputs[2])
    entry_state = exclusive_prefix(local_kept, local_state, "sc", "sz", "sx")

    def mix_pass(carry_state, pieces):
        by_head, key_block, query_block, running, doc_block, before, block_state, through = pieces
        carried = entry_terms(query_block, carry_state, running, doc_block, before)
        mixed_block = (
            inner_terms(by_head, key_block, query_block, running, doc_block)
            + carried
            + skip_gain[None, :, None] * by_head.astype(jnp.float32)
        )
        return (through[:, None, None] * carry_state + block_state, mixed_block)

    final_state, mixed = lax.scan(
        mix_pass,
        entry_state,
        (
            inputs_blocks,
            key_blocks,
            query_blocks,
            runnings,
            doc_ids,
            doc_before,
            block_states,
            throughs,
        ),
    )
    mixed = mixed.reshape(tok_dev, heads_here * width)
    gated = mixed * jax.nn.silu(gate_rows.astype(jnp.float32))
    squares = jnp.sum(gated * gated, axis=1)
    square_hi = squares.astype(jnp.bfloat16)
    square_lo = (squares - square_hi.astype(jnp.float32)).astype(jnp.bfloat16)
    unscaled = (gated * norm_gain[None, :]).astype(jnp.bfloat16)
    partial = jnp.dot(unscaled, out_weight, preferred_element_type=jnp.float32).astype(jnp.bfloat16)
    groups = lax.axis_size("head")
    chunk = tok_dev // groups
    d_model = partial.shape[1]
    extra = jnp.concatenate(
        [square_hi.reshape(groups, 1, chunk), square_lo.reshape(groups, 1, chunk)], axis=1
    )
    extra = jnp.pad(extra, ((0, 0), (0, 6), (0, d_model - chunk)))
    sent = jnp.concatenate([partial.reshape(groups, chunk, d_model), extra], axis=1)
    arrived_parts = lax.all_to_all(sent, "head", split_axis=0, concat_axis=0, tiled=True)
    summed = jnp.sum(arrived_parts.astype(jnp.float32), axis=0)
    total_squares = summed[chunk, :chunk] + summed[chunk + 1, :chunk]
    row_scale = lax.rsqrt(total_squares / (ATTENTION_LANES * HEAD_DIM) + norm_eps)
    return (summed[:chunk] * row_scale[:, None]).astype(jnp.bfloat16)


def solution(mesh):
    seq = mesh.shape["seq"]
    devices = mesh.devices.reshape(seq // 16, 8, 2, mesh.shape["head"])
    split_mesh = jax.sharding.Mesh(devices, ROWS + ("head",))
    in_specs = (
        P(ROWS, "head"),
        P(ROWS, "head"),
        P(ROWS, None),
        P(ROWS, None),
        P(ROWS, "head"),
        P(ROWS),
        P(),
        P("head"),
        P("head"),
        P("head", None),
    )
    out_specs = P(ROWS + ("head",), None)
    return jax.shard_map(
        body, mesh=split_mesh, in_specs=in_specs, out_specs=out_specs, check_vma=False
    )
```

```python
import jax
import jax.numpy as jnp
from jax import lax
from jax.sharding import PartitionSpec as P

ATTENTION_LANES = 48
ROWS = ("sx", "zh", "zl", "sc")
LEVELS = ("zl", "zh", "sx")
HEAD_DIM = 64
BLOCK = 512


far_below = -1e30
norm_eps = 1e-05


def combine(earlier, later):
    return (earlier[0] * later[0], later[0][:, None, None] * earlier[1] + later[1])


def pack_state(kept, state):
    flat = jnp.broadcast_to(kept[:, None, None], (kept.shape[0], 1, state.shape[2]))
    return jnp.concatenate([state, flat], axis=1).astype(jnp.bfloat16)


def group_weights(kept, here):
    count = kept.shape[0]
    j = lax.broadcasted_iota(jnp.int32, (count, count), 0)
    k = lax.broadcasted_iota(jnp.int32, (count, count), 1)
    ahead = lax.broadcasted_iota(jnp.int32, (count, 1), 0) < here
    between = (j < k) & (k < here)
    into_here = jnp.prod(jnp.where(between[:, :, None], kept[None, :, :], 1.0), axis=1) * ahead
    into_end = jnp.prod(jnp.where((j < k)[:, :, None], kept[None, :, :], 1.0), axis=1)
    kept_before = jnp.prod(jnp.where(ahead, kept, 1.0), axis=0)
    return into_here, into_end, kept_before, jnp.prod(kept, axis=0)


def gathered_level(kept, state, axis):
    gathered = lax.all_gather(pack_state(kept, state), axis)
    g_kept = gathered[:, :, -1, 0].astype(jnp.float32)
    into_here, into_end, kept_before, kept_all = group_weights(g_kept, lax.axis_index(axis))
    rows = state.shape[1]
    before = jnp.einsum("jh,jhpn->hpn", into_here, gathered.astype(jnp.float32))[:, :rows]
    total = jnp.einsum("jh,jhpn->hpn", into_end, gathered.astype(jnp.float32))[:, :rows]
    return before, kept_before, total, kept_all


def exclusive_prefix(kept, state, pair, levels):
    pair_before, pair_kept_before, pair_total, pair_kept = gathered_level(kept, state, pair)
    half = kept.shape[0] // 2
    mine = lax.axis_index(pair) * half
    part_total = lax.dynamic_slice_in_dim(pair_total, mine, half, 0)
    part_kept = lax.dynamic_slice_in_dim(pair_kept, mine, half, 0)
    found = []
    for axis in levels:
        before, kept_before, part_total, part_kept = gathered_level(part_kept, part_total, axis)
        found.append((before, kept_before))
    start_state = found[-1][0]
    for before, kept_before in reversed(found[:-1]):
        start_state = kept_before[:, None, None] * start_state + before
    whole = lax.all_gather(start_state, pair, tiled=True)
    return pair_kept_before[:, None, None] * whole + pair_before


def doc_index(places, starts):
    return jnp.sum((starts[None, :] <= places[:, None]).astype(jnp.int32), axis=1) - 1


def state_terms(by_head, key_block, decay_block, doc_block, before):
    running = jnp.cumsum(decay_block.astype(jnp.float32), axis=0)
    same_doc = (doc_block == doc_block[-1]).astype(jnp.float32)
    closing_weight = jnp.exp(running[-1][None, :] - running) * same_doc[:, None]
    weighted = (key_block.astype(jnp.float32)[None, :, :] * closing_weight.T[:, :, None]).astype(
        jnp.bfloat16
    )
    block_state = jnp.einsum("hsn,shp->hpn", weighted, by_head, preferred_element_type=jnp.float32)
    through = jnp.exp(running[-1]) * (doc_block[-1] == before).astype(jnp.float32)
    return (block_state, through, running)


def inner_terms(by_head, key_block, query_block, running, doc_block):
    length = running.shape[0]
    later = lax.broadcasted_iota(jnp.int32, (length, length), 0)
    earlier = lax.broadcasted_iota(jnp.int32, (length, length), 1)
    allowed = (later >= earlier) & (doc_block[:, None] == doc_block[None, :])
    running_heads = running.T
    decay_gaps = jnp.where(
        allowed[None, :, :], running_heads[:, :, None] - running_heads[:, None, :], far_below
    )
    products = jnp.einsum("tn,sn->ts", query_block, key_block, preferred_element_type=jnp.float32)
    affinity_logits = (products[None, :, :] * jnp.exp(decay_gaps)).astype(jnp.bfloat16)
    return jnp.einsum("hts,shp->thp", affinity_logits, by_head, preferred_element_type=jnp.float32)


def entry_terms(query_block, carry_state, running, doc_block, before):
    entry_weight = jnp.exp(running) * (doc_block == before).astype(jnp.float32)[:, None]
    carried = jnp.einsum(
        "tn,hpn->thp", query_block.astype(jnp.float32), carry_state, precision=lax.Precision.HIGHEST
    )
    return carried * entry_weight[:, :, None]


def body(
    features_in,
    gate_in,
    b_input,
    c_input,
    log_decay,
    row_target,
    doc_lengths,
    skip_gain,
    norm_gain,
    out_weight,
):
    tok_dev = features_in.shape[0]
    heads_here = log_decay.shape[1]
    feats = features_in.shape[1]
    width = feats // heads_here
    n_state = b_input.shape[1]
    shards = lax.axis_size(ROWS)
    capacity = tok_dev // shards
    owner = row_target // tok_dev
    local_place = row_target - owner * tok_dev
    owner_hits = (owner[:, None] == lax.broadcasted_iota(jnp.int32, (tok_dev, shards), 1)).astype(
        jnp.int32
    )
    slot_rank = jnp.sum((jnp.cumsum(owner_hits, axis=0) - owner_hits) * owner_hits, axis=1)
    slot_index = owner * capacity + slot_rank
    place_hi = (local_place // 32).astype(jnp.bfloat16)
    place_lo = (local_place % 32).astype(jnp.bfloat16)
    rows_out = jnp.concatenate(
        [features_in, gate_in, b_input, c_input, log_decay, place_hi[:, None], place_lo[:, None]],
        axis=1,
    )
    to_slot = (
        lax.broadcasted_iota(jnp.int32, (tok_dev, tok_dev), 0) == slot_index[None, :]
    ).astype(jnp.bfloat16)

    def send(values):
        packed = jnp.dot(to_slot, values, preferred_element_type=jnp.float32).astype(jnp.bfloat16)
        return lax.all_to_all(
            packed.reshape(shards, capacity, packed.shape[1]),
            ROWS,
            split_axis=0,
            concat_axis=0,
            tiled=True,
        ).reshape(tok_dev, packed.shape[1])

    moved = send(rows_out)
    columns = rows_out.shape[1]
    arrived = (
        moved[:, columns - 2].astype(jnp.int32) * 32 + moved[:, columns - 1].astype(jnp.int32)
    )
    to_place = (
        lax.broadcasted_iota(jnp.int32, (tok_dev, tok_dev), 0) == arrived[None, :]
    ).astype(jnp.bfloat16)

    def place(values):
        return jnp.dot(to_place, values, preferred_element_type=jnp.float32).astype(jnp.bfloat16)

    rows = place(moved)
    features = rows[:, :feats]
    gate_rows = rows[:, feats : 2 * feats]
    key_full = rows[:, 2 * feats : 2 * feats + n_state]
    query_full = rows[:, 2 * feats + n_state : 2 * feats + 2 * n_state]
    decays = rows[:, 2 * feats + 2 * n_state : 2 * feats + 2 * n_state + heads_here]

    doc_starts = jnp.cumsum(doc_lengths) - doc_lengths
    first_place = lax.axis_index(ROWS) * tok_dev
    blocks = tok_dev // BLOCK
    places = first_place + lax.broadcasted_iota(jnp.int32, (tok_dev,), 0)
    doc_ids = doc_index(places, doc_starts).reshape(blocks, BLOCK)
    doc_before = doc_index(
        first_place + lax.broadcasted_iota(jnp.int32, (blocks,), 0) * BLOCK - 1, doc_starts
    )
    inputs_blocks = features.reshape(blocks, BLOCK, heads_here, width)
    key_blocks = key_full.reshape(blocks, BLOCK, n_state)
    query_blocks = query_full.reshape(blocks, BLOCK, n_state)
    decay_blocks = decays.reshape(blocks, BLOCK, heads_here)

    def state_pass(carry, pieces):
        carry_state, kept_share = carry
        by_head, key_block, query_block, decay_block, doc_block, before = pieces
        block_state, through, running = state_terms(
            by_head, key_block, decay_block, doc_block, before
        )
        new_carry = (through[:, None, None] * carry_state + block_state, through * kept_share)
        return (new_carry, (block_state, through, running))

    zero_state = jnp.zeros((heads_here, width, n_state), jnp.float32)
    ones_here = jnp.ones((heads_here,), jnp.float32)
    local_carry, block_outputs = lax.scan(
        state_pass,
        (zero_state, ones_here),
        (inputs_blocks, key_blocks, query_blocks, decay_blocks, doc_ids, doc_before),
    )
    local_state, local_kept = local_carry
    block_states, throughs, runnings = (block_outputs[0], block_outputs[1], block_outputs[2])
    entry_state = exclusive_prefix(local_kept, local_state, "sc", LEVELS)

    def mix_pass(carry_state, pieces):
        by_head, key_block, query_block, running, doc_block, before, block_state, through = pieces
        carried = entry_terms(query_block, carry_state, running, doc_block, before)
        mixed_block = (
            inner_terms(by_head, key_block, query_block, running, doc_block)
            + carried
            + skip_gain[None, :, None] * by_head.astype(jnp.float32)
        )
        return (through[:, None, None] * carry_state + block_state, mixed_block)

    final_state, mixed = lax.scan(
        mix_pass,
        entry_state,
        (
            inputs_blocks,
            key_blocks,
            query_blocks,
            runnings,
            doc_ids,
            doc_before,
            block_states,
            throughs,
        ),
    )
    mixed = mixed.reshape(tok_dev, heads_here * width)
    gated = mixed * jax.nn.silu(gate_rows.astype(jnp.float32))
    squares = jnp.sum(gated * gated, axis=1)
    square_hi = squares.astype(jnp.bfloat16)
    square_lo = (squares - square_hi.astype(jnp.float32)).astype(jnp.bfloat16)
    unscaled = (gated * norm_gain[None, :]).astype(jnp.bfloat16)
    partial = jnp.dot(unscaled, out_weight, preferred_element_type=jnp.float32).astype(jnp.bfloat16)
    groups = lax.axis_size("head")
    chunk = tok_dev // groups
    d_model = partial.shape[1]
    extra = jnp.concatenate(
        [square_hi.reshape(groups, 1, chunk), square_lo.reshape(groups, 1, chunk)], axis=1
    )
    extra = jnp.pad(extra, ((0, 0), (0, 6), (0, d_model - chunk)))
    sent = jnp.concatenate([partial.reshape(groups, chunk, d_model), extra], axis=1)
    arrived_parts = lax.all_to_all(sent, "head", split_axis=0, concat_axis=0, tiled=True)
    summed = jnp.sum(arrived_parts.astype(jnp.float32), axis=0)
    total_squares = summed[chunk, :chunk] + summed[chunk + 1, :chunk]
    row_scale = lax.rsqrt(total_squares / (ATTENTION_LANES * HEAD_DIM) + norm_eps)
    return (summed[:chunk] * row_scale[:, None]).astype(jnp.bfloat16)


def solution(mesh):
    seq = mesh.shape["seq"]
    devices = mesh.devices.reshape(seq // 16, 4, 2, 2, mesh.shape["head"])
    split_mesh = jax.sharding.Mesh(devices, ROWS + ("head",))
    in_specs = (
        P(ROWS, "head"),
        P(ROWS, "head"),
        P(ROWS, None),
        P(ROWS, None),
        P(ROWS, "head"),
        P(ROWS),
        P(),
        P("head"),
        P("head"),
        P("head", None),
    )
    out_specs = P(ROWS + ("head",), None)
    return jax.shard_map(
        body, mesh=split_mesh, in_specs=in_specs, out_specs=out_specs, check_vma=False
    )
```

```python
import jax
import jax.numpy as jnp
from jax import lax
from jax.sharding import PartitionSpec as P

ATTENTION_LANES = 48
ROWS = ("sx", "sz", "sc")
HEAD_DIM = 64
BLOCK = 512


far_below = -1e30
norm_eps = 1e-05


def combine(earlier, later):
    return (earlier[0] * later[0], later[0][:, None, None] * earlier[1] + later[1])


def pack_state(kept, state):
    flat = jnp.broadcast_to(kept[:, None, None], (kept.shape[0], 1, state.shape[2]))
    return jnp.concatenate([state, flat], axis=1).astype(jnp.bfloat16)


def group_weights(kept, here):
    count = kept.shape[0]
    j = lax.broadcasted_iota(jnp.int32, (count, count), 0)
    k = lax.broadcasted_iota(jnp.int32, (count, count), 1)
    ahead = lax.broadcasted_iota(jnp.int32, (count, 1), 0) < here
    between = (j < k) & (k < here)
    into_here = jnp.prod(jnp.where(between[:, :, None], kept[None, :, :], 1.0), axis=1) * ahead
    into_end = jnp.prod(jnp.where((j < k)[:, :, None], kept[None, :, :], 1.0), axis=1)
    kept_before = jnp.prod(jnp.where(ahead, kept, 1.0), axis=0)
    return into_here, into_end, kept_before, jnp.prod(kept, axis=0)


def gathered_level(kept, state, axis):
    gathered = lax.all_gather(pack_state(kept, state), axis)
    g_kept = gathered[:, :, -1, 0].astype(jnp.float32)
    into_here, into_end, kept_before, kept_all = group_weights(g_kept, lax.axis_index(axis))
    rows = state.shape[1]
    before = jnp.einsum("jh,jhpn->hpn", into_here, gathered.astype(jnp.float32))[:, :rows]
    total = jnp.einsum("jh,jhpn->hpn", into_end, gathered.astype(jnp.float32))[:, :rows]
    return before, kept_before, total, kept_all


def exclusive_prefix(kept, state, pair, line, lines):
    pair_before, pair_kept_before, pair_total, pair_kept = gathered_level(kept, state, pair)
    half = kept.shape[0] // 2
    mine = lax.axis_index(pair) * half
    part_total = lax.dynamic_slice_in_dim(pair_total, mine, half, 0)
    part_kept = lax.dynamic_slice_in_dim(pair_kept, mine, half, 0)
    line_before, line_kept_before, line_total, line_kept = gathered_level(
        part_kept, part_total, line
    )
    outer_before, _, _, _ = gathered_level(line_kept, line_total, lines)
    start_state = line_kept_before[:, None, None] * outer_before + line_before
    whole = lax.all_gather(start_state, pair, tiled=True)
    return pair_kept_before[:, None, None] * whole + pair_before


def doc_index(places, starts):
    return jnp.sum((starts[None, :] <= places[:, None]).astype(jnp.int32), axis=1) - 1


def state_terms(by_head, key_block, decay_block, doc_block, before):
    running = jnp.cumsum(decay_block.astype(jnp.float32), axis=0)
    same_doc = (doc_block == doc_block[-1]).astype(jnp.float32)
    closing_weight = jnp.exp(running[-1][None, :] - running) * same_doc[:, None]
    weighted = (key_block.astype(jnp.float32)[None, :, :] * closing_weight.T[:, :, None]).astype(
        jnp.bfloat16
    )
    block_state = jnp.einsum("hsn,shp->hpn", weighted, by_head, preferred_element_type=jnp.float32)
    through = jnp.exp(running[-1]) * (doc_block[-1] == before).astype(jnp.float32)
    return (block_state, through, running)


def inner_terms(by_head, key_block, query_block, running, doc_block):
    length = running.shape[0]
    later = lax.broadcasted_iota(jnp.int32, (length, length), 0)
    earlier = lax.broadcasted_iota(jnp.int32, (length, length), 1)
    allowed = (later >= earlier) & (doc_block[:, None] == doc_block[None, :])
    running_heads = running.T
    decay_gaps = jnp.where(
        allowed[None, :, :], running_heads[:, :, None] - running_heads[:, None, :], far_below
    )
    products = jnp.einsum("tn,sn->ts", query_block, key_block, preferred_element_type=jnp.float32)
    affinity_logits = (products[None, :, :] * jnp.exp(decay_gaps)).astype(jnp.bfloat16)
    return jnp.einsum("hts,shp->thp", affinity_logits, by_head, preferred_element_type=jnp.float32)


def entry_terms(query_block, carry_state, running, doc_block, before):
    entry_weight = jnp.exp(running) * (doc_block == before).astype(jnp.float32)[:, None]
    carried = jnp.einsum(
        "tn,hpn->thp", query_block.astype(jnp.float32), carry_state, precision=lax.Precision.HIGHEST
    )
    return carried * entry_weight[:, :, None]


def body(
    features_in,
    gate_in,
    b_input,
    c_input,
    log_decay,
    row_target,
    doc_lengths,
    skip_gain,
    norm_gain,
    out_weight,
):
    tok_dev = features_in.shape[0]
    heads_here = log_decay.shape[1]
    feats = features_in.shape[1]
    width = feats // heads_here
    n_state = b_input.shape[1]
    shards = lax.axis_size(ROWS)
    capacity = tok_dev // shards
    owner = row_target // tok_dev
    local_place = row_target - owner * tok_dev
    owner_hits = (owner[:, None] == lax.broadcasted_iota(jnp.int32, (tok_dev, shards), 1)).astype(
        jnp.int32
    )
    slot_rank = jnp.sum((jnp.cumsum(owner_hits, axis=0) - owner_hits) * owner_hits, axis=1)
    slot_index = owner * capacity + slot_rank
    place_hi = (local_place // 32).astype(jnp.bfloat16)
    place_lo = (local_place % 32).astype(jnp.bfloat16)
    pieces = [features_in, gate_in, b_input, c_input, log_decay, place_hi[:, None], place_lo[:, None]]
    to_slot = (
        lax.broadcasted_iota(jnp.int32, (tok_dev, tok_dev), 0) == slot_index[None, :]
    ).astype(jnp.bfloat16)

    def send(values):
        packed = jnp.concatenate(
            [
                jnp.dot(to_slot, v, preferred_element_type=jnp.float32).astype(jnp.bfloat16)
                for v in values
            ],
            axis=1,
        )
        return lax.all_to_all(
            packed.reshape(shards, capacity, packed.shape[1]),
            ROWS,
            split_axis=0,
            concat_axis=0,
            tiled=True,
        ).reshape(tok_dev, packed.shape[1])

    rows_out = jnp.concatenate(pieces[4:], axis=1)
    pieces = pieces[:4] + [rows_out]
    moved = send(pieces)
    columns = moved.shape[1]
    arrived = (
        moved[:, columns - 2].astype(jnp.int32) * 32 + moved[:, columns - 1].astype(jnp.int32)
    )
    to_place = (
        lax.broadcasted_iota(jnp.int32, (tok_dev, tok_dev), 0) == arrived[None, :]
    ).astype(jnp.bfloat16)

    def place(values):
        return jnp.dot(to_place, values, preferred_element_type=jnp.float32).astype(jnp.bfloat16)

    rows = place(moved)
    features = rows[:, :feats]
    gate_rows = rows[:, feats : 2 * feats]
    key_full = rows[:, 2 * feats : 2 * feats + n_state]
    query_full = rows[:, 2 * feats + n_state : 2 * feats + 2 * n_state]
    decays = rows[:, 2 * feats + 2 * n_state : 2 * feats + 2 * n_state + heads_here]

    doc_starts = jnp.cumsum(doc_lengths) - doc_lengths
    first_place = lax.axis_index(ROWS) * tok_dev
    blocks = tok_dev // BLOCK
    places = first_place + lax.broadcasted_iota(jnp.int32, (tok_dev,), 0)
    doc_ids = doc_index(places, doc_starts).reshape(blocks, BLOCK)
    doc_before = doc_index(
        first_place + lax.broadcasted_iota(jnp.int32, (blocks,), 0) * BLOCK - 1, doc_starts
    )
    inputs_blocks = features.reshape(blocks, BLOCK, heads_here, width)
    key_blocks = key_full.reshape(blocks, BLOCK, n_state)
    query_blocks = query_full.reshape(blocks, BLOCK, n_state)
    decay_blocks = decays.reshape(blocks, BLOCK, heads_here)

    def state_pass(carry, pieces):
        carry_state, kept_share = carry
        by_head, key_block, query_block, decay_block, doc_block, before = pieces
        block_state, through, running = state_terms(
            by_head, key_block, decay_block, doc_block, before
        )
        new_carry = (through[:, None, None] * carry_state + block_state, through * kept_share)
        return (new_carry, (block_state, through, running))

    zero_state = jnp.zeros((heads_here, width, n_state), jnp.float32)
    ones_here = jnp.ones((heads_here,), jnp.float32)
    local_carry, block_outputs = lax.scan(
        state_pass,
        (zero_state, ones_here),
        (inputs_blocks, key_blocks, query_blocks, decay_blocks, doc_ids, doc_before),
    )
    local_state, local_kept = local_carry
    block_states, throughs, runnings = (block_outputs[0], block_outputs[1], block_outputs[2])
    entry_state = exclusive_prefix(local_kept, local_state, "sc", "sz", "sx")

    def mix_pass(carry_state, pieces):
        by_head, key_block, query_block, running, doc_block, before, block_state, through = pieces
        carried = entry_terms(query_block, carry_state, running, doc_block, before)
        mixed_block = (
            inner_terms(by_head, key_block, query_block, running, doc_block)
            + carried
            + skip_gain[None, :, None] * by_head.astype(jnp.float32)
        )
        return (through[:, None, None] * carry_state + block_state, mixed_block)

    final_state, mixed = lax.scan(
        mix_pass,
        entry_state,
        (
            inputs_blocks,
            key_blocks,
            query_blocks,
            runnings,
            doc_ids,
            doc_before,
            block_states,
            throughs,
        ),
    )
    mixed = mixed.reshape(tok_dev, heads_here * width)
    gated = mixed * jax.nn.silu(gate_rows.astype(jnp.float32))
    squares = jnp.sum(gated * gated, axis=1)
    square_hi = squares.astype(jnp.bfloat16)
    square_lo = (squares - square_hi.astype(jnp.float32)).astype(jnp.bfloat16)
    unscaled = (gated * norm_gain[None, :]).astype(jnp.bfloat16)
    partial = jnp.dot(unscaled, out_weight, preferred_element_type=jnp.float32).astype(jnp.bfloat16)
    groups = lax.axis_size("head")
    chunk = tok_dev // groups
    d_model = partial.shape[1]
    extra = jnp.concatenate(
        [square_hi.reshape(groups, 1, chunk), square_lo.reshape(groups, 1, chunk)], axis=1
    )
    extra = jnp.pad(extra, ((0, 0), (0, 6), (0, d_model - chunk)))
    sent = jnp.concatenate([partial.reshape(groups, chunk, d_model), extra], axis=1)
    arrived_parts = lax.all_to_all(sent, "head", split_axis=0, concat_axis=0, tiled=True)
    summed = jnp.sum(arrived_parts.astype(jnp.float32), axis=0)
    total_squares = summed[chunk, :chunk] + summed[chunk + 1, :chunk]
    row_scale = lax.rsqrt(total_squares / (ATTENTION_LANES * HEAD_DIM) + norm_eps)
    return (summed[:chunk] * row_scale[:, None]).astype(jnp.bfloat16)


def solution(mesh):
    seq = mesh.shape["seq"]
    devices = mesh.devices.reshape(seq // 16, 8, 2, mesh.shape["head"])
    split_mesh = jax.sharding.Mesh(devices, ROWS + ("head",))
    in_specs = (
        P(ROWS, "head"),
        P(ROWS, "head"),
        P(ROWS, None),
        P(ROWS, None),
        P(ROWS, "head"),
        P(ROWS),
        P(),
        P("head"),
        P("head"),
        P("head", None),
    )
    out_specs = P(ROWS + ("head",), None)
    return jax.shard_map(
        body, mesh=split_mesh, in_specs=in_specs, out_specs=out_specs, check_vma=False
    )
```

```python
import jax
import jax.numpy as jnp
from jax import lax
from jax.sharding import PartitionSpec as P

ATTENTION_LANES = 48
ROWS = ("sx", "sz", "sc")
HEAD_DIM = 64
BLOCK = 512


far_below = -1e30
norm_eps = 1e-05


def combine(earlier, later):
    return (earlier[0] * later[0], later[0][:, None, None] * earlier[1] + later[1])


def pack_state(kept, state):
    flat = jnp.broadcast_to(kept[:, None, None], (kept.shape[0], 1, state.shape[2]))
    return jnp.concatenate([state, flat], axis=1).astype(jnp.bfloat16)


def group_weights(kept, here):
    count = kept.shape[0]
    j = lax.broadcasted_iota(jnp.int32, (count, count), 0)
    k = lax.broadcasted_iota(jnp.int32, (count, count), 1)
    ahead = lax.broadcasted_iota(jnp.int32, (count, 1), 0) < here
    between = (j < k) & (k < here)
    into_here = jnp.prod(jnp.where(between[:, :, None], kept[None, :, :], 1.0), axis=1) * ahead
    into_end = jnp.prod(jnp.where((j < k)[:, :, None], kept[None, :, :], 1.0), axis=1)
    kept_before = jnp.prod(jnp.where(ahead, kept, 1.0), axis=0)
    return into_here, into_end, kept_before, jnp.prod(kept, axis=0)


def gathered_level(kept, state, axis):
    gathered = lax.all_gather(pack_state(kept, state), axis)
    g_kept = gathered[:, :, -1, 0].astype(jnp.float32)
    into_here, into_end, kept_before, kept_all = group_weights(g_kept, lax.axis_index(axis))
    rows = state.shape[1]
    before = jnp.einsum("jh,jhpn->hpn", into_here, gathered.astype(jnp.float32))[:, :rows]
    total = jnp.einsum("jh,jhpn->hpn", into_end, gathered.astype(jnp.float32))[:, :rows]
    return before, kept_before, total, kept_all


def exclusive_prefix(kept, state, pair, line, lines):
    pair_before, pair_kept_before, pair_total, pair_kept = gathered_level(kept, state, pair)
    half = kept.shape[0] // 2
    mine = lax.axis_index(pair) * half
    part_total = lax.dynamic_slice_in_dim(pair_total, mine, half, 0)
    part_kept = lax.dynamic_slice_in_dim(pair_kept, mine, half, 0)
    line_before, line_kept_before, line_total, line_kept = gathered_level(
        part_kept, part_total, line
    )
    outer_before, _, _, _ = gathered_level(line_kept, line_total, lines)
    start_state = line_kept_before[:, None, None] * outer_before + line_before
    whole = lax.all_gather(start_state, pair, tiled=True)
    return pair_kept_before[:, None, None] * whole + pair_before


def doc_index(places, starts):
    return jnp.sum((starts[None, :] <= places[:, None]).astype(jnp.int32), axis=1) - 1


def state_terms(by_head, key_block, decay_block, doc_block, before):
    running = jnp.cumsum(decay_block.astype(jnp.float32), axis=0)
    same_doc = (doc_block == doc_block[-1]).astype(jnp.float32)
    closing_weight = jnp.exp(running[-1][None, :] - running) * same_doc[:, None]
    weighted = (key_block.astype(jnp.float32)[None, :, :] * closing_weight.T[:, :, None]).astype(
        jnp.bfloat16
    )
    block_state = jnp.einsum("hsn,shp->hpn", weighted, by_head, preferred_element_type=jnp.float32)
    through = jnp.exp(running[-1]) * (doc_block[-1] == before).astype(jnp.float32)
    return (block_state, through, running)


def inner_terms(by_head, key_block, query_block, running, doc_block):
    length = running.shape[0]
    later = lax.broadcasted_iota(jnp.int32, (length, length), 0)
    earlier = lax.broadcasted_iota(jnp.int32, (length, length), 1)
    allowed = (later >= earlier) & (doc_block[:, None] == doc_block[None, :])
    running_heads = running.T
    decay_gaps = jnp.where(
        allowed[None, :, :], running_heads[:, :, None] - running_heads[:, None, :], far_below
    )
    products = jnp.einsum("tn,sn->ts", query_block, key_block, preferred_element_type=jnp.float32)
    affinity_logits = (products[None, :, :] * jnp.exp(decay_gaps)).astype(jnp.bfloat16)
    return jnp.einsum("hts,shp->thp", affinity_logits, by_head, preferred_element_type=jnp.float32)


def entry_terms(query_block, carry_state, running, doc_block, before):
    entry_weight = jnp.exp(running) * (doc_block == before).astype(jnp.float32)[:, None]
    carried = jnp.einsum(
        "tn,hpn->thp", query_block.astype(jnp.float32), carry_state, precision=lax.Precision.HIGHEST
    )
    return carried * entry_weight[:, :, None]


def body(
    features_in,
    gate_in,
    b_input,
    c_input,
    log_decay,
    row_target,
    doc_lengths,
    skip_gain,
    norm_gain,
    out_weight,
):
    tok_dev = features_in.shape[0]
    heads_here = log_decay.shape[1]
    feats = features_in.shape[1]
    width = feats // heads_here
    n_state = b_input.shape[1]
    shards = lax.axis_size(ROWS)
    capacity = tok_dev // shards
    owner = row_target // tok_dev
    local_place = row_target - owner * tok_dev
    owner_hits = (owner[:, None] == lax.broadcasted_iota(jnp.int32, (tok_dev, shards), 1)).astype(
        jnp.int32
    )
    slot_rank = jnp.sum((jnp.cumsum(owner_hits, axis=0) - owner_hits) * owner_hits, axis=1)
    slot_index = owner * capacity + slot_rank
    place_hi = (local_place // 32).astype(jnp.bfloat16)
    place_lo = (local_place % 32).astype(jnp.bfloat16)
    pieces = [features_in, gate_in, b_input, c_input, log_decay, place_hi[:, None], place_lo[:, None]]
    to_slot = (
        lax.broadcasted_iota(jnp.int32, (tok_dev, tok_dev), 0) == slot_index[None, :]
    ).astype(jnp.bfloat16)

    def send(values):
        packed = jnp.concatenate(
            [
                jnp.dot(to_slot, v, preferred_element_type=jnp.float32).astype(jnp.bfloat16)
                for v in values
            ],
            axis=1,
        )
        return lax.all_to_all(
            packed.reshape(shards, capacity, packed.shape[1]),
            ROWS,
            split_axis=0,
            concat_axis=0,
            tiled=True,
        ).reshape(tok_dev, packed.shape[1])

    rows_out = jnp.concatenate(pieces[4:], axis=1)
    pieces = pieces[:4] + [rows_out]
    moved = send(pieces)
    columns = moved.shape[1]
    arrived = (
        moved[:, columns - 2].astype(jnp.int32) * 32 + moved[:, columns - 1].astype(jnp.int32)
    )
    to_place = (
        lax.broadcasted_iota(jnp.int32, (tok_dev, tok_dev), 0) == arrived[None, :]
    ).astype(jnp.bfloat16)

    def place(values):
        return jnp.dot(to_place, values, preferred_element_type=jnp.float32).astype(jnp.bfloat16)

    features = place(moved[:, :feats])
    gate_rows = place(moved[:, feats : 2 * feats])
    key_full = place(moved[:, 2 * feats : 2 * feats + n_state])
    query_full = place(moved[:, 2 * feats + n_state : 2 * feats + 2 * n_state])
    decays = place(moved[:, 2 * feats + 2 * n_state : 2 * feats + 2 * n_state + heads_here])

    doc_starts = jnp.cumsum(doc_lengths) - doc_lengths
    first_place = lax.axis_index(ROWS) * tok_dev
    blocks = tok_dev // BLOCK
    places = first_place + lax.broadcasted_iota(jnp.int32, (tok_dev,), 0)
    doc_ids = doc_index(places, doc_starts).reshape(blocks, BLOCK)
    doc_before = doc_index(
        first_place + lax.broadcasted_iota(jnp.int32, (blocks,), 0) * BLOCK - 1, doc_starts
    )
    inputs_blocks = features.reshape(blocks, BLOCK, heads_here, width)
    key_blocks = key_full.reshape(blocks, BLOCK, n_state)
    query_blocks = query_full.reshape(blocks, BLOCK, n_state)
    decay_blocks = decays.reshape(blocks, BLOCK, heads_here)

    def state_pass(carry, pieces):
        carry_state, kept_share = carry
        by_head, key_block, query_block, decay_block, doc_block, before = pieces
        block_state, through, running = state_terms(
            by_head, key_block, decay_block, doc_block, before
        )
        new_carry = (through[:, None, None] * carry_state + block_state, through * kept_share)
        return (new_carry, (block_state, through, running))

    zero_state = jnp.zeros((heads_here, width, n_state), jnp.float32)
    ones_here = jnp.ones((heads_here,), jnp.float32)
    local_carry, block_outputs = lax.scan(
        state_pass,
        (zero_state, ones_here),
        (inputs_blocks, key_blocks, query_blocks, decay_blocks, doc_ids, doc_before),
    )
    local_state, local_kept = local_carry
    block_states, throughs, runnings = (block_outputs[0], block_outputs[1], block_outputs[2])
    entry_state = exclusive_prefix(local_kept, local_state, "sc", "sz", "sx")

    def mix_pass(carry_state, pieces):
        by_head, key_block, query_block, running, doc_block, before, block_state, through = pieces
        carried = entry_terms(query_block, carry_state, running, doc_block, before)
        mixed_block = (
            inner_terms(by_head, key_block, query_block, running, doc_block)
            + carried
            + skip_gain[None, :, None] * by_head.astype(jnp.float32)
        )
        return (through[:, None, None] * carry_state + block_state, mixed_block)

    final_state, mixed = lax.scan(
        mix_pass,
        entry_state,
        (
            inputs_blocks,
            key_blocks,
            query_blocks,
            runnings,
            doc_ids,
            doc_before,
            block_states,
            throughs,
        ),
    )
    mixed = mixed.reshape(tok_dev, heads_here * width)
    gated = mixed * jax.nn.silu(gate_rows.astype(jnp.float32))
    squares = jnp.sum(gated * gated, axis=1)
    square_hi = squares.astype(jnp.bfloat16)
    square_lo = (squares - square_hi.astype(jnp.float32)).astype(jnp.bfloat16)
    unscaled = (gated * norm_gain[None, :]).astype(jnp.bfloat16)
    partial = jnp.dot(unscaled, out_weight, preferred_element_type=jnp.float32).astype(jnp.bfloat16)
    groups = lax.axis_size("head")
    chunk = tok_dev // groups
    d_model = partial.shape[1]
    extra = jnp.concatenate(
        [square_hi.reshape(groups, 1, chunk), square_lo.reshape(groups, 1, chunk)], axis=1
    )
    extra = jnp.pad(extra, ((0, 0), (0, 0), (0, d_model - chunk)))
    sent = jnp.concatenate([partial.reshape(groups, chunk, d_model), extra], axis=1)
    arrived_parts = lax.all_to_all(sent, "head", split_axis=0, concat_axis=0, tiled=True)
    summed = jnp.sum(arrived_parts.astype(jnp.float32), axis=0)
    total_squares = summed[chunk, :chunk] + summed[chunk + 1, :chunk]
    row_scale = lax.rsqrt(total_squares / (ATTENTION_LANES * HEAD_DIM) + norm_eps)
    return (summed[:chunk] * row_scale[:, None]).astype(jnp.bfloat16)


def solution(mesh):
    seq = mesh.shape["seq"]
    devices = mesh.devices.reshape(seq // 16, 8, 2, mesh.shape["head"])
    split_mesh = jax.sharding.Mesh(devices, ROWS + ("head",))
    in_specs = (
        P(ROWS, "head"),
        P(ROWS, "head"),
        P(ROWS, None),
        P(ROWS, None),
        P(ROWS, "head"),
        P(ROWS),
        P(),
        P("head"),
        P("head"),
        P("head", None),
    )
    out_specs = P(ROWS + ("head",), None)
    return jax.shard_map(
        body, mesh=split_mesh, in_specs=in_specs, out_specs=out_specs, check_vma=False
    )
```

```python
import jax
import jax.numpy as jnp
from jax import lax
from jax.sharding import PartitionSpec as P

ATTENTION_LANES = 48
ROWS = ("sx", "sz", "sc")
HEAD_DIM = 64
BLOCK = 512


far_below = -1e30
norm_eps = 1e-05


def combine(earlier, later):
    return (earlier[0] * later[0], later[0][:, None, None] * earlier[1] + later[1])


def pack_state(kept, state):
    flat = jnp.broadcast_to(kept[:, None, None], (kept.shape[0], 1, state.shape[2]))
    return jnp.concatenate([state, flat], axis=1).astype(jnp.bfloat16)


def group_weights(kept, here):
    count = kept.shape[0]
    j = lax.broadcasted_iota(jnp.int32, (count, count), 0)
    k = lax.broadcasted_iota(jnp.int32, (count, count), 1)
    ahead = lax.broadcasted_iota(jnp.int32, (count, 1), 0) < here
    between = (j < k) & (k < here)
    into_here = jnp.prod(jnp.where(between[:, :, None], kept[None, :, :], 1.0), axis=1) * ahead
    into_end = jnp.prod(jnp.where((j < k)[:, :, None], kept[None, :, :], 1.0), axis=1)
    kept_before = jnp.prod(jnp.where(ahead, kept, 1.0), axis=0)
    return into_here, into_end, kept_before, jnp.prod(kept, axis=0)


def gathered_level(kept, state, axis):
    gathered = lax.all_gather(pack_state(kept, state), axis)
    g_kept = gathered[:, :, -1, 0].astype(jnp.float32)
    into_here, into_end, kept_before, kept_all = group_weights(g_kept, lax.axis_index(axis))
    rows = state.shape[1]
    before = jnp.einsum("jh,jhpn->hpn", into_here, gathered.astype(jnp.float32))[:, :rows]
    total = jnp.einsum("jh,jhpn->hpn", into_end, gathered.astype(jnp.float32))[:, :rows]
    return before, kept_before, total, kept_all


def exclusive_prefix(kept, state, pair, line, lines):
    pair_before, pair_kept_before, pair_total, pair_kept = gathered_level(kept, state, pair)
    half = kept.shape[0] // 2
    mine = lax.axis_index(pair) * half
    part_total = lax.dynamic_slice_in_dim(pair_total, mine, half, 0)
    part_kept = lax.dynamic_slice_in_dim(pair_kept, mine, half, 0)
    line_before, line_kept_before, line_total, line_kept = gathered_level(
        part_kept, part_total, line
    )
    outer_before, _, _, _ = gathered_level(line_kept, line_total, lines)
    start_state = line_kept_before[:, None, None] * outer_before + line_before
    whole = lax.all_gather(start_state, pair, tiled=True)
    return pair_kept_before[:, None, None] * whole + pair_before


def doc_index(places, starts):
    return jnp.sum((starts[None, :] <= places[:, None]).astype(jnp.int32), axis=1) - 1


def state_terms(by_head, key_block, decay_block, doc_block, before):
    running = jnp.cumsum(decay_block.astype(jnp.float32), axis=0)
    same_doc = (doc_block == doc_block[-1]).astype(jnp.float32)
    closing_weight = jnp.exp(running[-1][None, :] - running) * same_doc[:, None]
    weighted = (key_block.astype(jnp.float32)[None, :, :] * closing_weight.T[:, :, None]).astype(
        jnp.bfloat16
    )
    block_state = jnp.einsum("hsn,shp->hpn", weighted, by_head, preferred_element_type=jnp.float32)
    through = jnp.exp(running[-1]) * (doc_block[-1] == before).astype(jnp.float32)
    return (block_state, through, running)


def inner_terms(by_head, key_block, query_block, running, doc_block):
    length = running.shape[0]
    later = lax.broadcasted_iota(jnp.int32, (length, length), 0)
    earlier = lax.broadcasted_iota(jnp.int32, (length, length), 1)
    allowed = (later >= earlier) & (doc_block[:, None] == doc_block[None, :])
    running_heads = running.T
    decay_gaps = jnp.where(
        allowed[None, :, :], running_heads[:, :, None] - running_heads[:, None, :], far_below
    )
    products = jnp.einsum("tn,sn->ts", query_block, key_block, preferred_element_type=jnp.float32)
    affinity_logits = (products[None, :, :] * jnp.exp(decay_gaps)).astype(jnp.bfloat16)
    return jnp.einsum("hts,shp->thp", affinity_logits, by_head, preferred_element_type=jnp.float32)


def entry_terms(query_block, carry_state, running, doc_block, before):
    entry_weight = jnp.exp(running) * (doc_block == before).astype(jnp.float32)[:, None]
    carried = jnp.einsum(
        "tn,hpn->thp", query_block.astype(jnp.float32), carry_state, precision=lax.Precision.HIGHEST
    )
    return carried * entry_weight[:, :, None]


def body(
    features_in,
    gate_in,
    b_input,
    c_input,
    log_decay,
    row_target,
    doc_lengths,
    skip_gain,
    norm_gain,
    out_weight,
):
    tok_dev = features_in.shape[0]
    heads_here = log_decay.shape[1]
    feats = features_in.shape[1]
    width = feats // heads_here
    n_state = b_input.shape[1]
    shards = lax.axis_size(ROWS)
    capacity = tok_dev // shards
    owner = row_target // tok_dev
    local_place = row_target - owner * tok_dev
    owner_hits = (owner[:, None] == lax.broadcasted_iota(jnp.int32, (tok_dev, shards), 1)).astype(
        jnp.int32
    )
    slot_rank = jnp.sum((jnp.cumsum(owner_hits, axis=0) - owner_hits) * owner_hits, axis=1)
    slot_index = owner * capacity + slot_rank
    place_hi = (local_place // 32).astype(jnp.bfloat16)
    place_lo = (local_place % 32).astype(jnp.bfloat16)
    pieces = [features_in, gate_in, b_input, c_input, log_decay, place_hi[:, None], place_lo[:, None]]
    to_slot = (
        lax.broadcasted_iota(jnp.int32, (tok_dev, tok_dev), 0) == slot_index[None, :]
    ).astype(jnp.bfloat16)

    def send(values):
        packed = jnp.concatenate(
            [
                jnp.dot(to_slot, v, preferred_element_type=jnp.float32).astype(jnp.bfloat16)
                for v in values
            ],
            axis=1,
        )
        return lax.all_to_all(
            packed.reshape(shards, capacity, packed.shape[1]),
            ROWS,
            split_axis=0,
            concat_axis=0,
            tiled=True,
        ).reshape(tok_dev, packed.shape[1])

    rows_out = jnp.concatenate(pieces[4:], axis=1)
    gate_piece = pieces[1]
    pieces = [pieces[0]] + pieces[2:4] + [rows_out]
    moved = send(pieces)
    columns = moved.shape[1]
    arrived = (
        moved[:, columns - 2].astype(jnp.int32) * 32 + moved[:, columns - 1].astype(jnp.int32)
    )
    to_place = (
        lax.broadcasted_iota(jnp.int32, (tok_dev, tok_dev), 0) == arrived[None, :]
    ).astype(jnp.bfloat16)

    def place(values):
        return jnp.dot(to_place, values, preferred_element_type=jnp.float32).astype(jnp.bfloat16)

    rows = place(moved)
    features = rows[:, :feats]
    key_full = rows[:, feats : feats + n_state]
    query_full = rows[:, feats + n_state : feats + 2 * n_state]
    decays = rows[:, feats + 2 * n_state : feats + 2 * n_state + heads_here]
    gate_moved = send([gate_piece])

    doc_starts = jnp.cumsum(doc_lengths) - doc_lengths
    first_place = lax.axis_index(ROWS) * tok_dev
    blocks = tok_dev // BLOCK
    places = first_place + lax.broadcasted_iota(jnp.int32, (tok_dev,), 0)
    doc_ids = doc_index(places, doc_starts).reshape(blocks, BLOCK)
    doc_before = doc_index(
        first_place + lax.broadcasted_iota(jnp.int32, (blocks,), 0) * BLOCK - 1, doc_starts
    )
    inputs_blocks = features.reshape(blocks, BLOCK, heads_here, width)
    key_blocks = key_full.reshape(blocks, BLOCK, n_state)
    query_blocks = query_full.reshape(blocks, BLOCK, n_state)
    decay_blocks = decays.reshape(blocks, BLOCK, heads_here)

    def state_pass(carry, pieces):
        carry_state, kept_share = carry
        by_head, key_block, query_block, decay_block, doc_block, before = pieces
        block_state, through, running = state_terms(
            by_head, key_block, decay_block, doc_block, before
        )
        new_carry = (through[:, None, None] * carry_state + block_state, through * kept_share)
        return (new_carry, (block_state, through, running))

    zero_state = jnp.zeros((heads_here, width, n_state), jnp.float32)
    ones_here = jnp.ones((heads_here,), jnp.float32)
    local_carry, block_outputs = lax.scan(
        state_pass,
        (zero_state, ones_here),
        (inputs_blocks, key_blocks, query_blocks, decay_blocks, doc_ids, doc_before),
    )
    local_state, local_kept = local_carry
    block_states, throughs, runnings = (block_outputs[0], block_outputs[1], block_outputs[2])
    entry_state = exclusive_prefix(local_kept, local_state, "sc", "sz", "sx")

    def mix_pass(carry_state, pieces):
        by_head, key_block, query_block, running, doc_block, before, block_state, through = pieces
        carried = entry_terms(query_block, carry_state, running, doc_block, before)
        mixed_block = (
            inner_terms(by_head, key_block, query_block, running, doc_block)
            + carried
            + skip_gain[None, :, None] * by_head.astype(jnp.float32)
        )
        return (through[:, None, None] * carry_state + block_state, mixed_block)

    final_state, mixed = lax.scan(
        mix_pass,
        entry_state,
        (
            inputs_blocks,
            key_blocks,
            query_blocks,
            runnings,
            doc_ids,
            doc_before,
            block_states,
            throughs,
        ),
    )
    mixed = mixed.reshape(tok_dev, heads_here * width)
    gate_rows = place(gate_moved)
    gated = mixed * jax.nn.silu(gate_rows.astype(jnp.float32))
    squares = jnp.sum(gated * gated, axis=1)
    square_hi = squares.astype(jnp.bfloat16)
    square_lo = (squares - square_hi.astype(jnp.float32)).astype(jnp.bfloat16)
    unscaled = (gated * norm_gain[None, :]).astype(jnp.bfloat16)
    partial = jnp.dot(unscaled, out_weight, preferred_element_type=jnp.float32).astype(jnp.bfloat16)
    groups = lax.axis_size("head")
    chunk = tok_dev // groups
    d_model = partial.shape[1]
    extra = jnp.concatenate(
        [square_hi.reshape(groups, 1, chunk), square_lo.reshape(groups, 1, chunk)], axis=1
    )
    extra = jnp.pad(extra, ((0, 0), (0, 6), (0, d_model - chunk)))
    sent = jnp.concatenate([partial.reshape(groups, chunk, d_model), extra], axis=1)
    arrived_parts = lax.all_to_all(sent, "head", split_axis=0, concat_axis=0, tiled=True)
    summed = jnp.sum(arrived_parts.astype(jnp.float32), axis=0)
    total_squares = summed[chunk, :chunk] + summed[chunk + 1, :chunk]
    row_scale = lax.rsqrt(total_squares / (ATTENTION_LANES * HEAD_DIM) + norm_eps)
    return (summed[:chunk] * row_scale[:, None]).astype(jnp.bfloat16)


def solution(mesh):
    seq = mesh.shape["seq"]
    devices = mesh.devices.reshape(seq // 16, 8, 2, mesh.shape["head"])
    split_mesh = jax.sharding.Mesh(devices, ROWS + ("head",))
    in_specs = (
        P(ROWS, "head"),
        P(ROWS, "head"),
        P(ROWS, None),
        P(ROWS, None),
        P(ROWS, "head"),
        P(ROWS),
        P(),
        P("head"),
        P("head"),
        P("head", None),
    )
    out_specs = P(ROWS + ("head",), None)
    return jax.shard_map(
        body, mesh=split_mesh, in_specs=in_specs, out_specs=out_specs, check_vma=False
    )
```

```python
import jax
import jax.numpy as jnp
from jax import lax
from jax.sharding import PartitionSpec as P

ATTENTION_LANES = 48
ROWS = ("sx", "sz", "sc")
HEAD_DIM = 64
BLOCK = 512


far_below = -1e30
norm_eps = 1e-05


def combine(earlier, later):
    return (earlier[0] * later[0], later[0][:, None, None] * earlier[1] + later[1])


def pack_state(kept, state):
    flat = jnp.broadcast_to(kept[:, None, None], (kept.shape[0], 1, state.shape[2]))
    return jnp.concatenate([state, flat], axis=1).astype(jnp.bfloat16)


def group_weights(kept, here):
    count = kept.shape[0]
    j = lax.broadcasted_iota(jnp.int32, (count, count), 0)
    k = lax.broadcasted_iota(jnp.int32, (count, count), 1)
    ahead = lax.broadcasted_iota(jnp.int32, (count, 1), 0) < here
    between = (j < k) & (k < here)
    into_here = jnp.prod(jnp.where(between[:, :, None], kept[None, :, :], 1.0), axis=1) * ahead
    into_end = jnp.prod(jnp.where((j < k)[:, :, None], kept[None, :, :], 1.0), axis=1)
    kept_before = jnp.prod(jnp.where(ahead, kept, 1.0), axis=0)
    return into_here, into_end, kept_before, jnp.prod(kept, axis=0)


def gathered_level(kept, state, axis):
    gathered = lax.all_gather(pack_state(kept, state), axis)
    g_kept = gathered[:, :, -1, 0].astype(jnp.float32)
    into_here, into_end, kept_before, kept_all = group_weights(g_kept, lax.axis_index(axis))
    rows = state.shape[1]
    before = jnp.einsum("jh,jhpn->hpn", into_here, gathered.astype(jnp.float32))[:, :rows]
    total = jnp.einsum("jh,jhpn->hpn", into_end, gathered.astype(jnp.float32))[:, :rows]
    return before, kept_before, total, kept_all


def exclusive_prefix(kept, state, pair, line, lines):
    pair_before, pair_kept_before, pair_total, pair_kept = gathered_level(kept, state, pair)
    half = kept.shape[0] // 2
    mine = lax.axis_index(pair) * half
    part_total = lax.dynamic_slice_in_dim(pair_total, mine, half, 0)
    part_kept = lax.dynamic_slice_in_dim(pair_kept, mine, half, 0)
    line_before, line_kept_before, line_total, line_kept = gathered_level(
        part_kept, part_total, line
    )
    outer_before, _, _, _ = gathered_level(line_kept, line_total, lines)
    start_state = line_kept_before[:, None, None] * outer_before + line_before
    whole = lax.all_gather(start_state, pair, tiled=True)
    return pair_kept_before[:, None, None] * whole + pair_before


def doc_index(places, starts):
    return jnp.sum((starts[None, :] <= places[:, None]).astype(jnp.int32), axis=1) - 1


def state_terms(by_head, key_block, decay_block, doc_block, before):
    running = jnp.cumsum(decay_block.astype(jnp.float32), axis=0)
    same_doc = (doc_block == doc_block[-1]).astype(jnp.float32)
    closing_weight = jnp.exp(running[-1][None, :] - running) * same_doc[:, None]
    weighted = (key_block.astype(jnp.float32)[None, :, :] * closing_weight.T[:, :, None]).astype(
        jnp.bfloat16
    )
    block_state = jnp.einsum("hsn,shp->hpn", weighted, by_head, preferred_element_type=jnp.float32)
    through = jnp.exp(running[-1]) * (doc_block[-1] == before).astype(jnp.float32)
    return (block_state, through, running)


def inner_terms(by_head, key_block, query_block, running, doc_block):
    length = running.shape[0]
    later = lax.broadcasted_iota(jnp.int32, (length, length), 0)
    earlier = lax.broadcasted_iota(jnp.int32, (length, length), 1)
    allowed = (later >= earlier) & (doc_block[:, None] == doc_block[None, :])
    running_heads = running.T
    decay_gaps = jnp.where(
        allowed[None, :, :], running_heads[:, :, None] - running_heads[:, None, :], far_below
    )
    products = jnp.einsum("tn,sn->ts", query_block, key_block, preferred_element_type=jnp.float32)
    affinity_logits = (products[None, :, :] * jnp.exp(decay_gaps)).astype(jnp.bfloat16)
    return jnp.einsum("hts,shp->thp", affinity_logits, by_head, preferred_element_type=jnp.float32)


def entry_terms(query_block, carry_state, running, doc_block, before):
    entry_weight = jnp.exp(running) * (doc_block == before).astype(jnp.float32)[:, None]
    carried = jnp.einsum(
        "tn,hpn->thp", query_block.astype(jnp.float32), carry_state, precision=lax.Precision.HIGHEST
    )
    return carried * entry_weight[:, :, None]


def body(
    features_in,
    gate_in,
    b_input,
    c_input,
    log_decay,
    row_target,
    doc_lengths,
    skip_gain,
    norm_gain,
    out_weight,
):
    tok_dev = features_in.shape[0]
    heads_here = log_decay.shape[1]
    feats = features_in.shape[1]
    width = feats // heads_here
    n_state = b_input.shape[1]
    shards = lax.axis_size(ROWS)
    capacity = tok_dev // shards
    owner = row_target // tok_dev
    local_place = row_target - owner * tok_dev
    owner_hits = (owner[:, None] == lax.broadcasted_iota(jnp.int32, (tok_dev, shards), 1)).astype(
        jnp.int32
    )
    slot_rank = jnp.sum((jnp.cumsum(owner_hits, axis=0) - owner_hits) * owner_hits, axis=1)
    slot_index = owner * capacity + slot_rank
    place_hi = (local_place // 32).astype(jnp.bfloat16)
    place_lo = (local_place % 32).astype(jnp.bfloat16)
    pieces = [features_in, gate_in, b_input, c_input, log_decay, place_hi[:, None], place_lo[:, None]]
    to_slot = (
        lax.broadcasted_iota(jnp.int32, (tok_dev, tok_dev), 0) == slot_index[None, :]
    ).astype(jnp.bfloat16)

    def send(values):
        packed = jnp.concatenate(
            [
                jnp.dot(to_slot, v, preferred_element_type=jnp.float32).astype(jnp.bfloat16)
                for v in values
            ],
            axis=1,
        )
        return lax.all_to_all(
            packed.reshape(shards, capacity, packed.shape[1]),
            ROWS,
            split_axis=0,
            concat_axis=0,
            tiled=True,
        ).reshape(tok_dev, packed.shape[1])

    rows_out = jnp.concatenate(pieces[4:], axis=1)
    late_pieces = [pieces[1], pieces[3]]
    pieces = [pieces[0], pieces[2], rows_out]
    moved = send(pieces)
    columns = moved.shape[1]
    arrived = (
        moved[:, columns - 2].astype(jnp.int32) * 32 + moved[:, columns - 1].astype(jnp.int32)
    )
    to_place = (
        lax.broadcasted_iota(jnp.int32, (tok_dev, tok_dev), 0) == arrived[None, :]
    ).astype(jnp.bfloat16)

    def place(values):
        return jnp.dot(to_place, values, preferred_element_type=jnp.float32).astype(jnp.bfloat16)

    rows = place(moved)
    features = rows[:, :feats]
    key_full = rows[:, feats : feats + n_state]
    decays = rows[:, feats + n_state : feats + n_state + heads_here]
    late_rows = place(send(late_pieces))
    gate_rows = late_rows[:, :feats]
    query_full = late_rows[:, feats : feats + n_state]

    doc_starts = jnp.cumsum(doc_lengths) - doc_lengths
    first_place = lax.axis_index(ROWS) * tok_dev
    blocks = tok_dev // BLOCK
    places = first_place + lax.broadcasted_iota(jnp.int32, (tok_dev,), 0)
    doc_ids = doc_index(places, doc_starts).reshape(blocks, BLOCK)
    doc_before = doc_index(
        first_place + lax.broadcasted_iota(jnp.int32, (blocks,), 0) * BLOCK - 1, doc_starts
    )
    inputs_blocks = features.reshape(blocks, BLOCK, heads_here, width)
    key_blocks = key_full.reshape(blocks, BLOCK, n_state)
    query_blocks = query_full.reshape(blocks, BLOCK, n_state)
    decay_blocks = decays.reshape(blocks, BLOCK, heads_here)

    def state_pass(carry, pieces):
        carry_state, kept_share = carry
        by_head, key_block, query_block, decay_block, doc_block, before = pieces
        block_state, through, running = state_terms(
            by_head, key_block, decay_block, doc_block, before
        )
        new_carry = (through[:, None, None] * carry_state + block_state, through * kept_share)
        return (new_carry, (block_state, through, running))

    zero_state = jnp.zeros((heads_here, width, n_state), jnp.float32)
    ones_here = jnp.ones((heads_here,), jnp.float32)
    local_carry, block_outputs = lax.scan(
        state_pass,
        (zero_state, ones_here),
        (inputs_blocks, key_blocks, query_blocks, decay_blocks, doc_ids, doc_before),
    )
    local_state, local_kept = local_carry
    block_states, throughs, runnings = (block_outputs[0], block_outputs[1], block_outputs[2])
    entry_state = exclusive_prefix(local_kept, local_state, "sc", "sz", "sx")

    def mix_pass(carry_state, pieces):
        by_head, key_block, query_block, running, doc_block, before, block_state, through = pieces
        carried = entry_terms(query_block, carry_state, running, doc_block, before)
        mixed_block = (
            inner_terms(by_head, key_block, query_block, running, doc_block)
            + carried
            + skip_gain[None, :, None] * by_head.astype(jnp.float32)
        )
        return (through[:, None, None] * carry_state + block_state, mixed_block)

    final_state, mixed = lax.scan(
        mix_pass,
        entry_state,
        (
            inputs_blocks,
            key_blocks,
            query_blocks,
            runnings,
            doc_ids,
            doc_before,
            block_states,
            throughs,
        ),
    )
    mixed = mixed.reshape(tok_dev, heads_here * width)
    gated = mixed * jax.nn.silu(gate_rows.astype(jnp.float32))
    squares = jnp.sum(gated * gated, axis=1)
    square_hi = squares.astype(jnp.bfloat16)
    square_lo = (squares - square_hi.astype(jnp.float32)).astype(jnp.bfloat16)
    unscaled = (gated * norm_gain[None, :]).astype(jnp.bfloat16)
    partial = jnp.dot(unscaled, out_weight, preferred_element_type=jnp.float32).astype(jnp.bfloat16)
    groups = lax.axis_size("head")
    chunk = tok_dev // groups
    d_model = partial.shape[1]
    extra = jnp.concatenate(
        [square_hi.reshape(groups, 1, chunk), square_lo.reshape(groups, 1, chunk)], axis=1
    )
    extra = jnp.pad(extra, ((0, 0), (0, 6), (0, d_model - chunk)))
    sent = jnp.concatenate([partial.reshape(groups, chunk, d_model), extra], axis=1)
    arrived_parts = lax.all_to_all(sent, "head", split_axis=0, concat_axis=0, tiled=True)
    summed = jnp.sum(arrived_parts.astype(jnp.float32), axis=0)
    total_squares = summed[chunk, :chunk] + summed[chunk + 1, :chunk]
    row_scale = lax.rsqrt(total_squares / (ATTENTION_LANES * HEAD_DIM) + norm_eps)
    return (summed[:chunk] * row_scale[:, None]).astype(jnp.bfloat16)


def solution(mesh):
    seq = mesh.shape["seq"]
    devices = mesh.devices.reshape(seq // 16, 8, 2, mesh.shape["head"])
    split_mesh = jax.sharding.Mesh(devices, ROWS + ("head",))
    in_specs = (
        P(ROWS, "head"),
        P(ROWS, "head"),
        P(ROWS, None),
        P(ROWS, None),
        P(ROWS, "head"),
        P(ROWS),
        P(),
        P("head"),
        P("head"),
        P("head", None),
    )
    out_specs = P(ROWS + ("head",), None)
    return jax.shard_map(
        body, mesh=split_mesh, in_specs=in_specs, out_specs=out_specs, check_vma=False
    )
```

```python
import jax
import jax.numpy as jnp
from jax import lax
from jax.sharding import PartitionSpec as P

ATTENTION_LANES = 48
ROWS = ("sx", "sz", "sc")
HEAD_DIM = 64
BLOCK = 512


far_below = -1e30
norm_eps = 1e-05


def combine(earlier, later):
    return (earlier[0] * later[0], later[0][:, None, None] * earlier[1] + later[1])


def pack_state(kept, state):
    flat = jnp.broadcast_to(kept[:, None, None], (kept.shape[0], 1, state.shape[2]))
    return jnp.concatenate([state, flat], axis=1).astype(jnp.bfloat16)


def group_weights(kept, here):
    count = kept.shape[0]
    j = lax.broadcasted_iota(jnp.int32, (count, count), 0)
    k = lax.broadcasted_iota(jnp.int32, (count, count), 1)
    ahead = lax.broadcasted_iota(jnp.int32, (count, 1), 0) < here
    between = (j < k) & (k < here)
    into_here = jnp.prod(jnp.where(between[:, :, None], kept[None, :, :], 1.0), axis=1) * ahead
    into_end = jnp.prod(jnp.where((j < k)[:, :, None], kept[None, :, :], 1.0), axis=1)
    kept_before = jnp.prod(jnp.where(ahead, kept, 1.0), axis=0)
    return into_here, into_end, kept_before, jnp.prod(kept, axis=0)


def gathered_level(kept, state, axis):
    gathered = lax.all_gather(pack_state(kept, state), axis)
    g_kept = gathered[:, :, -1, 0].astype(jnp.float32)
    into_here, into_end, kept_before, kept_all = group_weights(g_kept, lax.axis_index(axis))
    rows = state.shape[1]
    before = jnp.einsum("jh,jhpn->hpn", into_here, gathered.astype(jnp.float32))[:, :rows]
    total = jnp.einsum("jh,jhpn->hpn", into_end, gathered.astype(jnp.float32))[:, :rows]
    return before, kept_before, total, kept_all


def exclusive_prefix(kept, state, pair, line, lines):
    pair_before, pair_kept_before, pair_total, pair_kept = gathered_level(kept, state, pair)
    half = kept.shape[0] // 2
    mine = lax.axis_index(pair) * half
    part_total = lax.dynamic_slice_in_dim(pair_total, mine, half, 0)
    part_kept = lax.dynamic_slice_in_dim(pair_kept, mine, half, 0)
    line_before, line_kept_before, line_total, line_kept = gathered_level(
        part_kept, part_total, line
    )
    outer_before, _, _, _ = gathered_level(line_kept, line_total, lines)
    start_state = line_kept_before[:, None, None] * outer_before + line_before
    whole = lax.all_gather(start_state, pair, tiled=True)
    return pair_kept_before[:, None, None] * whole + pair_before


def doc_index(places, starts):
    return jnp.sum((starts[None, :] <= places[:, None]).astype(jnp.int32), axis=1) - 1


def state_terms(by_head, key_block, decay_block, doc_block, before):
    running = jnp.cumsum(decay_block.astype(jnp.float32), axis=0)
    same_doc = (doc_block == doc_block[-1]).astype(jnp.float32)
    closing_weight = jnp.exp(running[-1][None, :] - running) * same_doc[:, None]
    weighted = (key_block.astype(jnp.float32)[None, :, :] * closing_weight.T[:, :, None]).astype(
        jnp.bfloat16
    )
    block_state = jnp.einsum("hsn,shp->hpn", weighted, by_head, preferred_element_type=jnp.float32)
    through = jnp.exp(running[-1]) * (doc_block[-1] == before).astype(jnp.float32)
    return (block_state, through, running)


def inner_terms(by_head, key_block, query_block, running, doc_block):
    length = running.shape[0]
    later = lax.broadcasted_iota(jnp.int32, (length, length), 0)
    earlier = lax.broadcasted_iota(jnp.int32, (length, length), 1)
    allowed = (later >= earlier) & (doc_block[:, None] == doc_block[None, :])
    running_heads = running.T
    decay_gaps = jnp.where(
        allowed[None, :, :], running_heads[:, :, None] - running_heads[:, None, :], far_below
    )
    products = jnp.einsum("tn,sn->ts", query_block, key_block, preferred_element_type=jnp.float32)
    affinity_logits = (products[None, :, :] * jnp.exp(decay_gaps)).astype(jnp.bfloat16)
    return jnp.einsum("hts,shp->thp", affinity_logits, by_head, preferred_element_type=jnp.float32)


def entry_terms(query_block, carry_state, running, doc_block, before):
    entry_weight = jnp.exp(running) * (doc_block == before).astype(jnp.float32)[:, None]
    carried = jnp.einsum(
        "tn,hpn->thp", query_block.astype(jnp.float32), carry_state, precision=lax.Precision.HIGHEST
    )
    return carried * entry_weight[:, :, None]


def body(
    features_in,
    gate_in,
    b_input,
    c_input,
    log_decay,
    row_target,
    doc_lengths,
    skip_gain,
    norm_gain,
    out_weight,
):
    tok_dev = features_in.shape[0]
    heads_here = log_decay.shape[1]
    feats = features_in.shape[1]
    width = feats // heads_here
    n_state = b_input.shape[1]
    shards = lax.axis_size(ROWS)
    capacity = tok_dev // shards
    owner = row_target // tok_dev
    local_place = row_target - owner * tok_dev
    owner_hits = (owner[:, None] == lax.broadcasted_iota(jnp.int32, (tok_dev, shards), 1)).astype(
        jnp.int32
    )
    slot_rank = jnp.sum((jnp.cumsum(owner_hits, axis=0) - owner_hits) * owner_hits, axis=1)
    slot_index = owner * capacity + slot_rank
    place_hi = (local_place // 32).astype(jnp.bfloat16)
    place_lo = (local_place % 32).astype(jnp.bfloat16)
    pieces = [features_in, gate_in, b_input, c_input, log_decay, place_hi[:, None], place_lo[:, None]]
    to_slot = (
        lax.broadcasted_iota(jnp.int32, (tok_dev, tok_dev), 0) == slot_index[None, :]
    ).astype(jnp.bfloat16)

    def send(values):
        packed = jnp.concatenate(
            [
                jnp.dot(to_slot, v, preferred_element_type=jnp.float32).astype(jnp.bfloat16)
                for v in values
            ],
            axis=1,
        )
        return lax.all_to_all(
            packed.reshape(shards, capacity, packed.shape[1]),
            ROWS,
            split_axis=0,
            concat_axis=0,
            tiled=True,
        ).reshape(tok_dev, packed.shape[1])

    rows_out = jnp.concatenate(pieces[4:], axis=1)
    gate_piece = pieces[1]
    pieces = [pieces[0]] + pieces[2:4] + [rows_out]
    moved = send(pieces)
    columns = moved.shape[1]
    arrived = (
        moved[:, columns - 2].astype(jnp.int32) * 32 + moved[:, columns - 1].astype(jnp.int32)
    )
    to_place = (
        lax.broadcasted_iota(jnp.int32, (tok_dev, tok_dev), 0) == arrived[None, :]
    ).astype(jnp.bfloat16)

    def place(values):
        return jnp.dot(to_place, values, preferred_element_type=jnp.float32).astype(jnp.bfloat16)

    rows = place(moved)
    features = rows[:, :feats]
    key_full = rows[:, feats : feats + n_state]
    query_full = rows[:, feats + n_state : feats + 2 * n_state]
    decays = rows[:, feats + 2 * n_state : feats + 2 * n_state + heads_here]
    gate_moved = send([gate_piece])

    doc_starts = jnp.cumsum(doc_lengths) - doc_lengths
    first_place = lax.axis_index(ROWS) * tok_dev
    blocks = tok_dev // BLOCK
    places = first_place + lax.broadcasted_iota(jnp.int32, (tok_dev,), 0)
    doc_ids = doc_index(places, doc_starts).reshape(blocks, BLOCK)
    doc_before = doc_index(
        first_place + lax.broadcasted_iota(jnp.int32, (blocks,), 0) * BLOCK - 1, doc_starts
    )
    inputs_blocks = features.reshape(blocks, BLOCK, heads_here, width)
    key_blocks = key_full.reshape(blocks, BLOCK, n_state)
    query_blocks = query_full.reshape(blocks, BLOCK, n_state)
    decay_blocks = decays.reshape(blocks, BLOCK, heads_here)

    def state_pass(carry, pieces):
        carry_state, kept_share = carry
        by_head, key_block, query_block, decay_block, doc_block, before = pieces
        block_state, through, running = state_terms(
            by_head, key_block, decay_block, doc_block, before
        )
        new_carry = (through[:, None, None] * carry_state + block_state, through * kept_share)
        return (new_carry, (block_state, through, running))

    zero_state = jnp.zeros((heads_here, width, n_state), jnp.float32)
    ones_here = jnp.ones((heads_here,), jnp.float32)
    local_carry, block_outputs = lax.scan(
        state_pass,
        (zero_state, ones_here),
        (inputs_blocks, key_blocks, query_blocks, decay_blocks, doc_ids, doc_before),
    )
    local_state, local_kept = local_carry
    block_states, throughs, runnings = (block_outputs[0], block_outputs[1], block_outputs[2])
    entry_state = exclusive_prefix(local_kept, local_state, "sc", "sz", "sx")

    def mix_pass(carry_state, pieces):
        by_head, key_block, query_block, running, doc_block, before, block_state, through = pieces
        carried = entry_terms(query_block, carry_state, running, doc_block, before)
        mixed_block = (
            inner_terms(by_head, key_block, query_block, running, doc_block)
            + carried
            + skip_gain[None, :, None] * by_head.astype(jnp.float32)
        )
        return (through[:, None, None] * carry_state + block_state, mixed_block)

    final_state, mixed = lax.scan(
        mix_pass,
        entry_state,
        (
            inputs_blocks,
            key_blocks,
            query_blocks,
            runnings,
            doc_ids,
            doc_before,
            block_states,
            throughs,
        ),
    )
    mixed = mixed.reshape(tok_dev, heads_here * width)
    gate_rows = place(gate_moved)
    gated = mixed * jax.nn.silu(gate_rows.astype(jnp.float32))
    squares = jnp.sum(gated * gated, axis=1)
    square_hi = squares.astype(jnp.bfloat16)
    square_lo = (squares - square_hi.astype(jnp.float32)).astype(jnp.bfloat16)
    unscaled = (gated * norm_gain[None, :]).astype(jnp.bfloat16)
    partial = jnp.dot(unscaled, out_weight, preferred_element_type=jnp.float32).astype(jnp.bfloat16)
    groups = lax.axis_size("head")
    chunk = tok_dev // groups
    d_model = partial.shape[1]
    extra = jnp.concatenate(
        [square_hi.reshape(groups, 1, chunk), square_lo.reshape(groups, 1, chunk)], axis=1
    )
    extra = jnp.pad(extra, ((0, 0), (0, 0), (0, d_model - chunk)))
    sent = jnp.concatenate([partial.reshape(groups, chunk, d_model), extra], axis=1)
    arrived_parts = lax.all_to_all(sent, "head", split_axis=0, concat_axis=0, tiled=True)
    summed = jnp.sum(arrived_parts.astype(jnp.float32), axis=0)
    total_squares = summed[chunk, :chunk] + summed[chunk + 1, :chunk]
    row_scale = lax.rsqrt(total_squares / (ATTENTION_LANES * HEAD_DIM) + norm_eps)
    return (summed[:chunk] * row_scale[:, None]).astype(jnp.bfloat16)


def solution(mesh):
    seq = mesh.shape["seq"]
    devices = mesh.devices.reshape(seq // 16, 8, 2, mesh.shape["head"])
    split_mesh = jax.sharding.Mesh(devices, ROWS + ("head",))
    in_specs = (
        P(ROWS, "head"),
        P(ROWS, "head"),
        P(ROWS, None),
        P(ROWS, None),
        P(ROWS, "head"),
        P(ROWS),
        P(),
        P("head"),
        P("head"),
        P("head", None),
    )
    out_specs = P(ROWS + ("head",), None)
    return jax.shard_map(
        body, mesh=split_mesh, in_specs=in_specs, out_specs=out_specs, check_vma=False
    )
```

```python
import jax
import jax.numpy as jnp
from jax import lax
from jax.sharding import PartitionSpec as P

ATTENTION_LANES = 48
ROWS = ("sx", "sz", "sc")
HEAD_DIM = 64
BLOCK = 512


far_below = -1e30
norm_eps = 1e-05


def combine(earlier, later):
    return (earlier[0] * later[0], later[0][:, None, None] * earlier[1] + later[1])


def pack_state(kept, state):
    flat = jnp.broadcast_to(kept[:, None, None], (kept.shape[0], 1, state.shape[2]))
    return jnp.concatenate([state, flat], axis=1).astype(jnp.bfloat16)


def group_weights(kept, here):
    count = kept.shape[0]
    j = lax.broadcasted_iota(jnp.int32, (count, count), 0)
    k = lax.broadcasted_iota(jnp.int32, (count, count), 1)
    ahead = lax.broadcasted_iota(jnp.int32, (count, 1), 0) < here
    between = (j < k) & (k < here)
    into_here = jnp.prod(jnp.where(between[:, :, None], kept[None, :, :], 1.0), axis=1) * ahead
    into_end = jnp.prod(jnp.where((j < k)[:, :, None], kept[None, :, :], 1.0), axis=1)
    kept_before = jnp.prod(jnp.where(ahead, kept, 1.0), axis=0)
    return into_here, into_end, kept_before, jnp.prod(kept, axis=0)


def gathered_level(kept, state, axis):
    gathered = lax.all_gather(pack_state(kept, state), axis)
    g_kept = gathered[:, :, -1, 0].astype(jnp.float32)
    into_here, into_end, kept_before, kept_all = group_weights(g_kept, lax.axis_index(axis))
    rows = state.shape[1]
    before = jnp.einsum("jh,jhpn->hpn", into_here, gathered.astype(jnp.float32))[:, :rows]
    total = jnp.einsum("jh,jhpn->hpn", into_end, gathered.astype(jnp.float32))[:, :rows]
    return before, kept_before, total, kept_all


def exclusive_prefix(kept, state, pair, line, lines):
    pair_before, pair_kept_before, pair_total, pair_kept = gathered_level(kept, state, pair)
    half = kept.shape[0] // 2
    mine = lax.axis_index(pair) * half
    part_total = lax.dynamic_slice_in_dim(pair_total, mine, half, 0)
    part_kept = lax.dynamic_slice_in_dim(pair_kept, mine, half, 0)
    line_before, line_kept_before, line_total, line_kept = gathered_level(
        part_kept, part_total, line
    )
    outer_before, _, _, _ = gathered_level(line_kept, line_total, lines)
    start_state = line_kept_before[:, None, None] * outer_before + line_before
    whole = lax.all_gather(start_state, pair, tiled=True)
    return pair_kept_before[:, None, None] * whole + pair_before


def doc_index(places, starts):
    return jnp.sum((starts[None, :] <= places[:, None]).astype(jnp.int32), axis=1) - 1


def state_terms(by_head, key_block, decay_block, doc_block, before):
    running = jnp.cumsum(decay_block.astype(jnp.float32), axis=0)
    same_doc = (doc_block == doc_block[-1]).astype(jnp.float32)
    closing_weight = jnp.exp(running[-1][None, :] - running) * same_doc[:, None]
    weighted = (key_block.astype(jnp.float32)[None, :, :] * closing_weight.T[:, :, None]).astype(
        jnp.bfloat16
    )
    block_state = jnp.einsum("hsn,shp->hpn", weighted, by_head, preferred_element_type=jnp.float32)
    through = jnp.exp(running[-1]) * (doc_block[-1] == before).astype(jnp.float32)
    return (block_state, through, running)


def inner_terms(by_head, key_block, query_block, running, doc_block):
    length = running.shape[0]
    later = lax.broadcasted_iota(jnp.int32, (length, length), 0)
    earlier = lax.broadcasted_iota(jnp.int32, (length, length), 1)
    allowed = (later >= earlier) & (doc_block[:, None] == doc_block[None, :])
    running_heads = running.T
    decay_gaps = jnp.where(
        allowed[None, :, :], running_heads[:, :, None] - running_heads[:, None, :], far_below
    )
    products = jnp.einsum("tn,sn->ts", query_block, key_block, preferred_element_type=jnp.float32)
    affinity_logits = (products[None, :, :] * jnp.exp(decay_gaps)).astype(jnp.bfloat16)
    return jnp.einsum("hts,shp->htp", affinity_logits, by_head, preferred_element_type=jnp.float32)


def entry_terms(query_block, carry_state, running, doc_block, before):
    entry_weight = jnp.exp(running) * (doc_block == before).astype(jnp.float32)[:, None]
    carried = jnp.einsum(
        "tn,hpn->htp", query_block.astype(jnp.float32), carry_state, precision=lax.Precision.HIGHEST
    )
    return carried * entry_weight.T[:, :, None]


def body(
    features_in,
    gate_in,
    b_input,
    c_input,
    log_decay,
    row_target,
    doc_lengths,
    skip_gain,
    norm_gain,
    out_weight,
):
    tok_dev = features_in.shape[0]
    heads_here = log_decay.shape[1]
    feats = features_in.shape[1]
    width = feats // heads_here
    n_state = b_input.shape[1]
    shards = lax.axis_size(ROWS)
    capacity = tok_dev // shards
    owner = row_target // tok_dev
    local_place = row_target - owner * tok_dev
    owner_hits = (owner[:, None] == lax.broadcasted_iota(jnp.int32, (tok_dev, shards), 1)).astype(
        jnp.int32
    )
    slot_rank = jnp.sum((jnp.cumsum(owner_hits, axis=0) - owner_hits) * owner_hits, axis=1)
    slot_index = owner * capacity + slot_rank
    place_hi = (local_place // 32).astype(jnp.bfloat16)
    place_lo = (local_place % 32).astype(jnp.bfloat16)
    pieces = [features_in, gate_in, b_input, c_input, log_decay, place_hi[:, None], place_lo[:, None]]
    to_slot = (
        lax.broadcasted_iota(jnp.int32, (tok_dev, tok_dev), 0) == slot_index[None, :]
    ).astype(jnp.bfloat16)

    def send(values):
        packed = jnp.concatenate(
            [
                jnp.dot(to_slot, v, preferred_element_type=jnp.float32).astype(jnp.bfloat16)
                for v in values
            ],
            axis=1,
        )
        return lax.all_to_all(
            packed.reshape(shards, capacity, packed.shape[1]),
            ROWS,
            split_axis=0,
            concat_axis=0,
            tiled=True,
        ).reshape(tok_dev, packed.shape[1])

    rows_out = jnp.concatenate(pieces[4:], axis=1)
    gate_piece = pieces[1]
    pieces = [pieces[0]] + pieces[2:4] + [rows_out]
    moved = send(pieces)
    columns = moved.shape[1]
    arrived = (
        moved[:, columns - 2].astype(jnp.int32) * 32 + moved[:, columns - 1].astype(jnp.int32)
    )
    to_place = (
        lax.broadcasted_iota(jnp.int32, (tok_dev, tok_dev), 0) == arrived[None, :]
    ).astype(jnp.bfloat16)

    def place(values):
        return jnp.dot(to_place, values, preferred_element_type=jnp.float32).astype(jnp.bfloat16)

    rows = place(moved)
    features = rows[:, :feats]
    key_full = rows[:, feats : feats + n_state]
    query_full = rows[:, feats + n_state : feats + 2 * n_state]
    decays = rows[:, feats + 2 * n_state : feats + 2 * n_state + heads_here]
    gate_moved = send([gate_piece])

    doc_starts = jnp.cumsum(doc_lengths) - doc_lengths
    first_place = lax.axis_index(ROWS) * tok_dev
    blocks = tok_dev // BLOCK
    places = first_place + lax.broadcasted_iota(jnp.int32, (tok_dev,), 0)
    doc_ids = doc_index(places, doc_starts).reshape(blocks, BLOCK)
    doc_before = doc_index(
        first_place + lax.broadcasted_iota(jnp.int32, (blocks,), 0) * BLOCK - 1, doc_starts
    )
    inputs_blocks = features.reshape(blocks, BLOCK, heads_here, width)
    key_blocks = key_full.reshape(blocks, BLOCK, n_state)
    query_blocks = query_full.reshape(blocks, BLOCK, n_state)
    decay_blocks = decays.reshape(blocks, BLOCK, heads_here)

    def state_pass(carry, pieces):
        carry_state, kept_share = carry
        by_head, key_block, query_block, decay_block, doc_block, before = pieces
        block_state, through, running = state_terms(
            by_head, key_block, decay_block, doc_block, before
        )
        new_carry = (through[:, None, None] * carry_state + block_state, through * kept_share)
        return (new_carry, (block_state, through, running))

    zero_state = jnp.zeros((heads_here, width, n_state), jnp.float32)
    ones_here = jnp.ones((heads_here,), jnp.float32)
    local_carry, block_outputs = lax.scan(
        state_pass,
        (zero_state, ones_here),
        (inputs_blocks, key_blocks, query_blocks, decay_blocks, doc_ids, doc_before),
    )
    local_state, local_kept = local_carry
    block_states, throughs, runnings = (block_outputs[0], block_outputs[1], block_outputs[2])
    entry_state = exclusive_prefix(local_kept, local_state, "sc", "sz", "sx")

    def mix_pass(carry_state, pieces):
        by_head, key_block, query_block, running, doc_block, before, block_state, through = pieces
        carried = entry_terms(query_block, carry_state, running, doc_block, before)
        mixed_block = (
            inner_terms(by_head, key_block, query_block, running, doc_block)
            + carried
            + skip_gain[:, None, None] * by_head.astype(jnp.float32).transpose(1, 0, 2)
        )
        return (through[:, None, None] * carry_state + block_state, mixed_block)

    final_state, mixed = lax.scan(
        mix_pass,
        entry_state,
        (
            inputs_blocks,
            key_blocks,
            query_blocks,
            runnings,
            doc_ids,
            doc_before,
            block_states,
            throughs,
        ),
    )
    mixed = mixed.transpose(1, 0, 2, 3).reshape(heads_here, tok_dev, width)
    gate_rows = place(gate_moved).reshape(tok_dev, heads_here, width).transpose(1, 0, 2)
    gated = mixed * jax.nn.silu(gate_rows.astype(jnp.float32))
    squares = jnp.sum(gated * gated, axis=(0, 2))
    square_hi = squares.astype(jnp.bfloat16)
    square_lo = (squares - square_hi.astype(jnp.float32)).astype(jnp.bfloat16)
    unscaled = (gated * norm_gain.reshape(heads_here, 1, width)).astype(jnp.bfloat16)
    partial = jnp.einsum(
        "htp,hpd->td",
        unscaled,
        out_weight.reshape(heads_here, width, out_weight.shape[1]),
        preferred_element_type=jnp.float32,
    ).astype(jnp.bfloat16)
    groups = lax.axis_size("head")
    chunk = tok_dev // groups
    d_model = partial.shape[1]
    extra = jnp.concatenate(
        [square_hi.reshape(groups, 1, chunk), square_lo.reshape(groups, 1, chunk)], axis=1
    )
    extra = jnp.pad(extra, ((0, 0), (0, 6), (0, d_model - chunk)))
    sent = jnp.concatenate([partial.reshape(groups, chunk, d_model), extra], axis=1)
    arrived_parts = lax.all_to_all(sent, "head", split_axis=0, concat_axis=0, tiled=True)
    summed = jnp.sum(arrived_parts.astype(jnp.float32), axis=0)
    total_squares = summed[chunk, :chunk] + summed[chunk + 1, :chunk]
    row_scale = lax.rsqrt(total_squares / (ATTENTION_LANES * HEAD_DIM) + norm_eps)
    return (summed[:chunk] * row_scale[:, None]).astype(jnp.bfloat16)


def solution(mesh):
    seq = mesh.shape["seq"]
    devices = mesh.devices.reshape(seq // 16, 8, 2, mesh.shape["head"])
    split_mesh = jax.sharding.Mesh(devices, ROWS + ("head",))
    in_specs = (
        P(ROWS, "head"),
        P(ROWS, "head"),
        P(ROWS, None),
        P(ROWS, None),
        P(ROWS, "head"),
        P(ROWS),
        P(),
        P("head"),
        P("head"),
        P("head", None),
    )
    out_specs = P(ROWS + ("head",), None)
    return jax.shard_map(
        body, mesh=split_mesh, in_specs=in_specs, out_specs=out_specs, check_vma=False
    )
```

```python
import jax
import jax.numpy as jnp
from jax import lax
from jax.sharding import PartitionSpec as P

ATTENTION_LANES = 48
ROWS = ("sx", "sz", "sc")
HEAD_DIM = 64
BLOCK = 512


far_below = -1e30
norm_eps = 1e-05


def combine(earlier, later):
    return (earlier[0] * later[0], later[0][:, None, None] * earlier[1] + later[1])


def pack_state(kept, state):
    flat = jnp.broadcast_to(kept[:, None, None], (kept.shape[0], 1, state.shape[2]))
    return jnp.concatenate([state, flat], axis=1).astype(jnp.bfloat16)


def group_weights(kept, here):
    count = kept.shape[0]
    j = lax.broadcasted_iota(jnp.int32, (count, count), 0)
    k = lax.broadcasted_iota(jnp.int32, (count, count), 1)
    ahead = lax.broadcasted_iota(jnp.int32, (count, 1), 0) < here
    between = (j < k) & (k < here)
    into_here = jnp.prod(jnp.where(between[:, :, None], kept[None, :, :], 1.0), axis=1) * ahead
    into_end = jnp.prod(jnp.where((j < k)[:, :, None], kept[None, :, :], 1.0), axis=1)
    kept_before = jnp.prod(jnp.where(ahead, kept, 1.0), axis=0)
    return into_here, into_end, kept_before, jnp.prod(kept, axis=0)


def gathered_level(kept, state, axis):
    gathered = lax.all_gather(pack_state(kept, state), axis)
    g_kept = gathered[:, :, -1, 0].astype(jnp.float32)
    into_here, into_end, kept_before, kept_all = group_weights(g_kept, lax.axis_index(axis))
    rows = state.shape[1]
    before = jnp.einsum("jh,jhpn->hpn", into_here, gathered.astype(jnp.float32))[:, :rows]
    total = jnp.einsum("jh,jhpn->hpn", into_end, gathered.astype(jnp.float32))[:, :rows]
    return before, kept_before, total, kept_all


def exclusive_prefix(kept, state, pair, line, lines):
    pair_before, pair_kept_before, pair_total, pair_kept = gathered_level(kept, state, pair)
    half = kept.shape[0] // 2
    mine = lax.axis_index(pair) * half
    part_total = lax.dynamic_slice_in_dim(pair_total, mine, half, 0)
    part_kept = lax.dynamic_slice_in_dim(pair_kept, mine, half, 0)
    line_before, line_kept_before, line_total, line_kept = gathered_level(
        part_kept, part_total, line
    )
    outer_before, _, _, _ = gathered_level(line_kept, line_total, lines)
    start_state = line_kept_before[:, None, None] * outer_before + line_before
    whole = lax.all_gather(start_state, pair, tiled=True)
    return pair_kept_before[:, None, None] * whole + pair_before


def doc_index(places, starts):
    return jnp.sum((starts[None, :] <= places[:, None]).astype(jnp.int32), axis=1) - 1


def state_terms(by_head, key_block, decay_block, doc_block, before):
    running = jnp.cumsum(decay_block.astype(jnp.float32), axis=0)
    same_doc = (doc_block == doc_block[-1]).astype(jnp.float32)
    closing_weight = jnp.exp(running[-1][None, :] - running) * same_doc[:, None]
    weighted = (key_block.astype(jnp.float32)[None, :, :] * closing_weight.T[:, :, None]).astype(
        jnp.bfloat16
    )
    block_state = jnp.einsum("hsn,shp->hpn", weighted, by_head, preferred_element_type=jnp.float32)
    through = jnp.exp(running[-1]) * (doc_block[-1] == before).astype(jnp.float32)
    return (block_state, through, running)


def inner_terms(by_head, key_block, query_block, running, doc_block):
    length = running.shape[0]
    later = lax.broadcasted_iota(jnp.int32, (length, length), 0)
    earlier = lax.broadcasted_iota(jnp.int32, (length, length), 1)
    allowed = (later >= earlier) & (doc_block[:, None] == doc_block[None, :])
    running_heads = running.T
    decay_gaps = jnp.where(
        allowed[None, :, :], running_heads[:, :, None] - running_heads[:, None, :], far_below
    )
    products = jnp.einsum("tn,sn->ts", query_block, key_block, preferred_element_type=jnp.float32)
    affinity_logits = (products[None, :, :] * jnp.exp(decay_gaps)).astype(jnp.bfloat16)
    return jnp.einsum("hts,shp->thp", affinity_logits, by_head, preferred_element_type=jnp.float32)


def entry_terms(query_block, carry_state, running, doc_block, before):
    entry_weight = jnp.exp(running) * (doc_block == before).astype(jnp.float32)[:, None]
    carried = jnp.einsum(
        "tn,hpn->thp", query_block.astype(jnp.float32), carry_state, precision=lax.Precision.HIGH
    )
    return carried * entry_weight[:, :, None]


def body(
    features_in,
    gate_in,
    b_input,
    c_input,
    log_decay,
    row_target,
    doc_lengths,
    skip_gain,
    norm_gain,
    out_weight,
):
    tok_dev = features_in.shape[0]
    heads_here = log_decay.shape[1]
    feats = features_in.shape[1]
    width = feats // heads_here
    n_state = b_input.shape[1]
    shards = lax.axis_size(ROWS)
    capacity = tok_dev // shards
    owner = row_target // tok_dev
    local_place = row_target - owner * tok_dev
    owner_hits = (owner[:, None] == lax.broadcasted_iota(jnp.int32, (tok_dev, shards), 1)).astype(
        jnp.int32
    )
    slot_rank = jnp.sum((jnp.cumsum(owner_hits, axis=0) - owner_hits) * owner_hits, axis=1)
    slot_index = owner * capacity + slot_rank
    place_hi = (local_place // 32).astype(jnp.bfloat16)
    place_lo = (local_place % 32).astype(jnp.bfloat16)
    pieces = [features_in, gate_in, b_input, c_input, log_decay, place_hi[:, None], place_lo[:, None]]
    to_slot = (
        lax.broadcasted_iota(jnp.int32, (tok_dev, tok_dev), 0) == slot_index[None, :]
    ).astype(jnp.bfloat16)

    def send(values):
        packed = jnp.concatenate(
            [
                jnp.dot(to_slot, v, preferred_element_type=jnp.float32).astype(jnp.bfloat16)
                for v in values
            ],
            axis=1,
        )
        return lax.all_to_all(
            packed.reshape(shards, capacity, packed.shape[1]),
            ROWS,
            split_axis=0,
            concat_axis=0,
            tiled=True,
        ).reshape(tok_dev, packed.shape[1])

    rows_out = jnp.concatenate(pieces[4:], axis=1)
    gate_piece = pieces[1]
    pieces = [pieces[0]] + pieces[2:4] + [rows_out]
    moved = send(pieces)
    columns = moved.shape[1]
    arrived = (
        moved[:, columns - 2].astype(jnp.int32) * 32 + moved[:, columns - 1].astype(jnp.int32)
    )
    to_place = (
        lax.broadcasted_iota(jnp.int32, (tok_dev, tok_dev), 0) == arrived[None, :]
    ).astype(jnp.bfloat16)

    def place(values):
        return jnp.dot(to_place, values, preferred_element_type=jnp.float32).astype(jnp.bfloat16)

    rows = place(moved)
    features = rows[:, :feats]
    key_full = rows[:, feats : feats + n_state]
    query_full = rows[:, feats + n_state : feats + 2 * n_state]
    decays = rows[:, feats + 2 * n_state : feats + 2 * n_state + heads_here]
    gate_moved = send([gate_piece])

    doc_starts = jnp.cumsum(doc_lengths) - doc_lengths
    first_place = lax.axis_index(ROWS) * tok_dev
    blocks = tok_dev // BLOCK
    places = first_place + lax.broadcasted_iota(jnp.int32, (tok_dev,), 0)
    doc_ids = doc_index(places, doc_starts).reshape(blocks, BLOCK)
    doc_before = doc_index(
        first_place + lax.broadcasted_iota(jnp.int32, (blocks,), 0) * BLOCK - 1, doc_starts
    )
    inputs_blocks = features.reshape(blocks, BLOCK, heads_here, width)
    key_blocks = key_full.reshape(blocks, BLOCK, n_state)
    query_blocks = query_full.reshape(blocks, BLOCK, n_state)
    decay_blocks = decays.reshape(blocks, BLOCK, heads_here)

    def state_pass(carry, pieces):
        carry_state, kept_share = carry
        by_head, key_block, query_block, decay_block, doc_block, before = pieces
        block_state, through, running = state_terms(
            by_head, key_block, decay_block, doc_block, before
        )
        new_carry = (through[:, None, None] * carry_state + block_state, through * kept_share)
        return (new_carry, (block_state, through, running))

    zero_state = jnp.zeros((heads_here, width, n_state), jnp.float32)
    ones_here = jnp.ones((heads_here,), jnp.float32)
    local_carry, block_outputs = lax.scan(
        state_pass,
        (zero_state, ones_here),
        (inputs_blocks, key_blocks, query_blocks, decay_blocks, doc_ids, doc_before),
    )
    local_state, local_kept = local_carry
    block_states, throughs, runnings = (block_outputs[0], block_outputs[1], block_outputs[2])
    entry_state = exclusive_prefix(local_kept, local_state, "sc", "sz", "sx")

    def mix_pass(carry_state, pieces):
        by_head, key_block, query_block, running, doc_block, before, block_state, through = pieces
        carried = entry_terms(query_block, carry_state, running, doc_block, before)
        mixed_block = (
            inner_terms(by_head, key_block, query_block, running, doc_block)
            + carried
            + skip_gain[None, :, None] * by_head.astype(jnp.float32)
        )
        return (through[:, None, None] * carry_state + block_state, mixed_block)

    final_state, mixed = lax.scan(
        mix_pass,
        entry_state,
        (
            inputs_blocks,
            key_blocks,
            query_blocks,
            runnings,
            doc_ids,
            doc_before,
            block_states,
            throughs,
        ),
    )
    mixed = mixed.reshape(tok_dev, heads_here * width)
    gate_rows = place(gate_moved)
    gated = mixed * jax.nn.silu(gate_rows.astype(jnp.float32))
    squares = jnp.sum(gated * gated, axis=1)
    square_hi = squares.astype(jnp.bfloat16)
    square_lo = (squares - square_hi.astype(jnp.float32)).astype(jnp.bfloat16)
    unscaled = (gated * norm_gain[None, :]).astype(jnp.bfloat16)
    partial = jnp.dot(unscaled, out_weight, preferred_element_type=jnp.float32).astype(jnp.bfloat16)
    groups = lax.axis_size("head")
    chunk = tok_dev // groups
    d_model = partial.shape[1]
    extra = jnp.concatenate(
        [square_hi.reshape(groups, 1, chunk), square_lo.reshape(groups, 1, chunk)], axis=1
    )
    extra = jnp.pad(extra, ((0, 0), (0, 6), (0, d_model - chunk)))
    sent = jnp.concatenate([partial.reshape(groups, chunk, d_model), extra], axis=1)
    arrived_parts = lax.all_to_all(sent, "head", split_axis=0, concat_axis=0, tiled=True)
    summed = jnp.sum(arrived_parts.astype(jnp.float32), axis=0)
    total_squares = summed[chunk, :chunk] + summed[chunk + 1, :chunk]
    row_scale = lax.rsqrt(total_squares / (ATTENTION_LANES * HEAD_DIM) + norm_eps)
    return (summed[:chunk] * row_scale[:, None]).astype(jnp.bfloat16)


def solution(mesh):
    seq = mesh.shape["seq"]
    devices = mesh.devices.reshape(seq // 16, 8, 2, mesh.shape["head"])
    split_mesh = jax.sharding.Mesh(devices, ROWS + ("head",))
    in_specs = (
        P(ROWS, "head"),
        P(ROWS, "head"),
        P(ROWS, None),
        P(ROWS, None),
        P(ROWS, "head"),
        P(ROWS),
        P(),
        P("head"),
        P("head"),
        P("head", None),
    )
    out_specs = P(ROWS + ("head",), None)
    return jax.shard_map(
        body, mesh=split_mesh, in_specs=in_specs, out_specs=out_specs, check_vma=False
    )
```

```python
import jax
import jax.numpy as jnp
from jax import lax
from jax.sharding import PartitionSpec as P

ATTENTION_LANES = 48
ROWS = ("sx", "sz", "sc")
HEAD_DIM = 64
BLOCK = 512


far_below = -1e30
norm_eps = 1e-05


def combine(earlier, later):
    return (earlier[0] * later[0], later[0][:, None, None] * earlier[1] + later[1])


def pack_state(kept, state):
    flat = jnp.broadcast_to(kept[:, None, None], (kept.shape[0], 1, state.shape[2]))
    return jnp.concatenate([state, flat], axis=1).astype(jnp.bfloat16)


def group_weights(kept, here):
    count = kept.shape[0]
    j = lax.broadcasted_iota(jnp.int32, (count, count), 0)
    k = lax.broadcasted_iota(jnp.int32, (count, count), 1)
    ahead = lax.broadcasted_iota(jnp.int32, (count, 1), 0) < here
    between = (j < k) & (k < here)
    into_here = jnp.prod(jnp.where(between[:, :, None], kept[None, :, :], 1.0), axis=1) * ahead
    into_end = jnp.prod(jnp.where((j < k)[:, :, None], kept[None, :, :], 1.0), axis=1)
    kept_before = jnp.prod(jnp.where(ahead, kept, 1.0), axis=0)
    return into_here, into_end, kept_before, jnp.prod(kept, axis=0)


def gathered_level(kept, state, axis):
    gathered = lax.all_gather(pack_state(kept, state), axis)
    g_kept = gathered[:, :, -1, 0].astype(jnp.float32)
    into_here, into_end, kept_before, kept_all = group_weights(g_kept, lax.axis_index(axis))
    rows = state.shape[1]
    before = jnp.einsum("jh,jhpn->hpn", into_here, gathered.astype(jnp.float32))[:, :rows]
    total = jnp.einsum("jh,jhpn->hpn", into_end, gathered.astype(jnp.float32))[:, :rows]
    return before, kept_before, total, kept_all


def exclusive_prefix(kept, state, pair, line, lines):
    pair_before, pair_kept_before, pair_total, pair_kept = gathered_level(kept, state, pair)
    half = kept.shape[0] // 2
    mine = lax.axis_index(pair) * half
    part_total = lax.dynamic_slice_in_dim(pair_total, mine, half, 0)
    part_kept = lax.dynamic_slice_in_dim(pair_kept, mine, half, 0)
    line_before, line_kept_before, line_total, line_kept = gathered_level(
        part_kept, part_total, line
    )
    outer_before, _, _, _ = gathered_level(line_kept, line_total, lines)
    start_state = line_kept_before[:, None, None] * outer_before + line_before
    whole = lax.all_gather(start_state.astype(jnp.bfloat16), pair, tiled=True)
    return pair_kept_before[:, None, None] * whole.astype(jnp.float32) + pair_before


def doc_index(places, starts):
    return jnp.sum((starts[None, :] <= places[:, None]).astype(jnp.int32), axis=1) - 1


def state_terms(by_head, key_block, decay_block, doc_block, before):
    running = jnp.cumsum(decay_block.astype(jnp.float32), axis=0)
    same_doc = (doc_block == doc_block[-1]).astype(jnp.float32)
    closing_weight = jnp.exp(running[-1][None, :] - running) * same_doc[:, None]
    weighted = (key_block.astype(jnp.float32)[None, :, :] * closing_weight.T[:, :, None]).astype(
        jnp.bfloat16
    )
    block_state = jnp.einsum("hsn,shp->hpn", weighted, by_head, preferred_element_type=jnp.float32)
    through = jnp.exp(running[-1]) * (doc_block[-1] == before).astype(jnp.float32)
    return (block_state, through, running)


def inner_terms(by_head, key_block, query_block, running, doc_block):
    length = running.shape[0]
    later = lax.broadcasted_iota(jnp.int32, (length, length), 0)
    earlier = lax.broadcasted_iota(jnp.int32, (length, length), 1)
    allowed = (later >= earlier) & (doc_block[:, None] == doc_block[None, :])
    running_heads = running.T
    decay_gaps = jnp.where(
        allowed[None, :, :], running_heads[:, :, None] - running_heads[:, None, :], far_below
    )
    products = jnp.einsum("tn,sn->ts", query_block, key_block, preferred_element_type=jnp.float32)
    affinity_logits = (products[None, :, :] * jnp.exp(decay_gaps)).astype(jnp.bfloat16)
    return jnp.einsum("hts,shp->thp", affinity_logits, by_head, preferred_element_type=jnp.float32)


def entry_terms(query_block, carry_state, running, doc_block, before):
    entry_weight = jnp.exp(running) * (doc_block == before).astype(jnp.float32)[:, None]
    carried = jnp.einsum(
        "tn,hpn->thp",
        query_block,
        carry_state.astype(jnp.bfloat16),
        preferred_element_type=jnp.float32,
    )
    return carried * entry_weight[:, :, None]


def body(
    features_in,
    gate_in,
    b_input,
    c_input,
    log_decay,
    row_target,
    doc_lengths,
    skip_gain,
    norm_gain,
    out_weight,
):
    tok_dev = features_in.shape[0]
    heads_here = log_decay.shape[1]
    feats = features_in.shape[1]
    width = feats // heads_here
    n_state = b_input.shape[1]
    shards = lax.axis_size(ROWS)
    capacity = tok_dev // shards
    owner = row_target // tok_dev
    local_place = row_target - owner * tok_dev
    owner_hits = (owner[:, None] == lax.broadcasted_iota(jnp.int32, (tok_dev, shards), 1)).astype(
        jnp.int32
    )
    slot_rank = jnp.sum((jnp.cumsum(owner_hits, axis=0) - owner_hits) * owner_hits, axis=1)
    slot_index = owner * capacity + slot_rank
    place_hi = (local_place // 32).astype(jnp.bfloat16)
    place_lo = (local_place % 32).astype(jnp.bfloat16)
    pieces = [features_in, gate_in, b_input, c_input, log_decay, place_hi[:, None], place_lo[:, None]]
    to_slot = (
        lax.broadcasted_iota(jnp.int32, (tok_dev, tok_dev), 0) == slot_index[None, :]
    ).astype(jnp.bfloat16)

    def send(values):
        packed = jnp.concatenate(
            [
                jnp.dot(to_slot, v, preferred_element_type=jnp.float32).astype(jnp.bfloat16)
                for v in values
            ],
            axis=1,
        )
        return lax.all_to_all(
            packed.reshape(shards, capacity, packed.shape[1]),
            ROWS,
            split_axis=0,
            concat_axis=0,
            tiled=True,
        ).reshape(tok_dev, packed.shape[1])

    rows_out = jnp.concatenate(pieces[4:], axis=1)
    gate_piece = pieces[1]
    pieces = [pieces[0]] + pieces[2:4] + [rows_out]
    moved = send(pieces)
    columns = moved.shape[1]
    arrived = (
        moved[:, columns - 2].astype(jnp.int32) * 32 + moved[:, columns - 1].astype(jnp.int32)
    )
    to_place = (
        lax.broadcasted_iota(jnp.int32, (tok_dev, tok_dev), 0) == arrived[None, :]
    ).astype(jnp.bfloat16)

    def place(values):
        return jnp.dot(to_place, values, preferred_element_type=jnp.float32).astype(jnp.bfloat16)

    rows = place(moved)
    features = rows[:, :feats]
    key_full = rows[:, feats : feats + n_state]
    query_full = rows[:, feats + n_state : feats + 2 * n_state]
    decays = rows[:, feats + 2 * n_state : feats + 2 * n_state + heads_here]
    gate_moved = send([gate_piece])

    doc_starts = jnp.cumsum(doc_lengths) - doc_lengths
    first_place = lax.axis_index(ROWS) * tok_dev
    blocks = tok_dev // BLOCK
    places = first_place + lax.broadcasted_iota(jnp.int32, (tok_dev,), 0)
    doc_ids = doc_index(places, doc_starts).reshape(blocks, BLOCK)
    doc_before = doc_index(
        first_place + lax.broadcasted_iota(jnp.int32, (blocks,), 0) * BLOCK - 1, doc_starts
    )
    inputs_blocks = features.reshape(blocks, BLOCK, heads_here, width)
    key_blocks = key_full.reshape(blocks, BLOCK, n_state)
    query_blocks = query_full.reshape(blocks, BLOCK, n_state)
    decay_blocks = decays.reshape(blocks, BLOCK, heads_here)

    def state_pass(carry, pieces):
        carry_state, kept_share = carry
        by_head, key_block, query_block, decay_block, doc_block, before = pieces
        block_state, through, running = state_terms(
            by_head, key_block, decay_block, doc_block, before
        )
        new_carry = (through[:, None, None] * carry_state + block_state, through * kept_share)
        return (new_carry, (block_state, through, running))

    zero_state = jnp.zeros((heads_here, width, n_state), jnp.float32)
    ones_here = jnp.ones((heads_here,), jnp.float32)
    local_carry, block_outputs = lax.scan(
        state_pass,
        (zero_state, ones_here),
        (inputs_blocks, key_blocks, query_blocks, decay_blocks, doc_ids, doc_before),
    )
    local_state, local_kept = local_carry
    block_states, throughs, runnings = (block_outputs[0], block_outputs[1], block_outputs[2])
    entry_state = exclusive_prefix(local_kept, local_state, "sc", "sz", "sx")

    def mix_pass(carry_state, pieces):
        by_head, key_block, query_block, running, doc_block, before, block_state, through = pieces
        carried = entry_terms(query_block, carry_state, running, doc_block, before)
        mixed_block = (
            inner_terms(by_head, key_block, query_block, running, doc_block)
            + carried
            + skip_gain[None, :, None] * by_head.astype(jnp.float32)
        )
        return (through[:, None, None] * carry_state + block_state, mixed_block)

    final_state, mixed = lax.scan(
        mix_pass,
        entry_state,
        (
            inputs_blocks,
            key_blocks,
            query_blocks,
            runnings,
            doc_ids,
            doc_before,
            block_states,
            throughs,
        ),
    )
    mixed = mixed.reshape(tok_dev, heads_here * width)
    gate_rows = place(gate_moved)
    gated = mixed * jax.nn.silu(gate_rows.astype(jnp.float32))
    squares = jnp.sum(gated * gated, axis=1)
    square_hi = squares.astype(jnp.bfloat16)
    square_lo = (squares - square_hi.astype(jnp.float32)).astype(jnp.bfloat16)
    unscaled = (gated * norm_gain[None, :]).astype(jnp.bfloat16)
    partial = jnp.dot(unscaled, out_weight, preferred_element_type=jnp.float32).astype(jnp.bfloat16)
    groups = lax.axis_size("head")
    chunk = tok_dev // groups
    d_model = partial.shape[1]
    extra = jnp.concatenate(
        [square_hi.reshape(groups, 1, chunk), square_lo.reshape(groups, 1, chunk)], axis=1
    )
    extra = jnp.pad(extra, ((0, 0), (0, 6), (0, d_model - chunk)))
    sent = jnp.concatenate([partial.reshape(groups, chunk, d_model), extra], axis=1)
    arrived_parts = lax.all_to_all(sent, "head", split_axis=0, concat_axis=0, tiled=True)
    summed = jnp.sum(arrived_parts.astype(jnp.float32), axis=0)
    total_squares = summed[chunk, :chunk] + summed[chunk + 1, :chunk]
    row_scale = lax.rsqrt(total_squares / (ATTENTION_LANES * HEAD_DIM) + norm_eps)
    return (summed[:chunk] * row_scale[:, None]).astype(jnp.bfloat16)


def solution(mesh):
    seq = mesh.shape["seq"]
    devices = mesh.devices.reshape(seq // 16, 8, 2, mesh.shape["head"])
    split_mesh = jax.sharding.Mesh(devices, ROWS + ("head",))
    in_specs = (
        P(ROWS, "head"),
        P(ROWS, "head"),
        P(ROWS, None),
        P(ROWS, None),
        P(ROWS, "head"),
        P(ROWS),
        P(),
        P("head"),
        P("head"),
        P("head", None),
    )
    out_specs = P(ROWS + ("head",), None)
    return jax.shard_map(
        body, mesh=split_mesh, in_specs=in_specs, out_specs=out_specs, check_vma=False
    )
```
